32 devices in a mesh: groups: 2 (over x), ctx: 16 (over z, y, core).
Axes of the slice: x: 2, y: 2, z: 4, core: 2. Of those that a mesh axis runs over, the one named last changes fastest.
Arguments:
- queries: bfloat16 [4096, 2048], P(('groups', 'ctx')), parts along dimension 0, may hold values from -22 to 22
- key_rows: bfloat16 [4096, 512], P(('groups', 'ctx')), parts along dimension 0, may hold values from -4 to 4
- value_rows: bfloat16 [4096, 512], P(('groups', 'ctx')), parts along dimension 0, may hold values from -6 to 6
- output_gradient: bfloat16 [4096, 2048], P(('groups', 'ctx')), parts along dimension 0, may hold values from -6 to 6
- lengths: int32 [16], P('groups'), parts along dimension 0, may hold values from 1 to 512, 2048 in all
Outputs:
- attended: bfloat16 [4096, 2048], P(('groups', 'ctx')), parts along dimension 0
- grad_queries: bfloat16 [4096, 2048], P(('groups', 'ctx')), parts along dimension 0
- key_gradient: bfloat16 [4096, 512], P(('groups', 'ctx')), parts along dimension 0
- value_gradient: bfloat16 [4096, 512], P(('groups', 'ctx')), parts along dimension 0
The draws below stay inside these ranges and needn't reach their ends.
There are 2 independent parts, one for each index of `groups`. The reference program is written for one: setup_inputs(seed, part) draws one part's arguments, and reference() takes and returns one part's arrays. A program takes and returns all parts, laid end to end along the dimension named above; each array names one. Nothing has to cross between parts.
Inputs may be any that keep to these rules, and one draw needn't show every extreme that they name: `lengths`: each document has 1 to 512 tokens, one exactly 512; they sum to 2048.
All inputs are finite; a program needn't handle non-finite values.
Results may differ from the reference program's by a relative error of at most 0.035.
Values may be sent and summed in bfloat16 or wider, within the bound.
No kernel may reach another device: no remote copies, remote signals or barrier semaphores. Data moves between devices by JAX's collectives and lax.ppermute only.
A program may use at most 128 MiB of HBM per device.

```python
import math
import jax
import jax.numpy as jnp
import numpy as np
from jax import lax

QUERY_HEADS = 16
KEY_VALUE_HEADS = 4
HEAD_SIZE = 128
DOCUMENT_REACH = 8
T_DEV = 128
TILE_TOKENS = 64
MOST_DOC = 512
SEQUENCE_TOKENS = 2048
DOCS = 8


def draw_key_rows(key, part):
    gaussian_part = jax.random.normal(jax.random.fold_in(key, 21), (SEQUENCE_TOKENS, KEY_VALUE_HEADS * HEAD_SIZE), jnp.float32)
    return jnp.clip(gaussian_part, -4.0, 4.0).astype(jnp.bfloat16)


def draw_queries(key, part):
    gaussian_part = jax.random.normal(jax.random.fold_in(key, 31), (SEQUENCE_TOKENS, QUERY_HEADS * HEAD_SIZE), jnp.float32)
    return jnp.clip(gaussian_part, -4.0, 4.0).astype(jnp.bfloat16)


def steps_of(rng, shape, split, least, top_value):
    level = 1.0
    for axis_at, parts in split:
        steps = jax.random.uniform(jax.random.fold_in(jax.random.fold_in(rng, 6), axis_at), (parts,), jnp.float32, least / len(split), top_value / len(split))
        level = level * jnp.repeat(jnp.exp(steps), shape[axis_at] // parts).reshape((-1,) + (1,) * (len(shape) - 1 - axis_at))
    return level


def split_up(amount, total, bound, slope):
    portions = [(1 << 20) // math.isqrt(rank ** slope) + 1 for rank in range(2, amount + 1)]
    rest, holding = total - bound - (amount - 1), [1] * (amount - 1)
    while rest > 0:
        free = [i for i in range(amount - 1) if holding[i] < bound]
        pool, remaining = sum([portions[i] for i in free]), rest
        for i in free:
            extra = min(bound - holding[i], max(1, remaining * portions[i] // pool), rest)
            holding[i] = holding[i] + extra
            rest = rest - extra
    return np.array([bound] + holding)


def uneven_parts(rng, count, total, reach, skew):
    if count == 2:
        one = jax.random.randint(rng, (), max(1, total - reach), min(reach, total - 1) + 1)
        return jnp.stack([one, total - one])
    sizes = jnp.asarray(split_up(count, total, reach, skew), jnp.int32)
    pairs = (count - 1) // 2
    donor, taker = sizes[1:1 + 2 * pairs:2], sizes[2:2 + 2 * pairs:2]
    slack = jnp.minimum(donor - 1, reach - taker)
    moved = jax.random.randint(jax.random.fold_in(rng, 1), (pairs,), 0, 1 << 20) % (slack + 1)
    sizes = sizes.at[1:1 + 2 * pairs:2].set(donor - moved).at[2:2 + 2 * pairs:2].set(taker + moved)
    return sizes[jax.random.permutation(jax.random.fold_in(rng, 2), count)]


def normal_values(rng, dims, width, limit, pieces=(), kind=jnp.bfloat16):
    values = width * jax.random.normal(rng, dims, jnp.float32)
    if pieces:
        values = values * steps_of(rng, dims, pieces, -0.22, 0.18)
    return jnp.clip(values, -limit, limit).astype(kind)


def setup_inputs(seed: int = 0, part: int = 0) -> dict:
    key_list = jax.random.split(jax.random.key(seed), 6)
    part_keys = jax.random.split(jax.random.fold_in(key_list[5], part), 6)
    return {
        "queries": draw_queries(jax.random.fold_in(jax.random.fold_in(key_list[5], part), 71), part),
        "key_rows": draw_key_rows(jax.random.fold_in(jax.random.fold_in(key_list[5], part), 71), part),
        "value_rows": normal_values(part_keys[2], (SEQUENCE_TOKENS, KEY_VALUE_HEADS * HEAD_SIZE), 1.0, 6.0, ((0, 16),)),
        "output_gradient": normal_values(part_keys[3], (SEQUENCE_TOKENS, QUERY_HEADS * HEAD_SIZE), 1.0, 6.0, ((0, 16),)),
        "lengths": uneven_parts(part_keys[4], DOCS, SEQUENCE_TOKENS, MOST_DOC, 2).astype(jnp.int32),
    }


NEGATIVE_FLOOR = -1e+30

def row_positions(count, per_device, tile_rows):
    row_ids = jnp.arange(count, dtype=jnp.int32)
    device_id = row_ids // per_device
    within = row_ids % per_device
    block_id = jnp.where(within < tile_rows, device_id, count // tile_rows - 1 - device_id)
    return (block_id * tile_rows + within % tile_rows).astype(jnp.int32)

def doc_number(lengths, places):
    doc_ends = jnp.cumsum(lengths).astype(jnp.int32)
    doc_hits = (doc_ends[None, :] <= places[:, None]).astype(jnp.int32)
    return lax.optimization_barrier(jnp.sum(doc_hits, axis=1)).astype(jnp.int32)

def rounded(values):
    return lax.optimization_barrier(values.astype(jnp.bfloat16)).astype(jnp.float32)

def reference(queries, key_rows, value_rows, output_gradient, lengths):
    group_width = QUERY_HEADS // KEY_VALUE_HEADS
    tile_number_count = SEQUENCE_TOKENS // TILE_TOKENS
    score_scale = 1.0 / math.sqrt(HEAD_SIZE)
    highest = lax.Precision.HIGHEST
    row_location = row_positions(SEQUENCE_TOKENS, T_DEV, TILE_TOKENS)

    def into_positions(values, trailing):
        return jnp.zeros_like(values).at[row_location].set(values).reshape((tile_number_count, TILE_TOKENS) + trailing)
    query_sequence = into_positions(queries, (KEY_VALUE_HEADS, group_width, HEAD_SIZE))
    sequence_gradient = into_positions(output_gradient, (KEY_VALUE_HEADS, group_width, HEAD_SIZE))
    empty_blocks = jnp.zeros((DOCUMENT_REACH, TILE_TOKENS, KEY_VALUE_HEADS, HEAD_SIZE), key_rows.dtype)
    padded_keys = jnp.concatenate([empty_blocks, into_positions(key_rows, (KEY_VALUE_HEADS, HEAD_SIZE))], axis=0)
    padded_values = jnp.concatenate([empty_blocks, into_positions(value_rows, (KEY_VALUE_HEADS, HEAD_SIZE))], axis=0)
    offsets = jnp.arange(TILE_TOKENS, dtype=jnp.int32)
    zero_heads = jnp.zeros((TILE_TOKENS, KEY_VALUE_HEADS, group_width, HEAD_SIZE), jnp.float32)
    key_value_zeros = jnp.zeros((TILE_TOKENS, KEY_VALUE_HEADS, HEAD_SIZE), jnp.float32)

    def one_tile(carry, tile_id):
        key_gradient_part, value_gradient_part = carry
        query_tile_rows = lax.dynamic_index_in_dim(query_sequence, tile_id, 0, keepdims=False).astype(jnp.float32)
        tile_gradient = lax.dynamic_index_in_dim(sequence_gradient, tile_id, 0, keepdims=False).astype(jnp.float32)
        query_place = tile_id * TILE_TOKENS + offsets
        query_doc = doc_number(lengths, query_place)
        blocks = []
        for distance in range(DOCUMENT_REACH + 1):
            slot_id = tile_id + DOCUMENT_REACH - distance
            key_place = (tile_id - distance) * TILE_TOKENS + offsets
            key_doc = doc_number(lengths, key_place)
            visible = (query_doc[:, None] == key_doc[None, :]) & (key_place[None, :] <= query_place[:, None]) & (key_place[None, :] >= 0)
            key_tile = lax.dynamic_index_in_dim(padded_keys, slot_id, 0, keepdims=False).astype(jnp.float32)
            value_tile = lax.dynamic_index_in_dim(padded_values, slot_id, 0, keepdims=False).astype(jnp.float32)
            active = jnp.any(visible)

            def score_block(key_in=key_tile):
                return jnp.einsum('imgx,jmx->mgij', query_tile_rows, key_in, precision=highest) * score_scale

            def score_empty():
                return jnp.zeros((KEY_VALUE_HEADS, group_width, TILE_TOKENS, TILE_TOKENS), jnp.float32)
            raw_scores = lax.cond(active, score_block, score_empty)
            scores = jnp.where(visible, raw_scores, NEGATIVE_FLOOR)
            blocks.append((slot_id, visible, active, key_tile, value_tile, scores))
        row_maximum = lax.optimization_barrier(jnp.max(blocks[0][5], axis=-1))
        for block in blocks[1:]:
            row_maximum = jnp.maximum(row_maximum, lax.optimization_barrier(jnp.max(block[5], axis=-1)))
        row_total_sum = jnp.zeros_like(row_maximum)
        for block in blocks:
            row_total_sum = row_total_sum + lax.optimization_barrier(jnp.sum(jnp.where(block[1], jnp.exp(block[5] - row_maximum[..., None]), 0.0), axis=-1))
        log_norm = row_maximum + jnp.log(row_total_sum)
        attended = zero_heads
        for slot_id, visible, active, key_tile, value_tile, scores in blocks:

            def weigh_block(mask_in=visible, score_in=scores, value_in=value_tile):
                probs_b = rounded(jnp.where(mask_in, jnp.exp(score_in - log_norm[..., None]), 0.0))
                return jnp.einsum('mgij,jmx->imgx', probs_b, value_in, precision=highest)
            attended = attended + lax.cond(active, weigh_block, lambda: zero_heads)
        output_bf = rounded(attended)
        delta_dot = jnp.einsum('imgx,imgx->mgi', tile_gradient, output_bf, precision=highest)
        query_grad = zero_heads
        for slot_id, visible, active, key_tile, value_tile, scores in blocks:

            def tile_grads(mask_in=visible, score_in=scores, key_in=key_tile, value_in=value_tile):
                probs = jnp.where(mask_in, jnp.exp(score_in - log_norm[..., None]), 0.0)
                probs_b = rounded(probs)
                dprob = jnp.einsum('imgx,jmx->mgij', tile_gradient, value_in, precision=highest)
                dscore = rounded(probs * (dprob - delta_dot[..., None]))
                part_q = jnp.einsum('mgij,jmx->imgx', dscore, key_in, precision=highest) * score_scale
                part_k = jnp.einsum('mgij,imgx->jmx', dscore, query_tile_rows, precision=highest) * score_scale
                part_v = jnp.einsum('mgij,imgx->jmx', probs_b, tile_gradient, precision=highest)
                return (part_q, part_k, part_v)

            def no_grads():
                return (zero_heads, key_value_zeros, key_value_zeros)
            part_q, part_k, part_v = lax.cond(active, tile_grads, no_grads)
            query_grad = query_grad + part_q
            key_gradient_part = key_gradient_part.at[slot_id].add(part_k)
            value_gradient_part = value_gradient_part.at[slot_id].add(part_v)
        return ((key_gradient_part, value_gradient_part), (output_bf, query_grad))
    initial_gradients = jnp.zeros((tile_number_count + DOCUMENT_REACH, TILE_TOKENS, KEY_VALUE_HEADS, HEAD_SIZE), jnp.float32)
    carry, stacked = lax.scan(one_tile, (initial_gradients, initial_gradients), jnp.arange(tile_number_count, dtype=jnp.int32))
    key_gradient_part, value_gradient_part = carry
    output_seq, query_grad = stacked
    attended = output_seq.reshape(SEQUENCE_TOKENS, QUERY_HEADS * HEAD_SIZE)[row_location].astype(jnp.bfloat16)
    grad_queries = query_grad.reshape(SEQUENCE_TOKENS, QUERY_HEADS * HEAD_SIZE)[row_location].astype(jnp.bfloat16)
    key_gradient = key_gradient_part[DOCUMENT_REACH:].reshape(SEQUENCE_TOKENS, KEY_VALUE_HEADS * HEAD_SIZE)[row_location].astype(jnp.bfloat16)
    value_gradient = value_gradient_part[DOCUMENT_REACH:].reshape(SEQUENCE_TOKENS, KEY_VALUE_HEADS * HEAD_SIZE)[row_location].astype(jnp.bfloat16)
    return (attended, grad_queries, key_gradient, value_gradient)
```

```python
import math

import jax
import jax.numpy as jnp
from jax import lax
from jax.sharding import PartitionSpec as P

QUERY_HEADS = 16
KEY_VALUE_HEADS = 4
HEAD_SIZE = 128
DOCUMENT_REACH = 8

NEGATIVE_FLOOR = -1e30


def doc_number(lengths, places):
    doc_ends = jnp.cumsum(lengths)
    flat_places = places.reshape(-1)
    doc_hits = (doc_ends[None, :] <= flat_places[:, None]).astype(jnp.int32)
    return jnp.sum(doc_hits, axis=1).reshape(places.shape)


def permute(value, pairs):
    if not pairs:
        return jnp.zeros_like(value)
    return lax.ppermute(value, "ctx", pairs)


def block_routes(count, distance):
    lower_to_lower = [(s, s + distance) for s in range(count) if s + distance < count]
    upper_to_upper = [(s, s - distance) for s in range(count) if s - distance >= 0]
    lower_to_upper = [
        (s, 2 * count - 1 - s - distance)
        for s in range(count)
        if s + distance >= count and 2 * count - 1 - s - distance >= 0
    ]
    return lower_to_lower, upper_to_upper, lower_to_upper


def inverse(pairs):
    return [(d, s) for s, d in pairs]


def on_device(queries, key_rows, value_rows, output_gradient, lengths):
    count = lax.axis_size("ctx")
    my_index = lax.axis_index("ctx")
    row_count = queries.shape[0]
    block_rows = row_count // 2
    group_width = QUERY_HEADS // KEY_VALUE_HEADS
    key_value_width = KEY_VALUE_HEADS * HEAD_SIZE
    score_scale = 1.0 / math.sqrt(HEAD_SIZE)
    reach = DOCUMENT_REACH
    window = reach + 1

    own_blocks = jnp.stack([my_index, 2 * count - 1 - my_index])
    offsets = jnp.arange(block_rows, dtype=jnp.int32)
    query_place = own_blocks[:, None] * block_rows + offsets[None, :]
    key_block = own_blocks[:, None] - (reach - jnp.arange(window, dtype=jnp.int32))[None, :]
    key_place = (key_block[:, :, None] * block_rows + offsets[None, None, :]).reshape(2, -1)
    query_doc = doc_number(lengths, query_place)
    key_doc = doc_number(lengths, key_place)
    visible = (
        (query_doc[:, :, None] == key_doc[:, None, :])
        & (key_place[:, None, :] <= query_place[:, :, None])
        & (key_place[:, None, :] >= 0)
    )

    key_value = jnp.concatenate([key_rows, value_rows], axis=1).reshape(
        2, block_rows, 2 * key_value_width
    )
    lower_kv, upper_kv = key_value[0], key_value[1]
    fits_upper = [None] * (reach + 1)
    lower_window = [None] * (reach + 1)
    upper_window = [None] * (reach + 1)
    lower_window[0] = lower_kv
    upper_window[0] = upper_kv
    for distance in range(1, reach + 1):
        to_lower, to_upper, cross = block_routes(count, distance)
        lower_window[distance] = permute(lower_kv, to_lower)
        from_upper = permute(upper_kv, to_upper)
        from_cross = permute(lower_kv, cross)
        fits_upper[distance] = my_index + distance < count
        upper_window[distance] = jnp.where(fits_upper[distance], from_upper, from_cross)
    window_kv = jnp.stack(
        [
            jnp.stack([lower_window[reach - w] for w in range(window)]),
            jnp.stack([upper_window[reach - w] for w in range(window)]),
        ]
    ).reshape(2, window * block_rows, 2 * key_value_width)
    key_tile = window_kv[..., :key_value_width].reshape(
        2, window * block_rows, KEY_VALUE_HEADS, HEAD_SIZE
    )
    value_tile = window_kv[..., key_value_width:].reshape(
        2, window * block_rows, KEY_VALUE_HEADS, HEAD_SIZE
    )

    query_tile = queries.reshape(2, block_rows, KEY_VALUE_HEADS, group_width, HEAD_SIZE)
    grad_tile = output_gradient.reshape(2, block_rows, KEY_VALUE_HEADS, group_width, HEAD_SIZE)
    mask = visible[:, None, None]

    scores = (
        jnp.einsum("aimgx,ajmx->amgij", query_tile, key_tile, preferred_element_type=jnp.float32)
        * score_scale
    )
    masked = jnp.where(mask, scores, NEGATIVE_FLOOR)
    row_maximum = jnp.max(masked, axis=-1)
    row_sum = jnp.sum(jnp.where(mask, jnp.exp(masked - row_maximum[..., None]), 0.0), axis=-1)
    log_norm = row_maximum + jnp.log(row_sum)
    probs = jnp.where(mask, jnp.exp(scores - log_norm[..., None]), 0.0)
    probs_b = probs.astype(jnp.bfloat16)
    attended = jnp.einsum(
        "amgij,ajmx->aimgx", probs_b, value_tile, preferred_element_type=jnp.float32
    )
    output_bf = attended.astype(jnp.bfloat16)
    delta_dot = jnp.einsum(
        "aimgx,aimgx->amgi", grad_tile, output_bf, preferred_element_type=jnp.float32
    )
    dprob = jnp.einsum(
        "aimgx,ajmx->amgij", grad_tile, value_tile, preferred_element_type=jnp.float32
    )
    dscore = (probs * (dprob - delta_dot[..., None])).astype(jnp.bfloat16)
    query_grad = (
        jnp.einsum("amgij,ajmx->aimgx", dscore, key_tile, preferred_element_type=jnp.float32)
        * score_scale
    )
    key_part = (
        jnp.einsum("amgij,aimgx->ajmx", dscore, query_tile, preferred_element_type=jnp.float32)
        * score_scale
    )
    value_part = jnp.einsum(
        "amgij,aimgx->ajmx", probs_b, grad_tile, preferred_element_type=jnp.float32
    )
    grad_window = jnp.concatenate(
        [
            key_part.reshape(2, window, block_rows, key_value_width),
            value_part.reshape(2, window, block_rows, key_value_width),
        ],
        axis=-1,
    )
    lower_grad = grad_window[0, reach]
    upper_grad = grad_window[1, reach]
    for distance in range(1, reach + 1):
        to_lower, to_upper, cross = block_routes(count, distance)
        lower_part = grad_window[0, reach - distance]
        upper_part = grad_window[1, reach - distance]
        lower_grad = lower_grad + permute(lower_part, inverse(to_lower))
        keep_upper = jnp.where(fits_upper[distance], upper_part, 0.0)
        keep_cross = jnp.where(fits_upper[distance], 0.0, upper_part)
        upper_grad = upper_grad + permute(keep_upper, inverse(to_upper))
        lower_grad = lower_grad + permute(keep_cross, inverse(cross))
    grad_both = jnp.stack([lower_grad, upper_grad]).reshape(row_count, 2 * key_value_width)
    attended_rows = output_bf.reshape(row_count, QUERY_HEADS * HEAD_SIZE)
    query_rows = query_grad.astype(jnp.bfloat16).reshape(row_count, QUERY_HEADS * HEAD_SIZE)
    return (
        attended_rows,
        query_rows,
        grad_both[:, :key_value_width].astype(jnp.bfloat16),
        grad_both[:, key_value_width:].astype(jnp.bfloat16),
    )


def solution(mesh):
    return jax.shard_map(
        on_device,
        mesh=mesh,
        in_specs=(
            P(("groups", "ctx"), None),
            P(("groups", "ctx"), None),
            P(("groups", "ctx"), None),
            P(("groups", "ctx"), None),
            P("groups"),
        ),
        out_specs=(
            P(("groups", "ctx"), None),
            P(("groups", "ctx"), None),
            P(("groups", "ctx"), None),
            P(("groups", "ctx"), None),
        ),
        check_vma=False,
    )
```

```python
import math

import jax
import jax.numpy as jnp
from jax import lax
from jax.sharding import PartitionSpec as P

QUERY_HEADS = 16
KEY_VALUE_HEADS = 4
HEAD_SIZE = 128
DOCUMENT_REACH = 8

NEGATIVE_FLOOR = -1e30


def doc_number(lengths, places):
    doc_ends = jnp.cumsum(lengths)
    flat_places = places.reshape(-1)
    doc_hits = (doc_ends[None, :] <= flat_places[:, None]).astype(jnp.int32)
    return jnp.sum(doc_hits, axis=1).reshape(places.shape)


def permute(value, pairs):
    if not pairs:
        return jnp.zeros_like(value)
    return lax.ppermute(value, "ctx", pairs)


def block_routes(count, distance):
    lower_to_lower = [(s, s + distance) for s in range(count) if s + distance < count]
    upper_to_upper = [(s, s - distance) for s in range(count) if s - distance >= 0]
    lower_to_upper = [
        (s, 2 * count - 1 - s - distance)
        for s in range(count)
        if s + distance >= count and 2 * count - 1 - s - distance >= 0
    ]
    return lower_to_lower, upper_to_upper, lower_to_upper


def inverse(pairs):
    return [(d, s) for s, d in pairs]


def on_device(queries, key_rows, value_rows, output_gradient, lengths):
    count = lax.axis_size("ctx")
    my_index = lax.axis_index("ctx")
    row_count = queries.shape[0]
    block_rows = row_count // 2
    group_width = QUERY_HEADS // KEY_VALUE_HEADS
    key_value_width = KEY_VALUE_HEADS * HEAD_SIZE
    score_scale = 1.0 / math.sqrt(HEAD_SIZE)
    reach = DOCUMENT_REACH
    window = reach + 1

    own_blocks = jnp.stack([my_index, 2 * count - 1 - my_index])
    offsets = jnp.arange(block_rows, dtype=jnp.int32)
    query_place = own_blocks[:, None] * block_rows + offsets[None, :]
    key_block = own_blocks[:, None] - (reach - jnp.arange(window, dtype=jnp.int32))[None, :]
    key_place = (key_block[:, :, None] * block_rows + offsets[None, None, :]).reshape(2, -1)
    query_doc = doc_number(lengths, query_place)
    key_doc = doc_number(lengths, key_place)
    visible = (
        (query_doc[:, :, None] == key_doc[:, None, :])
        & (key_place[:, None, :] <= query_place[:, :, None])
        & (key_place[:, None, :] >= 0)
    )

    key_value = jnp.concatenate([key_rows, value_rows], axis=1)
    gathered = lax.all_gather(key_value, "ctx", axis=0, tiled=True).reshape(
        count, 2, block_rows, 2 * key_value_width
    )
    padded_kv = jnp.concatenate(
        [
            jnp.zeros((reach, block_rows, 2 * key_value_width), key_value.dtype),
            gathered[:, 0],
            gathered[::-1, 1],
        ]
    )
    window_kv = jnp.stack(
        [
            lax.dynamic_slice_in_dim(padded_kv, own_blocks[0], window, 0),
            lax.dynamic_slice_in_dim(padded_kv, own_blocks[1], window, 0),
        ]
    ).reshape(2, window * block_rows, 2 * key_value_width)
    key_tile = window_kv[..., :key_value_width].reshape(
        2, window * block_rows, KEY_VALUE_HEADS, HEAD_SIZE
    )
    value_tile = window_kv[..., key_value_width:].reshape(
        2, window * block_rows, KEY_VALUE_HEADS, HEAD_SIZE
    )

    query_tile = queries.reshape(2, block_rows, KEY_VALUE_HEADS, group_width, HEAD_SIZE)
    grad_tile = output_gradient.reshape(2, block_rows, KEY_VALUE_HEADS, group_width, HEAD_SIZE)
    mask = visible[:, None, None]

    scores = (
        jnp.einsum("aimgx,ajmx->amgij", query_tile, key_tile, preferred_element_type=jnp.float32)
        * score_scale
    )
    masked = jnp.where(mask, scores, NEGATIVE_FLOOR)
    row_maximum = jnp.max(masked, axis=-1)
    row_sum = jnp.sum(jnp.where(mask, jnp.exp(masked - row_maximum[..., None]), 0.0), axis=-1)
    log_norm = row_maximum + jnp.log(row_sum)
    probs = jnp.where(mask, jnp.exp(scores - log_norm[..., None]), 0.0)
    probs_b = probs.astype(jnp.bfloat16)
    attended = jnp.einsum(
        "amgij,ajmx->aimgx", probs_b, value_tile, preferred_element_type=jnp.float32
    )
    output_bf = attended.astype(jnp.bfloat16)
    delta_dot = jnp.einsum(
        "aimgx,aimgx->amgi", grad_tile, output_bf, preferred_element_type=jnp.float32
    )
    dprob = jnp.einsum(
        "aimgx,ajmx->amgij", grad_tile, value_tile, preferred_element_type=jnp.float32
    )
    dscore = (probs * (dprob - delta_dot[..., None])).astype(jnp.bfloat16)
    query_grad = (
        jnp.einsum("amgij,ajmx->aimgx", dscore, key_tile, preferred_element_type=jnp.float32)
        * score_scale
    )
    key_part = (
        jnp.einsum("amgij,aimgx->ajmx", dscore, query_tile, preferred_element_type=jnp.float32)
        * score_scale
    )
    value_part = jnp.einsum(
        "amgij,aimgx->ajmx", probs_b, grad_tile, preferred_element_type=jnp.float32
    )
    grad_window = jnp.concatenate(
        [
            key_part.reshape(2, window, block_rows, key_value_width),
            value_part.reshape(2, window, block_rows, key_value_width),
        ],
        axis=-1,
    )
    empty = jnp.zeros(
        (2 * count + reach, block_rows, 2 * key_value_width), jnp.float32
    )
    position_grad = lax.dynamic_update_slice_in_dim(
        empty, grad_window[0], own_blocks[0], 0
    ) + lax.dynamic_update_slice_in_dim(empty, grad_window[1], own_blocks[1], 0)
    position_grad = position_grad[reach:]
    storage_grad = jnp.stack(
        [position_grad[:count], position_grad[count:][::-1]], axis=1
    ).reshape(count * row_count, 2 * key_value_width)
    grad_both = lax.psum_scatter(storage_grad, "ctx", scatter_dimension=0, tiled=True)
    attended_rows = output_bf.reshape(row_count, QUERY_HEADS * HEAD_SIZE)
    query_rows = query_grad.astype(jnp.bfloat16).reshape(row_count, QUERY_HEADS * HEAD_SIZE)
    return (
        attended_rows,
        query_rows,
        grad_both[:, :key_value_width].astype(jnp.bfloat16),
        grad_both[:, key_value_width:].astype(jnp.bfloat16),
    )


def solution(mesh):
    return jax.shard_map(
        on_device,
        mesh=mesh,
        in_specs=(
            P(("groups", "ctx"), None),
            P(("groups", "ctx"), None),
            P(("groups", "ctx"), None),
            P(("groups", "ctx"), None),
            P("groups"),
        ),
        out_specs=(
            P(("groups", "ctx"), None),
            P(("groups", "ctx"), None),
            P(("groups", "ctx"), None),
            P(("groups", "ctx"), None),
        ),
        check_vma=False,
    )
```

```python
import math

import jax
import jax.numpy as jnp
import numpy as np
from jax import lax
from jax.experimental import pallas as pl
from jax.experimental.pallas import tpu as pltpu
from jax.sharding import PartitionSpec as P

QUERY_HEADS = 16
KEY_VALUE_HEADS = 4
HEAD_SIZE = 128
DOCUMENT_REACH = 8

NEGATIVE_FLOOR = -1e30


def block_home(count, block):
    if block < count:
        return block, 0
    return 2 * count - 1 - block, 1


def colored_moves(count, distance):
    edges = []
    for block in range(2 * count - distance):
        source, source_slot = block_home(count, block)
        target, target_slot = block_home(count, block + distance)
        edges.append((source, source_slot, target, target_slot))
    by_source, by_target = {}, {}
    for i, (s, _, t, _) in enumerate(edges):
        by_source.setdefault(s, []).append(i)
        by_target.setdefault(t, []).append(i)

    def partner(table, key, i):
        rest = [j for j in table[key] if j != i]
        return rest[0] if rest else None

    color = [None] * len(edges)

    def walk(i, through_target):
        while True:
            s, _, t, _ = edges[i]
            j = partner(by_target, t, i) if through_target else partner(by_source, s, i)
            if j is None or color[j] is not None:
                return
            color[j] = 1 - color[i]
            i, through_target = j, not through_target

    def degree(i):
        s, _, t, _ = edges[i]
        return min(len(by_source[s]), len(by_target[t]))

    for i in sorted(range(len(edges)), key=degree):
        if color[i] is None:
            color[i] = 0
            walk(i, True)
            walk(i, False)
    pairs = [[], []]
    send_slot = np.zeros((2, count), np.int32)
    receive_slot = np.full((2, count), -1, np.int32)
    for (s, ss, t, ts), c in zip(edges, color):
        pairs[c].append((s, t))
        send_slot[c, s] = ss
        receive_slot[c, t] = ts
    for c in range(2):
        assert len({s for s, _ in pairs[c]}) == len(pairs[c])
        assert len({t for _, t in pairs[c]}) == len(pairs[c])
    return pairs, send_slot, receive_slot


def permute(value, pairs):
    if not pairs:
        return jnp.zeros_like(value)
    return lax.ppermute(value, "ctx", pairs)


def prep_kernel(send_ref, key_ref, value_ref, own_ref, *pay_refs):
    both = jnp.concatenate([key_ref[...], value_ref[...]], axis=1)
    own_ref[...] = both
    rows = both.shape[0] // 2
    for n, pay_ref in enumerate(pay_refs):
        upper = send_ref[n] == 1

        @pl.when(upper)
        def _():
            pay_ref[...] = both[rows:]

        @pl.when(jnp.logical_not(upper))
        def _():
            pay_ref[...] = both[:rows]


def attention_kernel(
    meta_ref, ends_ref, query_ref, grad_ref, own_ref, *refs, count, reach, docs, scale
):
    moves = 2 * reach
    receive_refs = refs[:moves]
    out_ref, dquery_ref, own_grad_ref = refs[moves : moves + 3]
    pay_refs = refs[moves + 3 : 2 * moves + 3]
    window_ref = refs[2 * moves + 3]
    block_rows = own_ref.shape[0] // 2
    window = reach + 1
    group_width = QUERY_HEADS // KEY_VALUE_HEADS
    my_index = meta_ref[0]

    for n in range(moves):
        who = meta_ref[1 + n]

        @pl.when(who < 0)
        def _():
            pay_refs[n][...] = jnp.zeros(pay_refs[n].shape, jnp.float32)

    for slot in range(2):
        own_block = my_index if slot == 0 else 2 * count - 1 - my_index
        window_ref[reach * block_rows :, :] = own_ref[
            slot * block_rows : (slot + 1) * block_rows, :
        ]
        for distance in range(1, reach + 1):
            w = reach - distance
            first = meta_ref[1 + distance - 1] == slot
            second = meta_ref[1 + reach + distance - 1] == slot

            @pl.when(first)
            def _():
                window_ref[w * block_rows : (w + 1) * block_rows, :] = receive_refs[
                    distance - 1
                ][...]

            @pl.when(jnp.logical_and(second, jnp.logical_not(first)))
            def _():
                window_ref[w * block_rows : (w + 1) * block_rows, :] = receive_refs[
                    reach + distance - 1
                ][...]

            @pl.when(jnp.logical_and(jnp.logical_not(second), jnp.logical_not(first)))
            def _():
                window_ref[w * block_rows : (w + 1) * block_rows, :] = jnp.zeros(
                    (block_rows, window_ref.shape[1]), window_ref.dtype
                )

        query_place = own_block * block_rows + lax.broadcasted_iota(
            jnp.int32, (block_rows, window * block_rows), 0
        )
        key_place = (own_block - reach) * block_rows + lax.broadcasted_iota(
            jnp.int32, (block_rows, window * block_rows), 1
        )
        query_doc = jnp.zeros((block_rows, window * block_rows), jnp.int32)
        key_doc = jnp.zeros((block_rows, window * block_rows), jnp.int32)
        for j in range(docs):
            end = ends_ref[j]
            query_doc = query_doc + (query_place >= end).astype(jnp.int32)
            key_doc = key_doc + (key_place >= end).astype(jnp.int32)
        visible = (query_doc == key_doc) & (key_place <= query_place) & (key_place >= 0)
        mask = jnp.concatenate([visible] * group_width, axis=0)

        rows = slice(slot * block_rows, (slot + 1) * block_rows)
        query = jnp.concatenate(
            [query_ref[rows, g * HEAD_SIZE : (g + 1) * HEAD_SIZE] for g in range(group_width)],
            axis=0,
        )
        grad = jnp.concatenate(
            [grad_ref[rows, g * HEAD_SIZE : (g + 1) * HEAD_SIZE] for g in range(group_width)],
            axis=0,
        )
        keys = window_ref[:, :HEAD_SIZE]
        values = window_ref[:, HEAD_SIZE:]
        contract_last = (((1,), (1,)), ((), ()))
        contract_first = (((0,), (0,)), ((), ()))
        scores = (
            lax.dot_general(query, keys, contract_last, preferred_element_type=jnp.float32)
            * scale
        )
        masked = jnp.where(mask, scores, NEGATIVE_FLOOR)
        row_maximum = jnp.max(masked, axis=1, keepdims=True)
        row_sum = jnp.sum(
            jnp.where(mask, jnp.exp(masked - row_maximum), 0.0), axis=1, keepdims=True
        )
        log_norm = row_maximum + jnp.log(row_sum)
        probs = jnp.where(mask, jnp.exp(scores - log_norm), 0.0)
        probs_b = probs.astype(jnp.bfloat16)
        attended = jnp.dot(probs_b, values, preferred_element_type=jnp.float32)
        attended_b = attended.astype(jnp.bfloat16)
        delta = jnp.sum(
            grad.astype(jnp.float32) * attended_b.astype(jnp.float32), axis=1, keepdims=True
        )
        dprob = lax.dot_general(grad, values, contract_last, preferred_element_type=jnp.float32)
        dscore = (probs * (dprob - delta)).astype(jnp.bfloat16)
        dquery = jnp.dot(dscore, keys, preferred_element_type=jnp.float32) * scale
        dkey = (
            lax.dot_general(dscore, query, contract_first, preferred_element_type=jnp.float32)
            * scale
        )
        dvalue = lax.dot_general(
            probs_b, grad, contract_first, preferred_element_type=jnp.float32
        )
        dquery_b = dquery.astype(jnp.bfloat16)
        for g in range(group_width):
            cols = slice(g * HEAD_SIZE, (g + 1) * HEAD_SIZE)
            out_ref[rows, cols] = attended_b[g * block_rows : (g + 1) * block_rows]
            dquery_ref[rows, cols] = dquery_b[g * block_rows : (g + 1) * block_rows]
        own_grad_ref[rows, :HEAD_SIZE] = dkey[reach * block_rows :]
        own_grad_ref[rows, HEAD_SIZE:] = dvalue[reach * block_rows :]
        for n in range(moves):
            distance = n % reach + 1
            w = reach - distance
            part = slice(w * block_rows, (w + 1) * block_rows)

            @pl.when(meta_ref[1 + n] == slot)
            def _():
                pay_refs[n][:, :HEAD_SIZE] = dkey[part]
                pay_refs[n][:, HEAD_SIZE:] = dvalue[part]


def on_device(queries, key_rows, value_rows, output_gradient, lengths):
    count = lax.axis_size("ctx")
    my_index = lax.axis_index("ctx")
    row_count = queries.shape[0]
    block_rows = row_count // 2
    pair_width = 2 * HEAD_SIZE
    reach = DOCUMENT_REACH
    moves = 2 * reach
    docs = lengths.shape[0]
    score_scale = 1.0 / math.sqrt(HEAD_SIZE)

    routes = [colored_moves(count, distance) for distance in range(1, reach + 1)]
    move_pairs = [routes[n % reach][0][n // reach] for n in range(moves)]
    send_table = np.stack([routes[n % reach][1][n // reach] for n in range(moves)], axis=1)
    receive_table = np.stack(
        [routes[n % reach][2][n // reach] for n in range(moves)], axis=1
    )
    send_slot = jnp.asarray(send_table)[my_index]
    receive_slot = jnp.asarray(receive_table)[my_index]
    doc_ends = jnp.cumsum(lengths).astype(jnp.int32)

    kv_spec = pl.BlockSpec((row_count, HEAD_SIZE), lambda m, *_: (0, m))
    pair_spec = pl.BlockSpec((row_count, pair_width), lambda m, *_: (0, m))
    move_spec = pl.BlockSpec((block_rows, pair_width), lambda m, *_: (0, m))
    prep = pl.pallas_call(
        prep_kernel,
        grid_spec=pltpu.PrefetchScalarGridSpec(
            num_scalar_prefetch=1,
            grid=(KEY_VALUE_HEADS,),
            in_specs=[kv_spec, kv_spec],
            out_specs=[pair_spec] + [move_spec] * moves,
        ),
        out_shape=[jax.ShapeDtypeStruct((row_count, KEY_VALUE_HEADS * pair_width), jnp.bfloat16)]
        + [jax.ShapeDtypeStruct((block_rows, KEY_VALUE_HEADS * pair_width), jnp.bfloat16)]
        * moves,
    )
    own_kv, *payloads = prep(send_slot, key_rows, value_rows)
    received = [permute(payloads[n], move_pairs[n]) for n in range(moves)]

    head_group = QUERY_HEADS // KEY_VALUE_HEADS * HEAD_SIZE
    query_spec = pl.BlockSpec((row_count, head_group), lambda m, *_: (0, m))
    meta = jnp.concatenate([my_index.reshape(1).astype(jnp.int32), receive_slot])
    kernel = pl.pallas_call(
        lambda *refs: attention_kernel(
            *refs, count=count, reach=reach, docs=docs, scale=score_scale
        ),
        grid_spec=pltpu.PrefetchScalarGridSpec(
            num_scalar_prefetch=2,
            grid=(KEY_VALUE_HEADS,),
            in_specs=[query_spec, query_spec, pair_spec] + [move_spec] * moves,
            out_specs=[query_spec, query_spec, pair_spec] + [move_spec] * moves,
            scratch_shapes=[pltpu.VMEM(((reach + 1) * block_rows, pair_width), jnp.bfloat16)],
        ),
        out_shape=[
            jax.ShapeDtypeStruct(queries.shape, jnp.bfloat16),
            jax.ShapeDtypeStruct(queries.shape, jnp.bfloat16),
            jax.ShapeDtypeStruct((row_count, KEY_VALUE_HEADS * pair_width), jnp.float32),
        ]
        + [jax.ShapeDtypeStruct((block_rows, KEY_VALUE_HEADS * pair_width), jnp.float32)]
        * moves,
    )
    attended, query_grad, own_grad, *returns = kernel(
        meta, doc_ends, queries, output_gradient, own_kv, *received
    )
    lower_grad = own_grad[:block_rows]
    upper_grad = own_grad[block_rows:]
    for n in range(moves):
        back = permute(returns[n], [(t, s) for s, t in move_pairs[n]])
        lower_grad = lower_grad + jnp.where(send_slot[n] == 0, back, 0.0)
        upper_grad = upper_grad + jnp.where(send_slot[n] == 1, back, 0.0)
    grad_both = jnp.concatenate([lower_grad, upper_grad]).reshape(
        row_count, KEY_VALUE_HEADS, 2, HEAD_SIZE
    )
    key_width = KEY_VALUE_HEADS * HEAD_SIZE
    return (
        attended,
        query_grad,
        grad_both[:, :, 0].reshape(row_count, key_width).astype(jnp.bfloat16),
        grad_both[:, :, 1].reshape(row_count, key_width).astype(jnp.bfloat16),
    )


def solution(mesh):
    return jax.shard_map(
        on_device,
        mesh=mesh,
        in_specs=(
            P(("groups", "ctx"), None),
            P(("groups", "ctx"), None),
            P(("groups", "ctx"), None),
            P(("groups", "ctx"), None),
            P("groups"),
        ),
        out_specs=(
            P(("groups", "ctx"), None),
            P(("groups", "ctx"), None),
            P(("groups", "ctx"), None),
            P(("groups", "ctx"), None),
        ),
        check_vma=False,
    )
```

```python
import math

import jax
import jax.numpy as jnp
import numpy as np
from jax import lax
from jax.experimental import pallas as pl
from jax.experimental.pallas import tpu as pltpu
from jax.sharding import PartitionSpec as P

QUERY_HEADS = 16
KEY_VALUE_HEADS = 4
HEAD_SIZE = 128
DOCUMENT_REACH = 8

NEGATIVE_FLOOR = -1e30


def block_home(count, block):
    if block < count:
        return block, 0
    return 2 * count - 1 - block, 1


def colored_moves(count, distance):
    edges = []
    for block in range(2 * count - distance):
        source, source_slot = block_home(count, block)
        target, target_slot = block_home(count, block + distance)
        edges.append((source, source_slot, target, target_slot))
    by_source, by_target = {}, {}
    for i, (s, _, t, _) in enumerate(edges):
        by_source.setdefault(s, []).append(i)
        by_target.setdefault(t, []).append(i)

    def partner(table, key, i):
        rest = [j for j in table[key] if j != i]
        return rest[0] if rest else None

    color = [None] * len(edges)

    def walk(i, through_target):
        while True:
            s, _, t, _ = edges[i]
            j = partner(by_target, t, i) if through_target else partner(by_source, s, i)
            if j is None or color[j] is not None:
                return
            color[j] = 1 - color[i]
            i, through_target = j, not through_target

    def degree(i):
        s, _, t, _ = edges[i]
        return min(len(by_source[s]), len(by_target[t]))

    for i in sorted(range(len(edges)), key=degree):
        if color[i] is None:
            color[i] = 0
            walk(i, True)
            walk(i, False)
    pairs = [[], []]
    send_slot = np.zeros((2, count), np.int32)
    receive_slot = np.full((2, count), -1, np.int32)
    for (s, ss, t, ts), c in zip(edges, color):
        pairs[c].append((s, t))
        send_slot[c, s] = ss
        receive_slot[c, t] = ts
    for c in range(2):
        assert len({s for s, _ in pairs[c]}) == len(pairs[c])
        assert len({t for _, t in pairs[c]}) == len(pairs[c])
    return pairs, send_slot, receive_slot


def permute(value, pairs):
    if not pairs:
        return jnp.zeros_like(value)
    return lax.ppermute(value, "ctx", pairs)


def prep_kernel(send_ref, key_ref, value_ref, own_ref, *pay_refs):
    both = jnp.concatenate([key_ref[...], value_ref[...]], axis=1)
    own_ref[...] = both
    rows = both.shape[0] // 2
    for n, pay_ref in enumerate(pay_refs):
        upper = send_ref[n] == 1

        @pl.when(upper)
        def _():
            pay_ref[...] = both[rows:]

        @pl.when(jnp.logical_not(upper))
        def _():
            pay_ref[...] = both[:rows]


def attention_kernel(
    meta_ref, ends_ref, query_ref, grad_ref, own_ref, *refs, count, reach, docs, scale
):
    moves = 2 * reach
    receive_refs = refs[:moves]
    out_ref, dquery_ref, own_grad_ref = refs[moves : moves + 3]
    pay_refs = refs[moves + 3 : 2 * moves + 3]
    window_ref = refs[2 * moves + 3]
    block_rows = own_ref.shape[0] // 2
    window = reach + 1
    group_width = QUERY_HEADS // KEY_VALUE_HEADS
    my_index = meta_ref[0]

    for n in range(moves):
        who = meta_ref[1 + n]

        @pl.when(who < 0)
        def _():
            pay_refs[n][...] = jnp.zeros(pay_refs[n].shape, pay_refs[n].dtype)

    for slot in range(2):
        own_block = my_index if slot == 0 else 2 * count - 1 - my_index
        window_ref[reach * block_rows :, :] = own_ref[
            slot * block_rows : (slot + 1) * block_rows, :
        ]
        for distance in range(1, reach + 1):
            w = reach - distance
            first = meta_ref[1 + distance - 1] == slot
            second = meta_ref[1 + reach + distance - 1] == slot

            @pl.when(first)
            def _():
                window_ref[w * block_rows : (w + 1) * block_rows, :] = receive_refs[
                    distance - 1
                ][...]

            @pl.when(jnp.logical_and(second, jnp.logical_not(first)))
            def _():
                window_ref[w * block_rows : (w + 1) * block_rows, :] = receive_refs[
                    reach + distance - 1
                ][...]

            @pl.when(jnp.logical_and(jnp.logical_not(second), jnp.logical_not(first)))
            def _():
                window_ref[w * block_rows : (w + 1) * block_rows, :] = jnp.zeros(
                    (block_rows, window_ref.shape[1]), window_ref.dtype
                )

        query_place = own_block * block_rows + lax.broadcasted_iota(
            jnp.int32, (block_rows, window * block_rows), 0
        )
        key_place = (own_block - reach) * block_rows + lax.broadcasted_iota(
            jnp.int32, (block_rows, window * block_rows), 1
        )
        query_doc = jnp.zeros((block_rows, window * block_rows), jnp.int32)
        key_doc = jnp.zeros((block_rows, window * block_rows), jnp.int32)
        for j in range(docs):
            end = ends_ref[j]
            query_doc = query_doc + (query_place >= end).astype(jnp.int32)
            key_doc = key_doc + (key_place >= end).astype(jnp.int32)
        visible = (query_doc == key_doc) & (key_place <= query_place) & (key_place >= 0)
        mask = jnp.concatenate([visible] * group_width, axis=0)

        rows = slice(slot * block_rows, (slot + 1) * block_rows)
        query = jnp.concatenate(
            [query_ref[rows, g * HEAD_SIZE : (g + 1) * HEAD_SIZE] for g in range(group_width)],
            axis=0,
        )
        grad = jnp.concatenate(
            [grad_ref[rows, g * HEAD_SIZE : (g + 1) * HEAD_SIZE] for g in range(group_width)],
            axis=0,
        )
        keys = window_ref[:, :HEAD_SIZE]
        values = window_ref[:, HEAD_SIZE:]
        contract_last = (((1,), (1,)), ((), ()))
        contract_first = (((0,), (0,)), ((), ()))
        scores = (
            lax.dot_general(query, keys, contract_last, preferred_element_type=jnp.float32)
            * scale
        )
        masked = jnp.where(mask, scores, NEGATIVE_FLOOR)
        row_maximum = jnp.max(masked, axis=1, keepdims=True)
        row_sum = jnp.sum(
            jnp.where(mask, jnp.exp(masked - row_maximum), 0.0), axis=1, keepdims=True
        )
        log_norm = row_maximum + jnp.log(row_sum)
        probs = jnp.where(mask, jnp.exp(scores - log_norm), 0.0)
        probs_b = probs.astype(jnp.bfloat16)
        attended = jnp.dot(probs_b, values, preferred_element_type=jnp.float32)
        attended_b = attended.astype(jnp.bfloat16)
        delta = jnp.sum(
            grad.astype(jnp.float32) * attended_b.astype(jnp.float32), axis=1, keepdims=True
        )
        dprob = lax.dot_general(grad, values, contract_last, preferred_element_type=jnp.float32)
        dscore = (probs * (dprob - delta)).astype(jnp.bfloat16)
        dquery = jnp.dot(dscore, keys, preferred_element_type=jnp.float32) * scale
        dkey = (
            lax.dot_general(dscore, query, contract_first, preferred_element_type=jnp.float32)
            * scale
        )
        dvalue = lax.dot_general(
            probs_b, grad, contract_first, preferred_element_type=jnp.float32
        )
        dquery_b = dquery.astype(jnp.bfloat16)
        for g in range(group_width):
            cols = slice(g * HEAD_SIZE, (g + 1) * HEAD_SIZE)
            out_ref[rows, cols] = attended_b[g * block_rows : (g + 1) * block_rows]
            dquery_ref[rows, cols] = dquery_b[g * block_rows : (g + 1) * block_rows]
        own_grad_ref[rows, :HEAD_SIZE] = dkey[reach * block_rows :]
        own_grad_ref[rows, HEAD_SIZE:] = dvalue[reach * block_rows :]
        for n in range(moves):
            distance = n % reach + 1
            w = reach - distance
            part = slice(w * block_rows, (w + 1) * block_rows)

            @pl.when(meta_ref[1 + n] == slot)
            def _():
                pay_refs[n][:, :HEAD_SIZE] = dkey[part].astype(pay_refs[n].dtype)
                pay_refs[n][:, HEAD_SIZE:] = dvalue[part].astype(pay_refs[n].dtype)


def on_device(queries, key_rows, value_rows, output_gradient, lengths):
    count = lax.axis_size("ctx")
    my_index = lax.axis_index("ctx")
    row_count = queries.shape[0]
    block_rows = row_count // 2
    pair_width = 2 * HEAD_SIZE
    reach = DOCUMENT_REACH
    moves = 2 * reach
    docs = lengths.shape[0]
    score_scale = 1.0 / math.sqrt(HEAD_SIZE)

    routes = [colored_moves(count, distance) for distance in range(1, reach + 1)]
    move_pairs = [routes[n % reach][0][n // reach] for n in range(moves)]
    send_table = np.stack([routes[n % reach][1][n // reach] for n in range(moves)], axis=1)
    receive_table = np.stack(
        [routes[n % reach][2][n // reach] for n in range(moves)], axis=1
    )
    send_slot = jnp.asarray(send_table)[my_index]
    receive_slot = jnp.asarray(receive_table)[my_index]
    doc_ends = jnp.cumsum(lengths).astype(jnp.int32)

    kv_spec = pl.BlockSpec((row_count, HEAD_SIZE), lambda m, *_: (0, m))
    pair_spec = pl.BlockSpec((row_count, pair_width), lambda m, *_: (0, m))
    move_spec = pl.BlockSpec((block_rows, pair_width), lambda m, *_: (0, m))
    prep = pl.pallas_call(
        prep_kernel,
        grid_spec=pltpu.PrefetchScalarGridSpec(
            num_scalar_prefetch=1,
            grid=(KEY_VALUE_HEADS,),
            in_specs=[kv_spec, kv_spec],
            out_specs=[pair_spec] + [move_spec] * moves,
        ),
        out_shape=[jax.ShapeDtypeStruct((row_count, KEY_VALUE_HEADS * pair_width), jnp.bfloat16)]
        + [jax.ShapeDtypeStruct((block_rows, KEY_VALUE_HEADS * pair_width), jnp.bfloat16)]
        * moves,
    )
    own_kv, *payloads = prep(send_slot, key_rows, value_rows)
    received = [permute(payloads[n], move_pairs[n]) for n in range(moves)]

    head_group = QUERY_HEADS // KEY_VALUE_HEADS * HEAD_SIZE
    query_spec = pl.BlockSpec((row_count, head_group), lambda m, *_: (0, m))
    meta = jnp.concatenate([my_index.reshape(1).astype(jnp.int32), receive_slot])
    kernel = pl.pallas_call(
        lambda *refs: attention_kernel(
            *refs, count=count, reach=reach, docs=docs, scale=score_scale
        ),
        grid_spec=pltpu.PrefetchScalarGridSpec(
            num_scalar_prefetch=2,
            grid=(KEY_VALUE_HEADS,),
            in_specs=[query_spec, query_spec, pair_spec] + [move_spec] * moves,
            out_specs=[query_spec, query_spec, pair_spec] + [move_spec] * moves,
            scratch_shapes=[pltpu.VMEM(((reach + 1) * block_rows, pair_width), jnp.bfloat16)],
        ),
        out_shape=[
            jax.ShapeDtypeStruct(queries.shape, jnp.bfloat16),
            jax.ShapeDtypeStruct(queries.shape, jnp.bfloat16),
            jax.ShapeDtypeStruct((row_count, KEY_VALUE_HEADS * pair_width), jnp.float32),
        ]
        + [jax.ShapeDtypeStruct((block_rows, KEY_VALUE_HEADS * pair_width), jnp.bfloat16)]
        * moves,
    )
    attended, query_grad, own_grad, *returns = kernel(
        meta, doc_ends, queries, output_gradient, own_kv, *received
    )
    lower_grad = own_grad[:block_rows]
    upper_grad = own_grad[block_rows:]
    for n in range(moves):
        back = permute(returns[n], [(t, s) for s, t in move_pairs[n]]).astype(jnp.float32)
        lower_grad = lower_grad + jnp.where(send_slot[n] == 0, back, 0.0)
        upper_grad = upper_grad + jnp.where(send_slot[n] == 1, back, 0.0)
    grad_both = jnp.concatenate([lower_grad, upper_grad]).reshape(
        row_count, KEY_VALUE_HEADS, 2, HEAD_SIZE
    )
    key_width = KEY_VALUE_HEADS * HEAD_SIZE
    return (
        attended,
        query_grad,
        grad_both[:, :, 0].reshape(row_count, key_width).astype(jnp.bfloat16),
        grad_both[:, :, 1].reshape(row_count, key_width).astype(jnp.bfloat16),
    )


def solution(mesh):
    return jax.shard_map(
        on_device,
        mesh=mesh,
        in_specs=(
            P(("groups", "ctx"), None),
            P(("groups", "ctx"), None),
            P(("groups", "ctx"), None),
            P(("groups", "ctx"), None),
            P("groups"),
        ),
        out_specs=(
            P(("groups", "ctx"), None),
            P(("groups", "ctx"), None),
            P(("groups", "ctx"), None),
            P(("groups", "ctx"), None),
        ),
        check_vma=False,
    )
```

```python
import math

import jax
import jax.numpy as jnp
import numpy as np
from jax import lax
from jax.experimental import pallas as pl
from jax.experimental.pallas import tpu as pltpu
from jax.sharding import PartitionSpec as P

QUERY_HEADS = 16
KEY_VALUE_HEADS = 4
HEAD_SIZE = 128
DOCUMENT_REACH = 8

NEGATIVE_FLOOR = -1e30


def block_home(count, block):
    if block < count:
        return block, 0
    return 2 * count - 1 - block, 1


def colored_moves(count, distance):
    edges = []
    for block in range(2 * count - distance):
        source, source_slot = block_home(count, block)
        target, target_slot = block_home(count, block + distance)
        edges.append((source, source_slot, target, target_slot))
    by_source, by_target = {}, {}
    for i, (s, _, t, _) in enumerate(edges):
        by_source.setdefault(s, []).append(i)
        by_target.setdefault(t, []).append(i)

    def partner(table, key, i):
        rest = [j for j in table[key] if j != i]
        return rest[0] if rest else None

    color = [None] * len(edges)

    def walk(i, through_target):
        while True:
            s, _, t, _ = edges[i]
            j = partner(by_target, t, i) if through_target else partner(by_source, s, i)
            if j is None or color[j] is not None:
                return
            color[j] = 1 - color[i]
            i, through_target = j, not through_target

    def degree(i):
        s, _, t, _ = edges[i]
        return min(len(by_source[s]), len(by_target[t]))

    for i in sorted(range(len(edges)), key=degree):
        if color[i] is None:
            color[i] = 0
            walk(i, True)
            walk(i, False)
    pairs = [[], []]
    send_slot = np.zeros((2, count), np.int32)
    receive_slot = np.full((2, count), -1, np.int32)
    for (s, ss, t, ts), c in zip(edges, color):
        pairs[c].append((s, t))
        send_slot[c, s] = ss
        receive_slot[c, t] = ts
    for c in range(2):
        assert len({s for s, _ in pairs[c]}) == len(pairs[c])
        assert len({t for _, t in pairs[c]}) == len(pairs[c])
    return pairs, send_slot, receive_slot


def permute(value, pairs):
    if not pairs:
        return jnp.zeros_like(value)
    return lax.ppermute(value, "ctx", pairs)


def prep_kernel(send_ref, key_ref, value_ref, own_ref, *pay_refs):
    both = jnp.concatenate([key_ref[...], value_ref[...]], axis=1)
    own_ref[...] = both
    rows = both.shape[0] // 2
    for n, pay_ref in enumerate(pay_refs):
        upper = send_ref[n] == 1

        @pl.when(upper)
        def _():
            pay_ref[...] = both[rows:]

        @pl.when(jnp.logical_not(upper))
        def _():
            pay_ref[...] = both[:rows]


def attention_kernel(
    meta_ref, ends_ref, query_ref, grad_ref, own_ref, *refs, count, reach, hop, docs, scale
):
    near = 2 * hop
    near_refs = refs[:near]
    far_refs = refs[near : near + 2]
    out_ref, dquery_ref, part_ref = refs[near + 2 : near + 5]
    window_ref = refs[near + 5]
    block_rows = own_ref.shape[0] // 2
    window = reach + 1
    span = window * block_rows
    group_width = QUERY_HEADS // KEY_VALUE_HEADS
    my_index = meta_ref[0]

    def fill(w, first, second, first_ref, second_ref, rows):
        @pl.when(first)
        def _():
            window_ref[w * block_rows : (w + 1) * block_rows, :] = first_ref[rows, :]

        @pl.when(jnp.logical_and(second, jnp.logical_not(first)))
        def _():
            window_ref[w * block_rows : (w + 1) * block_rows, :] = second_ref[rows, :]

        @pl.when(jnp.logical_and(jnp.logical_not(second), jnp.logical_not(first)))
        def _():
            window_ref[w * block_rows : (w + 1) * block_rows, :] = jnp.zeros(
                (block_rows, window_ref.shape[1]), window_ref.dtype
            )

    for slot in range(2):
        own_block = my_index if slot == 0 else 2 * count - 1 - my_index
        window_ref[reach * block_rows :, :] = own_ref[
            slot * block_rows : (slot + 1) * block_rows, :
        ]
        for distance in range(1, hop + 1):
            fill(
                reach - distance,
                meta_ref[distance] == slot,
                meta_ref[hop + distance] == slot,
                near_refs[distance - 1],
                near_refs[hop + distance - 1],
                slice(0, block_rows),
            )
        for k in range(hop):
            fill(
                reach - hop - 1 - k,
                meta_ref[1 + near] == slot,
                meta_ref[2 + near] == slot,
                far_refs[0],
                far_refs[1],
                slice(k * block_rows, (k + 1) * block_rows),
            )

        query_place = own_block * block_rows + lax.broadcasted_iota(
            jnp.int32, (block_rows, span), 0
        )
        key_place = (own_block - reach) * block_rows + lax.broadcasted_iota(
            jnp.int32, (block_rows, span), 1
        )
        query_doc = jnp.zeros((block_rows, span), jnp.int32)
        key_doc = jnp.zeros((block_rows, span), jnp.int32)
        for j in range(docs):
            end = ends_ref[j]
            query_doc = query_doc + (query_place >= end).astype(jnp.int32)
            key_doc = key_doc + (key_place >= end).astype(jnp.int32)
        visible = (query_doc == key_doc) & (key_place <= query_place) & (key_place >= 0)
        mask = jnp.concatenate([visible] * group_width, axis=0)

        rows = slice(slot * block_rows, (slot + 1) * block_rows)
        query = jnp.concatenate(
            [query_ref[rows, g * HEAD_SIZE : (g + 1) * HEAD_SIZE] for g in range(group_width)],
            axis=0,
        )
        grad = jnp.concatenate(
            [grad_ref[rows, g * HEAD_SIZE : (g + 1) * HEAD_SIZE] for g in range(group_width)],
            axis=0,
        )
        keys = window_ref[:, :HEAD_SIZE]
        values = window_ref[:, HEAD_SIZE:]
        contract_last = (((1,), (1,)), ((), ()))
        contract_first = (((0,), (0,)), ((), ()))
        scores = (
            lax.dot_general(query, keys, contract_last, preferred_element_type=jnp.float32)
            * scale
        )
        masked = jnp.where(mask, scores, NEGATIVE_FLOOR)
        row_maximum = jnp.max(masked, axis=1, keepdims=True)
        row_sum = jnp.sum(
            jnp.where(mask, jnp.exp(masked - row_maximum), 0.0), axis=1, keepdims=True
        )
        log_norm = row_maximum + jnp.log(row_sum)
        probs = jnp.where(mask, jnp.exp(scores - log_norm), 0.0)
        probs_b = probs.astype(jnp.bfloat16)
        attended = jnp.dot(probs_b, values, preferred_element_type=jnp.float32)
        attended_b = attended.astype(jnp.bfloat16)
        delta = jnp.sum(
            grad.astype(jnp.float32) * attended_b.astype(jnp.float32), axis=1, keepdims=True
        )
        dprob = lax.dot_general(grad, values, contract_last, preferred_element_type=jnp.float32)
        dscore = (probs * (dprob - delta)).astype(jnp.bfloat16)
        dquery = jnp.dot(dscore, keys, preferred_element_type=jnp.float32) * scale
        dkey = (
            lax.dot_general(dscore, query, contract_first, preferred_element_type=jnp.float32)
            * scale
        )
        dvalue = lax.dot_general(
            probs_b, grad, contract_first, preferred_element_type=jnp.float32
        )
        dquery_b = dquery.astype(jnp.bfloat16)
        for g in range(group_width):
            cols = slice(g * HEAD_SIZE, (g + 1) * HEAD_SIZE)
            out_ref[rows, cols] = attended_b[g * block_rows : (g + 1) * block_rows]
            dquery_ref[rows, cols] = dquery_b[g * block_rows : (g + 1) * block_rows]
        part_ref[slot * span : (slot + 1) * span, :HEAD_SIZE] = dkey
        part_ref[slot * span : (slot + 1) * span, HEAD_SIZE:] = dvalue


def on_device(queries, key_rows, value_rows, output_gradient, lengths):
    count = lax.axis_size("ctx")
    my_index = lax.axis_index("ctx")
    row_count = queries.shape[0]
    block_rows = row_count // 2
    pair_width = 2 * HEAD_SIZE
    width = KEY_VALUE_HEADS * pair_width
    reach = DOCUMENT_REACH
    hop = reach // 2
    near = 2 * hop
    window = reach + 1
    span = window * block_rows
    docs = lengths.shape[0]
    score_scale = 1.0 / math.sqrt(HEAD_SIZE)

    routes = [colored_moves(count, distance) for distance in range(1, hop + 1)]
    near_pairs = [routes[n % hop][0][n // hop] for n in range(near)]
    near_send = jnp.asarray(
        np.stack([routes[n % hop][1][n // hop] for n in range(near)], axis=1)
    )[my_index]
    near_receive = jnp.asarray(
        np.stack([routes[n % hop][2][n // hop] for n in range(near)], axis=1)
    )[my_index]
    far_pairs, far_send_table, far_receive_table = colored_moves(count, hop)
    far_send = jnp.asarray(far_send_table.T)[my_index]
    far_receive = jnp.asarray(far_receive_table.T)[my_index]
    doc_ends = jnp.cumsum(lengths).astype(jnp.int32)

    kv_spec = pl.BlockSpec((row_count, HEAD_SIZE), lambda m, *_: (0, m))
    pair_spec = pl.BlockSpec((row_count, pair_width), lambda m, *_: (0, m))
    move_spec = pl.BlockSpec((block_rows, pair_width), lambda m, *_: (0, m))
    run_spec = pl.BlockSpec((hop * block_rows, pair_width), lambda m, *_: (0, m))
    prep = pl.pallas_call(
        prep_kernel,
        grid_spec=pltpu.PrefetchScalarGridSpec(
            num_scalar_prefetch=1,
            grid=(KEY_VALUE_HEADS,),
            in_specs=[kv_spec, kv_spec],
            out_specs=[pair_spec] + [move_spec] * near,
        ),
        out_shape=[jax.ShapeDtypeStruct((row_count, width), jnp.bfloat16)]
        + [jax.ShapeDtypeStruct((block_rows, width), jnp.bfloat16)] * near,
    )
    own_kv, *payloads = prep(near_send, key_rows, value_rows)
    received = [permute(payloads[n], near_pairs[n]) for n in range(near)]

    def near_block(slot, distance):
        first = received[distance - 1]
        second = received[hop + distance - 1]
        return jnp.where(near_receive[distance - 1] == slot, first, second)

    runs = [
        jnp.concatenate([near_block(slot, d) for d in range(1, hop + 1)]) for slot in range(2)
    ]
    far_received = [
        permute(jnp.where(far_send[c] == 1, runs[1], runs[0]), far_pairs[c]) for c in range(2)
    ]

    head_group = QUERY_HEADS // KEY_VALUE_HEADS * HEAD_SIZE
    query_spec = pl.BlockSpec((row_count, head_group), lambda m, *_: (0, m))
    part_spec = pl.BlockSpec((2 * span, pair_width), lambda m, *_: (0, m))
    meta = jnp.concatenate([my_index.reshape(1).astype(jnp.int32), near_receive, far_receive])
    kernel = pl.pallas_call(
        lambda *refs: attention_kernel(
            *refs, count=count, reach=reach, hop=hop, docs=docs, scale=score_scale
        ),
        grid_spec=pltpu.PrefetchScalarGridSpec(
            num_scalar_prefetch=2,
            grid=(KEY_VALUE_HEADS,),
            in_specs=[query_spec, query_spec, pair_spec] + [move_spec] * near + [run_spec] * 2,
            out_specs=[query_spec, query_spec, part_spec],
            scratch_shapes=[pltpu.VMEM((span, pair_width), jnp.bfloat16)],
        ),
        out_shape=[
            jax.ShapeDtypeStruct(queries.shape, jnp.bfloat16),
            jax.ShapeDtypeStruct(queries.shape, jnp.bfloat16),
            jax.ShapeDtypeStruct((2 * span, width), jnp.float32),
        ],
    )
    attended, query_grad, part = kernel(
        meta, doc_ends, queries, output_gradient, own_kv, *received, *far_received
    )
    part = part.reshape(2, window, block_rows, width)

    far_back = []
    for c in range(2):
        run = [
            jnp.where(far_receive[c] == 1, part[1, reach - hop - 1 - k], part[0, reach - hop - 1 - k])
            for k in range(hop)
        ]
        payload = jnp.concatenate(run).astype(jnp.bfloat16)
        far_back.append(
            permute(payload, [(t, s) for s, t in far_pairs[c]]).astype(jnp.float32)
        )

    def relayed(slot, distance):
        rows = slice((distance - 1) * block_rows, distance * block_rows)
        total = jnp.where(far_send[0] == slot, far_back[0][rows], 0.0)
        return total + jnp.where(far_send[1] == slot, far_back[1][rows], 0.0)

    lower_grad = part[0, reach]
    upper_grad = part[1, reach]
    for n in range(near):
        distance = n % hop + 1
        w = reach - distance
        slot_is_upper = near_receive[n] == 1
        value = jnp.where(slot_is_upper, part[1, w], part[0, w]) + jnp.where(
            slot_is_upper, relayed(1, distance), relayed(0, distance)
        )
        back = permute(value.astype(jnp.bfloat16), [(t, s) for s, t in near_pairs[n]])
        back = back.astype(jnp.float32)
        lower_grad = lower_grad + jnp.where(near_send[n] == 0, back, 0.0)
        upper_grad = upper_grad + jnp.where(near_send[n] == 1, back, 0.0)
    grad_both = jnp.concatenate([lower_grad, upper_grad]).reshape(
        row_count, KEY_VALUE_HEADS, 2, HEAD_SIZE
    )
    key_width = KEY_VALUE_HEADS * HEAD_SIZE
    return (
        attended,
        query_grad,
        grad_both[:, :, 0].reshape(row_count, key_width).astype(jnp.bfloat16),
        grad_both[:, :, 1].reshape(row_count, key_width).astype(jnp.bfloat16),
    )


def solution(mesh):
    return jax.shard_map(
        on_device,
        mesh=mesh,
        in_specs=(
            P(("groups", "ctx"), None),
            P(("groups", "ctx"), None),
            P(("groups", "ctx"), None),
            P(("groups", "ctx"), None),
            P("groups"),
        ),
        out_specs=(
            P(("groups", "ctx"), None),
            P(("groups", "ctx"), None),
            P(("groups", "ctx"), None),
            P(("groups", "ctx"), None),
        ),
        check_vma=False,
    )
```

```python
import math

import jax
import jax.numpy as jnp
import numpy as np
from jax import lax
from jax.experimental import pallas as pl
from jax.experimental.pallas import tpu as pltpu
from jax.sharding import PartitionSpec as P

QUERY_HEADS = 16
KEY_VALUE_HEADS = 4
HEAD_SIZE = 128
DOCUMENT_REACH = 8

NEGATIVE_FLOOR = -1e30


def block_home(count, block):
    if block < count:
        return block, 0
    return 2 * count - 1 - block, 1


def colored_moves(count, distance):
    edges = []
    for block in range(2 * count - distance):
        source, source_slot = block_home(count, block)
        target, target_slot = block_home(count, block + distance)
        edges.append((source, source_slot, target, target_slot))
    by_source, by_target = {}, {}
    for i, (s, _, t, _) in enumerate(edges):
        by_source.setdefault(s, []).append(i)
        by_target.setdefault(t, []).append(i)

    def partner(table, key, i):
        rest = [j for j in table[key] if j != i]
        return rest[0] if rest else None

    color = [None] * len(edges)

    def walk(i, through_target):
        while True:
            s, _, t, _ = edges[i]
            j = partner(by_target, t, i) if through_target else partner(by_source, s, i)
            if j is None or color[j] is not None:
                return
            color[j] = 1 - color[i]
            i, through_target = j, not through_target

    def degree(i):
        s, _, t, _ = edges[i]
        return min(len(by_source[s]), len(by_target[t]))

    for i in sorted(range(len(edges)), key=degree):
        if color[i] is None:
            color[i] = 0
            walk(i, True)
            walk(i, False)
    pairs = [[], []]
    send_slot = np.zeros((2, count), np.int32)
    receive_slot = np.full((2, count), -1, np.int32)
    for (s, ss, t, ts), c in zip(edges, color):
        pairs[c].append((s, t))
        send_slot[c, s] = ss
        receive_slot[c, t] = ts
    for c in range(2):
        assert len({s for s, _ in pairs[c]}) == len(pairs[c])
        assert len({t for _, t in pairs[c]}) == len(pairs[c])
    return pairs, send_slot, receive_slot


def permute(value, pairs):
    if not pairs:
        return jnp.zeros_like(value)
    return lax.ppermute(value, "ctx", pairs)


def prep_kernel(send_ref, key_ref, value_ref, own_ref, *pay_refs):
    heads = key_ref.shape[1] // HEAD_SIZE
    both = jnp.concatenate(
        [
            part
            for m in range(heads)
            for part in (
                key_ref[:, m * HEAD_SIZE : (m + 1) * HEAD_SIZE],
                value_ref[:, m * HEAD_SIZE : (m + 1) * HEAD_SIZE],
            )
        ],
        axis=1,
    )
    own_ref[...] = both
    rows = both.shape[0] // 2
    for n, pay_ref in enumerate(pay_refs):
        upper = send_ref[n] == 1

        @pl.when(upper)
        def _():
            pay_ref[...] = both[rows:]

        @pl.when(jnp.logical_not(upper))
        def _():
            pay_ref[...] = both[:rows]


def attention_kernel(
    meta_ref, ends_ref, query_ref, grad_ref, own_ref, *refs, count, reach, hop, docs, scale
):
    near = 2 * hop
    near_refs = refs[:near]
    far_refs = refs[near : near + 2]
    out_ref, dquery_ref, part_ref = refs[near + 2 : near + 5]
    window_ref = refs[near + 5]
    block_rows = own_ref.shape[0] // 2
    window = reach + 1
    span = window * block_rows
    group_width = QUERY_HEADS // KEY_VALUE_HEADS
    my_index = meta_ref[0]

    def fill(w, first, second, first_ref, second_ref, rows):
        @pl.when(first)
        def _():
            window_ref[w * block_rows : (w + 1) * block_rows, :] = first_ref[rows, :]

        @pl.when(jnp.logical_and(second, jnp.logical_not(first)))
        def _():
            window_ref[w * block_rows : (w + 1) * block_rows, :] = second_ref[rows, :]

        @pl.when(jnp.logical_and(jnp.logical_not(second), jnp.logical_not(first)))
        def _():
            window_ref[w * block_rows : (w + 1) * block_rows, :] = jnp.zeros(
                (block_rows, window_ref.shape[1]), window_ref.dtype
            )

    for slot in range(2):
        own_block = my_index if slot == 0 else 2 * count - 1 - my_index
        window_ref[reach * block_rows :, :] = own_ref[
            slot * block_rows : (slot + 1) * block_rows, :
        ]
        for distance in range(1, hop + 1):
            fill(
                reach - distance,
                meta_ref[distance] == slot,
                meta_ref[hop + distance] == slot,
                near_refs[distance - 1],
                near_refs[hop + distance - 1],
                slice(0, block_rows),
            )
        for k in range(hop):
            fill(
                reach - hop - 1 - k,
                meta_ref[1 + near] == slot,
                meta_ref[2 + near] == slot,
                far_refs[0],
                far_refs[1],
                slice(k * block_rows, (k + 1) * block_rows),
            )

        query_place = own_block * block_rows + lax.broadcasted_iota(
            jnp.int32, (block_rows, 1), 0
        )
        key_place = (own_block - reach) * block_rows + lax.broadcasted_iota(
            jnp.int32, (1, span), 1
        )
        query_doc = jnp.zeros((block_rows, 1), jnp.int32)
        key_doc = jnp.zeros((1, span), jnp.int32)
        for j in range(docs):
            end = ends_ref[j]
            query_doc = query_doc + (query_place >= end).astype(jnp.int32)
            key_doc = key_doc + (key_place >= end).astype(jnp.int32)
        visible = (query_doc == key_doc) & (key_place <= query_place) & (key_place >= 0)
        mask = jnp.concatenate([visible] * group_width, axis=0)

        rows = slice(slot * block_rows, (slot + 1) * block_rows)
        query = jnp.concatenate(
            [query_ref[rows, g * HEAD_SIZE : (g + 1) * HEAD_SIZE] for g in range(group_width)],
            axis=0,
        )
        grad = jnp.concatenate(
            [grad_ref[rows, g * HEAD_SIZE : (g + 1) * HEAD_SIZE] for g in range(group_width)],
            axis=0,
        )
        keys = window_ref[:, :HEAD_SIZE]
        values = window_ref[:, HEAD_SIZE:]
        contract_last = (((1,), (1,)), ((), ()))
        contract_first = (((0,), (0,)), ((), ()))
        scores = (
            lax.dot_general(query, keys, contract_last, preferred_element_type=jnp.float32)
            * scale
        )
        masked = jnp.where(mask, scores, NEGATIVE_FLOOR)
        row_maximum = jnp.max(masked, axis=1, keepdims=True)
        row_sum = jnp.sum(jnp.exp(masked - row_maximum), axis=1, keepdims=True)
        log_norm = row_maximum + jnp.log(row_sum)
        probs = jnp.exp(masked - log_norm)
        probs_b = probs.astype(jnp.bfloat16)
        attended = jnp.dot(probs_b, values, preferred_element_type=jnp.float32)
        attended_b = attended.astype(jnp.bfloat16)
        delta = jnp.sum(
            grad.astype(jnp.float32) * attended_b.astype(jnp.float32), axis=1, keepdims=True
        )
        dprob = lax.dot_general(grad, values, contract_last, preferred_element_type=jnp.float32)
        dscore = (probs * (dprob - delta)).astype(jnp.bfloat16)
        dquery = jnp.dot(dscore, keys, preferred_element_type=jnp.float32) * scale
        dkey = (
            lax.dot_general(dscore, query, contract_first, preferred_element_type=jnp.float32)
            * scale
        )
        dvalue = lax.dot_general(
            probs_b, grad, contract_first, preferred_element_type=jnp.float32
        )
        dquery_b = dquery.astype(jnp.bfloat16)
        for g in range(group_width):
            cols = slice(g * HEAD_SIZE, (g + 1) * HEAD_SIZE)
            out_ref[rows, cols] = attended_b[g * block_rows : (g + 1) * block_rows]
            dquery_ref[rows, cols] = dquery_b[g * block_rows : (g + 1) * block_rows]
        part_ref[slot * span : (slot + 1) * span, :HEAD_SIZE] = dkey
        part_ref[slot * span : (slot + 1) * span, HEAD_SIZE:] = dvalue


def on_device(queries, key_rows, value_rows, output_gradient, lengths):
    count = lax.axis_size("ctx")
    my_index = lax.axis_index("ctx")
    row_count = queries.shape[0]
    block_rows = row_count // 2
    pair_width = 2 * HEAD_SIZE
    width = KEY_VALUE_HEADS * pair_width
    reach = DOCUMENT_REACH
    hop = reach // 2
    near = 2 * hop
    window = reach + 1
    span = window * block_rows
    docs = lengths.shape[0]
    score_scale = 1.0 / math.sqrt(HEAD_SIZE)

    routes = [colored_moves(count, distance) for distance in range(1, hop + 1)]
    near_pairs = [routes[n % hop][0][n // hop] for n in range(near)]
    near_send = jnp.asarray(
        np.stack([routes[n % hop][1][n // hop] for n in range(near)], axis=1)
    )[my_index]
    near_receive = jnp.asarray(
        np.stack([routes[n % hop][2][n // hop] for n in range(near)], axis=1)
    )[my_index]
    far_pairs, far_send_table, far_receive_table = colored_moves(count, hop)
    far_send = jnp.asarray(far_send_table.T)[my_index]
    far_receive = jnp.asarray(far_receive_table.T)[my_index]
    doc_ends = jnp.cumsum(lengths).astype(jnp.int32)

    whole_spec = pl.BlockSpec(index_map=lambda m, *_: (0, 0))
    pair_spec = pl.BlockSpec((row_count, pair_width), lambda m, *_: (0, m))
    move_spec = pl.BlockSpec((block_rows, pair_width), lambda m, *_: (0, m))
    run_spec = pl.BlockSpec((hop * block_rows, pair_width), lambda m, *_: (0, m))
    prep = pl.pallas_call(
        prep_kernel,
        grid_spec=pltpu.PrefetchScalarGridSpec(
            num_scalar_prefetch=1,
            grid=(1,),
            in_specs=[whole_spec, whole_spec],
            out_specs=[whole_spec] * (near + 1),
        ),
        out_shape=[jax.ShapeDtypeStruct((row_count, width), jnp.bfloat16)]
        + [jax.ShapeDtypeStruct((block_rows, width), jnp.bfloat16)] * near,
    )
    own_kv, *payloads = prep(near_send, key_rows, value_rows)
    received = [permute(payloads[n], near_pairs[n]) for n in range(near)]

    def near_block(slot, distance):
        first = received[distance - 1]
        second = received[hop + distance - 1]
        return jnp.where(near_receive[distance - 1] == slot, first, second)

    runs = [
        jnp.concatenate([near_block(slot, d) for d in range(1, hop + 1)]) for slot in range(2)
    ]
    far_received = [
        permute(jnp.where(far_send[c] == 1, runs[1], runs[0]), far_pairs[c]) for c in range(2)
    ]

    head_group = QUERY_HEADS // KEY_VALUE_HEADS * HEAD_SIZE
    query_spec = pl.BlockSpec((row_count, head_group), lambda m, *_: (0, m))
    part_spec = pl.BlockSpec((2 * span, pair_width), lambda m, *_: (0, m))
    meta = jnp.concatenate([my_index.reshape(1).astype(jnp.int32), near_receive, far_receive])
    kernel = pl.pallas_call(
        lambda *refs: attention_kernel(
            *refs, count=count, reach=reach, hop=hop, docs=docs, scale=score_scale
        ),
        grid_spec=pltpu.PrefetchScalarGridSpec(
            num_scalar_prefetch=2,
            grid=(KEY_VALUE_HEADS,),
            in_specs=[query_spec, query_spec, pair_spec] + [move_spec] * near + [run_spec] * 2,
            out_specs=[query_spec, query_spec, part_spec],
            scratch_shapes=[pltpu.VMEM((span, pair_width), jnp.bfloat16)],
        ),
        out_shape=[
            jax.ShapeDtypeStruct(queries.shape, jnp.bfloat16),
            jax.ShapeDtypeStruct(queries.shape, jnp.bfloat16),
            jax.ShapeDtypeStruct((2 * span, width), jnp.float32),
        ],
    )
    attended, query_grad, part = kernel(
        meta, doc_ends, queries, output_gradient, own_kv, *received, *far_received
    )
    part = part.reshape(2, window, block_rows, width)

    far_back = []
    for c in range(2):
        run = [
            jnp.where(far_receive[c] == 1, part[1, reach - hop - 1 - k], part[0, reach - hop - 1 - k])
            for k in range(hop)
        ]
        payload = jnp.concatenate(run).astype(jnp.bfloat16)
        far_back.append(
            permute(payload, [(t, s) for s, t in far_pairs[c]]).astype(jnp.float32)
        )

    def relayed(slot, distance):
        rows = slice((distance - 1) * block_rows, distance * block_rows)
        total = jnp.where(far_send[0] == slot, far_back[0][rows], 0.0)
        return total + jnp.where(far_send[1] == slot, far_back[1][rows], 0.0)

    lower_grad = part[0, reach]
    upper_grad = part[1, reach]
    for n in range(near):
        distance = n % hop + 1
        w = reach - distance
        slot_is_upper = near_receive[n] == 1
        value = jnp.where(slot_is_upper, part[1, w], part[0, w]) + jnp.where(
            slot_is_upper, relayed(1, distance), relayed(0, distance)
        )
        back = permute(value.astype(jnp.bfloat16), [(t, s) for s, t in near_pairs[n]])
        back = back.astype(jnp.float32)
        lower_grad = lower_grad + jnp.where(near_send[n] == 0, back, 0.0)
        upper_grad = upper_grad + jnp.where(near_send[n] == 1, back, 0.0)
    grad_both = jnp.concatenate([lower_grad, upper_grad]).reshape(
        row_count, KEY_VALUE_HEADS, 2, HEAD_SIZE
    )
    key_width = KEY_VALUE_HEADS * HEAD_SIZE
    return (
        attended,
        query_grad,
        grad_both[:, :, 0].reshape(row_count, key_width).astype(jnp.bfloat16),
        grad_both[:, :, 1].reshape(row_count, key_width).astype(jnp.bfloat16),
    )


def solution(mesh):
    return jax.shard_map(
        on_device,
        mesh=mesh,
        in_specs=(
            P(("groups", "ctx"), None),
            P(("groups", "ctx"), None),
            P(("groups", "ctx"), None),
            P(("groups", "ctx"), None),
            P("groups"),
        ),
        out_specs=(
            P(("groups", "ctx"), None),
            P(("groups", "ctx"), None),
            P(("groups", "ctx"), None),
            P(("groups", "ctx"), None),
        ),
        check_vma=False,
    )
```

```python
import math

import jax
import jax.numpy as jnp
import numpy as np
from jax import lax
from jax.experimental import pallas as pl
from jax.experimental.pallas import tpu as pltpu
from jax.sharding import PartitionSpec as P

QUERY_HEADS = 16
KEY_VALUE_HEADS = 4
HEAD_SIZE = 128
DOCUMENT_REACH = 8

NEGATIVE_FLOOR = -1e30


def block_home(count, block):
    if block < count:
        return block, 0
    return 2 * count - 1 - block, 1


def colored_moves(count, distance):
    edges = []
    for block in range(2 * count - distance):
        source, source_slot = block_home(count, block)
        target, target_slot = block_home(count, block + distance)
        edges.append((source, source_slot, target, target_slot))
    by_source, by_target = {}, {}
    for i, (s, _, t, _) in enumerate(edges):
        by_source.setdefault(s, []).append(i)
        by_target.setdefault(t, []).append(i)

    def partner(table, key, i):
        rest = [j for j in table[key] if j != i]
        return rest[0] if rest else None

    color = [None] * len(edges)

    def walk(i, through_target):
        while True:
            s, _, t, _ = edges[i]
            j = partner(by_target, t, i) if through_target else partner(by_source, s, i)
            if j is None or color[j] is not None:
                return
            color[j] = 1 - color[i]
            i, through_target = j, not through_target

    def degree(i):
        s, _, t, _ = edges[i]
        return min(len(by_source[s]), len(by_target[t]))

    for i in sorted(range(len(edges)), key=degree):
        if color[i] is None:
            color[i] = 0
            walk(i, True)
            walk(i, False)
    pairs = [[], []]
    send_slot = np.zeros((2, count), np.int32)
    receive_slot = np.full((2, count), -1, np.int32)
    for (s, ss, t, ts), c in zip(edges, color):
        pairs[c].append((s, t))
        send_slot[c, s] = ss
        receive_slot[c, t] = ts
    for c in range(2):
        assert len({s for s, _ in pairs[c]}) == len(pairs[c])
        assert len({t for _, t in pairs[c]}) == len(pairs[c])
    return pairs, send_slot, receive_slot


def permute(value, pairs):
    if not pairs:
        return jnp.zeros_like(value)
    return lax.ppermute(value, "ctx", pairs)


def prep_kernel(send_ref, key_ref, value_ref, own_ref, *pay_refs):
    heads = key_ref.shape[1] // HEAD_SIZE
    both = jnp.concatenate(
        [
            part
            for m in range(heads)
            for part in (
                key_ref[:, m * HEAD_SIZE : (m + 1) * HEAD_SIZE],
                value_ref[:, m * HEAD_SIZE : (m + 1) * HEAD_SIZE],
            )
        ],
        axis=1,
    )
    own_ref[...] = both
    rows = both.shape[0] // 2
    for n, pay_ref in enumerate(pay_refs):
        upper = send_ref[n] == 1

        @pl.when(upper)
        def _():
            pay_ref[...] = both[rows:]

        @pl.when(jnp.logical_not(upper))
        def _():
            pay_ref[...] = both[:rows]


def attention_kernel(
    meta_ref, ends_ref, query_ref, grad_ref, own_ref, *refs, count, reach, hop, docs, scale
):
    near = 2 * hop
    near_refs = refs[:near]
    far_refs = refs[near : near + 2]
    out_ref, dquery_ref, part_ref = refs[near + 2 : near + 5]
    far_pay_refs = refs[near + 5 : near + 7]
    window_ref = refs[near + 7]
    block_rows = own_ref.shape[0] // 2
    window = reach + 1
    span = window * block_rows
    group_width = QUERY_HEADS // KEY_VALUE_HEADS
    my_index = meta_ref[0]

    def fill(w, first, second, first_ref, second_ref, rows):
        @pl.when(first)
        def _():
            window_ref[w * block_rows : (w + 1) * block_rows, :] = first_ref[rows, :]

        @pl.when(jnp.logical_and(second, jnp.logical_not(first)))
        def _():
            window_ref[w * block_rows : (w + 1) * block_rows, :] = second_ref[rows, :]

        @pl.when(jnp.logical_and(jnp.logical_not(second), jnp.logical_not(first)))
        def _():
            window_ref[w * block_rows : (w + 1) * block_rows, :] = jnp.zeros(
                (block_rows, window_ref.shape[1]), window_ref.dtype
            )

    for c in range(2):

        @pl.when(meta_ref[1 + near + c] < 0)
        def _():
            far_pay_refs[c][...] = jnp.zeros(far_pay_refs[c].shape, far_pay_refs[c].dtype)

    for slot in range(2):
        own_block = my_index if slot == 0 else 2 * count - 1 - my_index
        window_ref[reach * block_rows :, :] = own_ref[
            slot * block_rows : (slot + 1) * block_rows, :
        ]
        for distance in range(1, hop + 1):
            fill(
                reach - distance,
                meta_ref[distance] == slot,
                meta_ref[hop + distance] == slot,
                near_refs[distance - 1],
                near_refs[hop + distance - 1],
                slice(0, block_rows),
            )
        for k in range(hop):
            fill(
                reach - hop - 1 - k,
                meta_ref[1 + near] == slot,
                meta_ref[2 + near] == slot,
                far_refs[0],
                far_refs[1],
                slice(k * block_rows, (k + 1) * block_rows),
            )

        query_place = own_block * block_rows + lax.broadcasted_iota(
            jnp.int32, (block_rows, 1), 0
        )
        key_place = (own_block - reach) * block_rows + lax.broadcasted_iota(
            jnp.int32, (1, span), 1
        )
        query_doc = jnp.zeros((block_rows, 1), jnp.int32)
        key_doc = jnp.zeros((1, span), jnp.int32)
        for j in range(docs):
            end = ends_ref[j]
            query_doc = query_doc + (query_place >= end).astype(jnp.int32)
            key_doc = key_doc + (key_place >= end).astype(jnp.int32)
        visible = (query_doc == key_doc) & (key_place <= query_place) & (key_place >= 0)
        mask = jnp.concatenate([visible] * group_width, axis=0)

        rows = slice(slot * block_rows, (slot + 1) * block_rows)
        query = jnp.concatenate(
            [query_ref[rows, g * HEAD_SIZE : (g + 1) * HEAD_SIZE] for g in range(group_width)],
            axis=0,
        )
        grad = jnp.concatenate(
            [grad_ref[rows, g * HEAD_SIZE : (g + 1) * HEAD_SIZE] for g in range(group_width)],
            axis=0,
        )
        keys = window_ref[:, :HEAD_SIZE]
        values = window_ref[:, HEAD_SIZE:]
        contract_last = (((1,), (1,)), ((), ()))
        contract_first = (((0,), (0,)), ((), ()))
        scores = (
            lax.dot_general(query, keys, contract_last, preferred_element_type=jnp.float32)
            * scale
        )
        masked = jnp.where(mask, scores, NEGATIVE_FLOOR)
        row_maximum = jnp.max(masked, axis=1, keepdims=True)
        row_sum = jnp.sum(jnp.exp(masked - row_maximum), axis=1, keepdims=True)
        log_norm = row_maximum + jnp.log(row_sum)
        probs = jnp.exp(masked - log_norm)
        probs_b = probs.astype(jnp.bfloat16)
        attended = jnp.dot(probs_b, values, preferred_element_type=jnp.float32)
        attended_b = attended.astype(jnp.bfloat16)
        delta = jnp.sum(
            grad.astype(jnp.float32) * attended_b.astype(jnp.float32), axis=1, keepdims=True
        )
        dprob = lax.dot_general(grad, values, contract_last, preferred_element_type=jnp.float32)
        dscore = (probs * (dprob - delta)).astype(jnp.bfloat16)
        dquery = jnp.dot(dscore, keys, preferred_element_type=jnp.float32) * scale
        dkey = (
            lax.dot_general(dscore, query, contract_first, preferred_element_type=jnp.float32)
            * scale
        )
        dvalue = lax.dot_general(
            probs_b, grad, contract_first, preferred_element_type=jnp.float32
        )
        dquery_b = dquery.astype(jnp.bfloat16)
        for g in range(group_width):
            cols = slice(g * HEAD_SIZE, (g + 1) * HEAD_SIZE)
            out_ref[rows, cols] = attended_b[g * block_rows : (g + 1) * block_rows]
            dquery_ref[rows, cols] = dquery_b[g * block_rows : (g + 1) * block_rows]
        part_ref[slot * span : (slot + 1) * span, :HEAD_SIZE] = dkey
        part_ref[slot * span : (slot + 1) * span, HEAD_SIZE:] = dvalue
        for c in range(2):

            @pl.when(meta_ref[1 + near + c] == slot)
            def _():
                for k in range(hop):
                    w = reach - hop - 1 - k
                    source = slice(w * block_rows, (w + 1) * block_rows)
                    target = slice(k * block_rows, (k + 1) * block_rows)
                    far_pay_refs[c][target, :HEAD_SIZE] = dkey[source].astype(jnp.bfloat16)
                    far_pay_refs[c][target, HEAD_SIZE:] = dvalue[source].astype(jnp.bfloat16)


def on_device(queries, key_rows, value_rows, output_gradient, lengths):
    count = lax.axis_size("ctx")
    my_index = lax.axis_index("ctx")
    row_count = queries.shape[0]
    block_rows = row_count // 2
    pair_width = 2 * HEAD_SIZE
    width = KEY_VALUE_HEADS * pair_width
    reach = DOCUMENT_REACH
    hop = reach // 2
    near = 2 * hop
    window = reach + 1
    span = window * block_rows
    docs = lengths.shape[0]
    score_scale = 1.0 / math.sqrt(HEAD_SIZE)

    routes = [colored_moves(count, distance) for distance in range(1, hop + 1)]
    near_pairs = [routes[n % hop][0][n // hop] for n in range(near)]
    near_send = jnp.asarray(
        np.stack([routes[n % hop][1][n // hop] for n in range(near)], axis=1)
    )[my_index]
    near_receive = jnp.asarray(
        np.stack([routes[n % hop][2][n // hop] for n in range(near)], axis=1)
    )[my_index]
    far_pairs, far_send_table, far_receive_table = colored_moves(count, hop)
    far_send = jnp.asarray(far_send_table.T)[my_index]
    far_receive = jnp.asarray(far_receive_table.T)[my_index]
    doc_ends = jnp.cumsum(lengths).astype(jnp.int32)

    whole_spec = pl.BlockSpec(index_map=lambda m, *_: (0, 0))
    pair_spec = pl.BlockSpec((row_count, pair_width), lambda m, *_: (0, m))
    move_spec = pl.BlockSpec((block_rows, pair_width), lambda m, *_: (0, m))
    run_spec = pl.BlockSpec((hop * block_rows, pair_width), lambda m, *_: (0, m))
    prep = pl.pallas_call(
        prep_kernel,
        grid_spec=pltpu.PrefetchScalarGridSpec(
            num_scalar_prefetch=1,
            grid=(1,),
            in_specs=[whole_spec, whole_spec],
            out_specs=[whole_spec] * (near + 1),
        ),
        out_shape=[jax.ShapeDtypeStruct((row_count, width), jnp.bfloat16)]
        + [jax.ShapeDtypeStruct((block_rows, width), jnp.bfloat16)] * near,
    )
    own_kv, *payloads = prep(near_send, key_rows, value_rows)
    received = [permute(payloads[n], near_pairs[n]) for n in range(near)]

    def near_block(slot, distance):
        first = received[distance - 1]
        second = received[hop + distance - 1]
        return jnp.where(near_receive[distance - 1] == slot, first, second)

    runs = [
        jnp.concatenate([near_block(slot, d) for d in range(1, hop + 1)]) for slot in range(2)
    ]
    far_received = [
        permute(jnp.where(far_send[c] == 1, runs[1], runs[0]), far_pairs[c]) for c in range(2)
    ]

    head_group = QUERY_HEADS // KEY_VALUE_HEADS * HEAD_SIZE
    query_spec = pl.BlockSpec((row_count, head_group), lambda m, *_: (0, m))
    part_spec = pl.BlockSpec((2 * span, pair_width), lambda m, *_: (0, m))
    meta = jnp.concatenate([my_index.reshape(1).astype(jnp.int32), near_receive, far_receive])
    kernel = pl.pallas_call(
        lambda *refs: attention_kernel(
            *refs, count=count, reach=reach, hop=hop, docs=docs, scale=score_scale
        ),
        grid_spec=pltpu.PrefetchScalarGridSpec(
            num_scalar_prefetch=2,
            grid=(KEY_VALUE_HEADS,),
            in_specs=[query_spec, query_spec, pair_spec] + [move_spec] * near + [run_spec] * 2,
            out_specs=[query_spec, query_spec, part_spec, run_spec, run_spec],
            scratch_shapes=[pltpu.VMEM((span, pair_width), jnp.bfloat16)],
        ),
        out_shape=[
            jax.ShapeDtypeStruct(queries.shape, jnp.bfloat16),
            jax.ShapeDtypeStruct(queries.shape, jnp.bfloat16),
            jax.ShapeDtypeStruct((2 * span, width), jnp.float32),
        ]
        + [jax.ShapeDtypeStruct((hop * block_rows, width), jnp.bfloat16)] * 2,
    )
    attended, query_grad, part, *far_payloads = kernel(
        meta, doc_ends, queries, output_gradient, own_kv, *received, *far_received
    )
    part = part.reshape(2, window, block_rows, width)

    far_back = [
        permute(far_payloads[c], [(t, s) for s, t in far_pairs[c]]).astype(jnp.float32)
        for c in range(2)
    ]

    def relayed(slot, distance):
        rows = slice((distance - 1) * block_rows, distance * block_rows)
        total = jnp.where(far_send[0] == slot, far_back[0][rows], 0.0)
        return total + jnp.where(far_send[1] == slot, far_back[1][rows], 0.0)

    lower_grad = part[0, reach]
    upper_grad = part[1, reach]
    for n in range(near):
        distance = n % hop + 1
        w = reach - distance
        slot_is_upper = near_receive[n] == 1
        value = jnp.where(slot_is_upper, part[1, w], part[0, w]) + jnp.where(
            slot_is_upper, relayed(1, distance), relayed(0, distance)
        )
        back = permute(value.astype(jnp.bfloat16), [(t, s) for s, t in near_pairs[n]])
        back = back.astype(jnp.float32)
        lower_grad = lower_grad + jnp.where(near_send[n] == 0, back, 0.0)
        upper_grad = upper_grad + jnp.where(near_send[n] == 1, back, 0.0)
    grad_both = jnp.concatenate([lower_grad, upper_grad]).reshape(
        row_count, KEY_VALUE_HEADS, 2, HEAD_SIZE
    )
    key_width = KEY_VALUE_HEADS * HEAD_SIZE
    return (
        attended,
        query_grad,
        grad_both[:, :, 0].reshape(row_count, key_width).astype(jnp.bfloat16),
        grad_both[:, :, 1].reshape(row_count, key_width).astype(jnp.bfloat16),
    )


def solution(mesh):
    return jax.shard_map(
        on_device,
        mesh=mesh,
        in_specs=(
            P(("groups", "ctx"), None),
            P(("groups", "ctx"), None),
            P(("groups", "ctx"), None),
            P(("groups", "ctx"), None),
            P("groups"),
        ),
        out_specs=(
            P(("groups", "ctx"), None),
            P(("groups", "ctx"), None),
            P(("groups", "ctx"), None),
            P(("groups", "ctx"), None),
        ),
        check_vma=False,
    )
```

```python
import math

import jax
import jax.numpy as jnp
import numpy as np
from jax import lax
from jax.experimental import pallas as pl
from jax.experimental.pallas import tpu as pltpu
from jax.sharding import PartitionSpec as P

QUERY_HEADS = 16
KEY_VALUE_HEADS = 4
HEAD_SIZE = 128
DOCUMENT_REACH = 8

NEGATIVE_FLOOR = -1e30
CHUNK_ROWS = 16


def block_home(count, block):
    if block < count:
        return block, 0
    return 2 * count - 1 - block, 1


def colored_moves(count, distance):
    edges = []
    for block in range(2 * count - distance):
        source, source_slot = block_home(count, block)
        target, target_slot = block_home(count, block + distance)
        edges.append((source, source_slot, target, target_slot))
    by_source, by_target = {}, {}
    for i, (s, _, t, _) in enumerate(edges):
        by_source.setdefault(s, []).append(i)
        by_target.setdefault(t, []).append(i)

    def partner(table, key, i):
        rest = [j for j in table[key] if j != i]
        return rest[0] if rest else None

    color = [None] * len(edges)

    def walk(i, through_target):
        while True:
            s, _, t, _ = edges[i]
            j = partner(by_target, t, i) if through_target else partner(by_source, s, i)
            if j is None or color[j] is not None:
                return
            color[j] = 1 - color[i]
            i, through_target = j, not through_target

    def degree(i):
        s, _, t, _ = edges[i]
        return min(len(by_source[s]), len(by_target[t]))

    for i in sorted(range(len(edges)), key=degree):
        if color[i] is None:
            color[i] = 0
            walk(i, True)
            walk(i, False)
    pairs = [[], []]
    send_slot = np.zeros((2, count), np.int32)
    receive_slot = np.full((2, count), -1, np.int32)
    for (s, ss, t, ts), c in zip(edges, color):
        pairs[c].append((s, t))
        send_slot[c, s] = ss
        receive_slot[c, t] = ts
    for c in range(2):
        assert len({s for s, _ in pairs[c]}) == len(pairs[c])
        assert len({t for _, t in pairs[c]}) == len(pairs[c])
    return pairs, send_slot, receive_slot


def permute(value, pairs):
    if not pairs:
        return jnp.zeros_like(value)
    return lax.ppermute(value, "ctx", pairs)


def prep_kernel(send_ref, key_ref, value_ref, own_ref, *pay_refs):
    heads = key_ref.shape[1] // HEAD_SIZE
    both = jnp.concatenate(
        [
            part
            for m in range(heads)
            for part in (
                key_ref[:, m * HEAD_SIZE : (m + 1) * HEAD_SIZE],
                value_ref[:, m * HEAD_SIZE : (m + 1) * HEAD_SIZE],
            )
        ],
        axis=1,
    )
    own_ref[...] = both
    rows = both.shape[0] // 2
    for n, pay_ref in enumerate(pay_refs):
        upper = send_ref[n] == 1

        @pl.when(upper)
        def _():
            pay_ref[...] = both[rows:]

        @pl.when(jnp.logical_not(upper))
        def _():
            pay_ref[...] = both[:rows]


def attention_kernel(
    meta_ref, ends_ref, query_ref, grad_ref, own_ref, *refs, count, reach, hop, docs, scale
):
    near = 2 * hop
    near_refs = refs[:near]
    far_refs = refs[near : near + 2]
    out_ref, dquery_ref, part_ref = refs[near + 2 : near + 5]
    window_ref, score_ref, probs_ref, probs_b_ref, dscore_ref, delta_ref = refs[near + 5 :]
    block_rows = own_ref.shape[0] // 2
    window = reach + 1
    span = window * block_rows
    group_width = QUERY_HEADS // KEY_VALUE_HEADS
    my_index = meta_ref[0]

    def fill(w, first, second, first_ref, second_ref, rows):
        @pl.when(first)
        def _():
            window_ref[w * block_rows : (w + 1) * block_rows, :] = first_ref[rows, :]

        @pl.when(jnp.logical_and(second, jnp.logical_not(first)))
        def _():
            window_ref[w * block_rows : (w + 1) * block_rows, :] = second_ref[rows, :]

        @pl.when(jnp.logical_and(jnp.logical_not(second), jnp.logical_not(first)))
        def _():
            window_ref[w * block_rows : (w + 1) * block_rows, :] = jnp.zeros(
                (block_rows, window_ref.shape[1]), window_ref.dtype
            )

    for slot in range(2):
        own_block = my_index if slot == 0 else 2 * count - 1 - my_index
        window_ref[reach * block_rows :, :] = own_ref[
            slot * block_rows : (slot + 1) * block_rows, :
        ]
        for distance in range(1, hop + 1):
            fill(
                reach - distance,
                meta_ref[distance] == slot,
                meta_ref[hop + distance] == slot,
                near_refs[distance - 1],
                near_refs[hop + distance - 1],
                slice(0, block_rows),
            )
        for k in range(hop):
            fill(
                reach - hop - 1 - k,
                meta_ref[1 + near] == slot,
                meta_ref[2 + near] == slot,
                far_refs[0],
                far_refs[1],
                slice(k * block_rows, (k + 1) * block_rows),
            )

        key_place = (own_block - reach) * block_rows + lax.broadcasted_iota(
            jnp.int32, (1, span), 1
        )
        key_doc = jnp.zeros((1, span), jnp.int32)
        for j in range(docs):
            key_doc = key_doc + (key_place >= ends_ref[j]).astype(jnp.int32)

        rows = slice(slot * block_rows, (slot + 1) * block_rows)
        query = jnp.concatenate(
            [query_ref[rows, g * HEAD_SIZE : (g + 1) * HEAD_SIZE] for g in range(group_width)],
            axis=0,
        )
        grad = jnp.concatenate(
            [grad_ref[rows, g * HEAD_SIZE : (g + 1) * HEAD_SIZE] for g in range(group_width)],
            axis=0,
        )
        keys = window_ref[:, :HEAD_SIZE]
        values = window_ref[:, HEAD_SIZE:]
        contract_last = (((1,), (1,)), ((), ()))
        contract_first = (((0,), (0,)), ((), ()))
        score_ref[...] = lax.dot_general(
            query, keys, contract_last, preferred_element_type=jnp.float32
        )
        chunks = group_width * block_rows // CHUNK_ROWS

        def softmax_chunk(r, carry):
            start = pl.multiple_of(r * CHUNK_ROWS, CHUNK_ROWS)
            query_place = own_block * block_rows + (
                (r * CHUNK_ROWS) % block_rows
                + lax.broadcasted_iota(jnp.int32, (CHUNK_ROWS, 1), 0)
            )
            query_doc = jnp.zeros((CHUNK_ROWS, 1), jnp.int32)
            for j in range(docs):
                query_doc = query_doc + (query_place >= ends_ref[j]).astype(jnp.int32)
            visible = (
                (query_doc == key_doc) & (key_place <= query_place) & (key_place >= 0)
            )
            scores = score_ref[pl.ds(start, CHUNK_ROWS), :] * scale
            masked = jnp.where(visible, scores, NEGATIVE_FLOOR)
            row_maximum = jnp.max(masked, axis=1, keepdims=True)
            row_sum = jnp.sum(jnp.exp(masked - row_maximum), axis=1, keepdims=True)
            log_norm = row_maximum + jnp.log(row_sum)
            probs = jnp.exp(masked - log_norm)
            probs_ref[pl.ds(start, CHUNK_ROWS), :] = probs
            probs_b_ref[pl.ds(start, CHUNK_ROWS), :] = probs.astype(jnp.bfloat16)
            return carry

        lax.fori_loop(0, chunks, softmax_chunk, 0)
        probs_b = probs_b_ref[...]
        attended = jnp.dot(probs_b, values, preferred_element_type=jnp.float32)
        attended_b = attended.astype(jnp.bfloat16)
        delta_ref[...] = jnp.sum(
            grad.astype(jnp.float32) * attended_b.astype(jnp.float32), axis=1, keepdims=True
        )
        score_ref[...] = lax.dot_general(
            grad, values, contract_last, preferred_element_type=jnp.float32
        )

        def dscore_chunk(r, carry):
            start = pl.multiple_of(r * CHUNK_ROWS, CHUNK_ROWS)
            here = pl.ds(start, CHUNK_ROWS)
            dscore_ref[here, :] = (
                probs_ref[here, :] * (score_ref[here, :] - delta_ref[here, :])
            ).astype(jnp.bfloat16)
            return carry

        lax.fori_loop(0, chunks, dscore_chunk, 0)
        dscore = dscore_ref[...]
        dquery = jnp.dot(dscore, keys, preferred_element_type=jnp.float32) * scale
        dkey = (
            lax.dot_general(dscore, query, contract_first, preferred_element_type=jnp.float32)
            * scale
        )
        dvalue = lax.dot_general(
            probs_b, grad, contract_first, preferred_element_type=jnp.float32
        )
        dquery_b = dquery.astype(jnp.bfloat16)
        for g in range(group_width):
            cols = slice(g * HEAD_SIZE, (g + 1) * HEAD_SIZE)
            out_ref[rows, cols] = attended_b[g * block_rows : (g + 1) * block_rows]
            dquery_ref[rows, cols] = dquery_b[g * block_rows : (g + 1) * block_rows]
        part_ref[slot * span : (slot + 1) * span, :HEAD_SIZE] = dkey
        part_ref[slot * span : (slot + 1) * span, HEAD_SIZE:] = dvalue


def on_device(queries, key_rows, value_rows, output_gradient, lengths):
    count = lax.axis_size("ctx")
    my_index = lax.axis_index("ctx")
    row_count = queries.shape[0]
    block_rows = row_count // 2
    pair_width = 2 * HEAD_SIZE
    width = KEY_VALUE_HEADS * pair_width
    reach = DOCUMENT_REACH
    hop = reach // 2
    near = 2 * hop
    window = reach + 1
    span = window * block_rows
    docs = lengths.shape[0]
    score_scale = 1.0 / math.sqrt(HEAD_SIZE)

    routes = [colored_moves(count, distance) for distance in range(1, hop + 1)]
    near_pairs = [routes[n % hop][0][n // hop] for n in range(near)]
    near_send = jnp.asarray(
        np.stack([routes[n % hop][1][n // hop] for n in range(near)], axis=1)
    )[my_index]
    near_receive = jnp.asarray(
        np.stack([routes[n % hop][2][n // hop] for n in range(near)], axis=1)
    )[my_index]
    far_pairs, far_send_table, far_receive_table = colored_moves(count, hop)
    far_send = jnp.asarray(far_send_table.T)[my_index]
    far_receive = jnp.asarray(far_receive_table.T)[my_index]
    doc_ends = jnp.cumsum(lengths).astype(jnp.int32)

    whole_spec = pl.BlockSpec(index_map=lambda m, *_: (0, 0))
    pair_spec = pl.BlockSpec((row_count, pair_width), lambda m, *_: (0, m))
    move_spec = pl.BlockSpec((block_rows, pair_width), lambda m, *_: (0, m))
    run_spec = pl.BlockSpec((hop * block_rows, pair_width), lambda m, *_: (0, m))
    prep = pl.pallas_call(
        prep_kernel,
        grid_spec=pltpu.PrefetchScalarGridSpec(
            num_scalar_prefetch=1,
            grid=(1,),
            in_specs=[whole_spec, whole_spec],
            out_specs=[whole_spec] * (near + 1),
        ),
        out_shape=[jax.ShapeDtypeStruct((row_count, width), jnp.bfloat16)]
        + [jax.ShapeDtypeStruct((block_rows, width), jnp.bfloat16)] * near,
    )
    own_kv, *payloads = prep(near_send, key_rows, value_rows)
    received = [permute(payloads[n], near_pairs[n]) for n in range(near)]

    def near_block(slot, distance):
        first = received[distance - 1]
        second = received[hop + distance - 1]
        return jnp.where(near_receive[distance - 1] == slot, first, second)

    runs = [
        jnp.concatenate([near_block(slot, d) for d in range(1, hop + 1)]) for slot in range(2)
    ]
    far_received = [
        permute(jnp.where(far_send[c] == 1, runs[1], runs[0]), far_pairs[c]) for c in range(2)
    ]

    head_group = QUERY_HEADS // KEY_VALUE_HEADS * HEAD_SIZE
    group_rows = QUERY_HEADS // KEY_VALUE_HEADS * block_rows
    query_spec = pl.BlockSpec((row_count, head_group), lambda m, *_: (0, m))
    part_spec = pl.BlockSpec((2 * span, pair_width), lambda m, *_: (0, m))
    meta = jnp.concatenate([my_index.reshape(1).astype(jnp.int32), near_receive, far_receive])
    kernel = pl.pallas_call(
        lambda *refs: attention_kernel(
            *refs, count=count, reach=reach, hop=hop, docs=docs, scale=score_scale
        ),
        grid_spec=pltpu.PrefetchScalarGridSpec(
            num_scalar_prefetch=2,
            grid=(KEY_VALUE_HEADS,),
            in_specs=[query_spec, query_spec, pair_spec] + [move_spec] * near + [run_spec] * 2,
            out_specs=[query_spec, query_spec, part_spec],
            scratch_shapes=[
                pltpu.VMEM((span, pair_width), jnp.bfloat16),
                pltpu.VMEM((group_rows, span), jnp.float32),
                pltpu.VMEM((group_rows, span), jnp.float32),
                pltpu.VMEM((group_rows, span), jnp.bfloat16),
                pltpu.VMEM((group_rows, span), jnp.bfloat16),
                pltpu.VMEM((group_rows, 1), jnp.float32),
            ],
        ),
        out_shape=[
            jax.ShapeDtypeStruct(queries.shape, jnp.bfloat16),
            jax.ShapeDtypeStruct(queries.shape, jnp.bfloat16),
            jax.ShapeDtypeStruct((2 * span, width), jnp.float32),
        ],
    )
    attended, query_grad, part = kernel(
        meta, doc_ends, queries, output_gradient, own_kv, *received, *far_received
    )
    part = part.reshape(2, window, block_rows, width)

    far_back = []
    for c in range(2):
        run = [
            jnp.where(far_receive[c] == 1, part[1, reach - hop - 1 - k], part[0, reach - hop - 1 - k])
            for k in range(hop)
        ]
        payload = jnp.concatenate(run).astype(jnp.bfloat16)
        far_back.append(
            permute(payload, [(t, s) for s, t in far_pairs[c]]).astype(jnp.float32)
        )

    def relayed(slot, distance):
        rows = slice((distance - 1) * block_rows, distance * block_rows)
        total = jnp.where(far_send[0] == slot, far_back[0][rows], 0.0)
        return total + jnp.where(far_send[1] == slot, far_back[1][rows], 0.0)

    lower_grad = part[0, reach]
    upper_grad = part[1, reach]
    for n in range(near):
        distance = n % hop + 1
        w = reach - distance
        slot_is_upper = near_receive[n] == 1
        value = jnp.where(slot_is_upper, part[1, w], part[0, w]) + jnp.where(
            slot_is_upper, relayed(1, distance), relayed(0, distance)
        )
        back = permute(value.astype(jnp.bfloat16), [(t, s) for s, t in near_pairs[n]])
        back = back.astype(jnp.float32)
        lower_grad = lower_grad + jnp.where(near_send[n] == 0, back, 0.0)
        upper_grad = upper_grad + jnp.where(near_send[n] == 1, back, 0.0)
    grad_both = jnp.concatenate([lower_grad, upper_grad]).reshape(
        row_count, KEY_VALUE_HEADS, 2, HEAD_SIZE
    )
    key_width = KEY_VALUE_HEADS * HEAD_SIZE
    return (
        attended,
        query_grad,
        grad_both[:, :, 0].reshape(row_count, key_width).astype(jnp.bfloat16),
        grad_both[:, :, 1].reshape(row_count, key_width).astype(jnp.bfloat16),
    )


def solution(mesh):
    return jax.shard_map(
        on_device,
        mesh=mesh,
        in_specs=(
            P(("groups", "ctx"), None),
            P(("groups", "ctx"), None),
            P(("groups", "ctx"), None),
            P(("groups", "ctx"), None),
            P("groups"),
        ),
        out_specs=(
            P(("groups", "ctx"), None),
            P(("groups", "ctx"), None),
            P(("groups", "ctx"), None),
            P(("groups", "ctx"), None),
        ),
        check_vma=False,
    )
```

```python
import math

import jax
import jax.numpy as jnp
import numpy as np
from jax import lax
from jax.experimental import pallas as pl
from jax.experimental.pallas import tpu as pltpu
from jax.sharding import PartitionSpec as P

QUERY_HEADS = 16
KEY_VALUE_HEADS = 4
HEAD_SIZE = 128
DOCUMENT_REACH = 8

NEGATIVE_FLOOR = -1e30


def block_home(count, block):
    if block < count:
        return block, 0
    return 2 * count - 1 - block, 1


def colored_moves(count, distance):
    edges = []
    for block in range(2 * count - distance):
        source, source_slot = block_home(count, block)
        target, target_slot = block_home(count, block + distance)
        edges.append((source, source_slot, target, target_slot))
    by_source, by_target = {}, {}
    for i, (s, _, t, _) in enumerate(edges):
        by_source.setdefault(s, []).append(i)
        by_target.setdefault(t, []).append(i)

    def partner(table, key, i):
        rest = [j for j in table[key] if j != i]
        return rest[0] if rest else None

    color = [None] * len(edges)

    def walk(i, through_target):
        while True:
            s, _, t, _ = edges[i]
            j = partner(by_target, t, i) if through_target else partner(by_source, s, i)
            if j is None or color[j] is not None:
                return
            color[j] = 1 - color[i]
            i, through_target = j, not through_target

    def degree(i):
        s, _, t, _ = edges[i]
        return min(len(by_source[s]), len(by_target[t]))

    for i in sorted(range(len(edges)), key=degree):
        if color[i] is None:
            color[i] = 0
            walk(i, True)
            walk(i, False)
    pairs = [[], []]
    send_slot = np.zeros((2, count), np.int32)
    receive_slot = np.full((2, count), -1, np.int32)
    for (s, ss, t, ts), c in zip(edges, color):
        pairs[c].append((s, t))
        send_slot[c, s] = ss
        receive_slot[c, t] = ts
    for c in range(2):
        assert len({s for s, _ in pairs[c]}) == len(pairs[c])
        assert len({t for _, t in pairs[c]}) == len(pairs[c])
    return pairs, send_slot, receive_slot


def permute(value, pairs):
    if not pairs:
        return jnp.zeros_like(value)
    return lax.ppermute(value, "ctx", pairs)


def prep_kernel(send_ref, key_ref, value_ref, own_ref, *pay_refs):
    heads = key_ref.shape[1] // HEAD_SIZE
    both = jnp.concatenate(
        [
            part
            for m in range(heads)
            for part in (
                key_ref[:, m * HEAD_SIZE : (m + 1) * HEAD_SIZE],
                value_ref[:, m * HEAD_SIZE : (m + 1) * HEAD_SIZE],
            )
        ],
        axis=1,
    )
    own_ref[...] = both
    rows = both.shape[0] // 2
    for n, pay_ref in enumerate(pay_refs):
        upper = send_ref[n] == 1

        @pl.when(upper)
        def _():
            pay_ref[...] = both[rows:]

        @pl.when(jnp.logical_not(upper))
        def _():
            pay_ref[...] = both[:rows]


def attention_kernel(
    meta_ref, ends_ref, query_ref, grad_ref, own_ref, *refs, count, reach, hop, docs, scale
):
    near = 2 * hop
    near_refs = refs[:near]
    far_refs = refs[near : near + 2]
    out_ref, dquery_ref, part_ref = refs[near + 2 : near + 5]
    window_ref = refs[near + 5]
    block_rows = own_ref.shape[0] // 2
    window = reach + 1
    span = window * block_rows
    group_width = QUERY_HEADS // KEY_VALUE_HEADS
    my_index = meta_ref[0]

    def fill(w, first, second, first_ref, second_ref, rows):
        @pl.when(first)
        def _():
            window_ref[w * block_rows : (w + 1) * block_rows, :] = first_ref[rows, :]

        @pl.when(jnp.logical_and(second, jnp.logical_not(first)))
        def _():
            window_ref[w * block_rows : (w + 1) * block_rows, :] = second_ref[rows, :]

        @pl.when(jnp.logical_and(jnp.logical_not(second), jnp.logical_not(first)))
        def _():
            window_ref[w * block_rows : (w + 1) * block_rows, :] = jnp.zeros(
                (block_rows, window_ref.shape[1]), window_ref.dtype
            )

    for slot in range(2):
        own_block = my_index if slot == 0 else 2 * count - 1 - my_index
        window_ref[reach * block_rows :, :] = own_ref[
            slot * block_rows : (slot + 1) * block_rows, :
        ]
        for distance in range(1, hop + 1):
            fill(
                reach - distance,
                meta_ref[distance] == slot,
                meta_ref[hop + distance] == slot,
                near_refs[distance - 1],
                near_refs[hop + distance - 1],
                slice(0, block_rows),
            )
        for k in range(hop):
            fill(
                reach - hop - 1 - k,
                meta_ref[1 + near] == slot,
                meta_ref[2 + near] == slot,
                far_refs[0],
                far_refs[1],
                slice(k * block_rows, (k + 1) * block_rows),
            )

        query_place = own_block * block_rows + lax.broadcasted_iota(
            jnp.int32, (block_rows, 1), 0
        )
        key_place = (own_block - reach) * block_rows + lax.broadcasted_iota(
            jnp.int32, (1, span), 1
        )
        query_doc = jnp.zeros((block_rows, 1), jnp.int32)
        key_doc = jnp.zeros((1, span), jnp.int32)
        for j in range(docs):
            end = ends_ref[j]
            query_doc = query_doc + (query_place >= end).astype(jnp.int32)
            key_doc = key_doc + (key_place >= end).astype(jnp.int32)
        visible = (query_doc == key_doc) & (key_place <= query_place) & (key_place >= 0)
        mask = jnp.concatenate([visible] * group_width, axis=0)

        rows = slice(slot * block_rows, (slot + 1) * block_rows)
        query = jnp.concatenate(
            [query_ref[rows, g * HEAD_SIZE : (g + 1) * HEAD_SIZE] for g in range(group_width)],
            axis=0,
        )
        grad = jnp.concatenate(
            [grad_ref[rows, g * HEAD_SIZE : (g + 1) * HEAD_SIZE] for g in range(group_width)],
            axis=0,
        )
        keys = window_ref[:, :HEAD_SIZE]
        values = window_ref[:, HEAD_SIZE:]
        contract_last = (((1,), (1,)), ((), ()))
        contract_first = (((0,), (0,)), ((), ()))
        scores = (
            lax.dot_general(query, keys, contract_last, preferred_element_type=jnp.float32)
            * scale
        )
        masked = jnp.where(mask, scores, NEGATIVE_FLOOR)
        row_maximum = jnp.max(masked, axis=1, keepdims=True)
        row_sum = jnp.sum(jnp.exp(masked - row_maximum), axis=1, keepdims=True)
        log_norm = row_maximum + jnp.log(row_sum)
        probs = jnp.exp(masked - log_norm)
        probs_b = probs.astype(jnp.bfloat16)
        attended = jnp.dot(probs_b, values, preferred_element_type=jnp.float32)
        attended_b = attended.astype(jnp.bfloat16)
        delta = jnp.sum(
            grad.astype(jnp.float32) * attended_b.astype(jnp.float32), axis=1, keepdims=True
        )
        dprob = lax.dot_general(grad, values, contract_last, preferred_element_type=jnp.float32)
        dscore = (probs * (dprob - delta)).astype(jnp.bfloat16)
        dquery = jnp.dot(dscore, keys, preferred_element_type=jnp.float32) * scale
        dkey = (
            lax.dot_general(dscore, query, contract_first, preferred_element_type=jnp.float32)
            * scale
        )
        dvalue = lax.dot_general(
            probs_b, grad, contract_first, preferred_element_type=jnp.float32
        )
        dquery_b = dquery.astype(jnp.bfloat16)
        for g in range(group_width):
            cols = slice(g * HEAD_SIZE, (g + 1) * HEAD_SIZE)
            out_ref[rows, cols] = attended_b[g * block_rows : (g + 1) * block_rows]
            dquery_ref[rows, cols] = dquery_b[g * block_rows : (g + 1) * block_rows]
        part_ref[slot * span : (slot + 1) * span, :HEAD_SIZE] = dkey
        part_ref[slot * span : (slot + 1) * span, HEAD_SIZE:] = dvalue


def on_device(queries, key_rows, value_rows, output_gradient, lengths):
    count = lax.axis_size("ctx")
    my_index = lax.axis_index("ctx")
    row_count = queries.shape[0]
    block_rows = row_count // 2
    pair_width = 2 * HEAD_SIZE
    width = KEY_VALUE_HEADS * pair_width
    reach = DOCUMENT_REACH
    hop = reach // 2
    near = 2 * hop
    window = reach + 1
    span = window * block_rows
    docs = lengths.shape[0]
    score_scale = 1.0 / math.sqrt(HEAD_SIZE)

    routes = [colored_moves(count, distance) for distance in range(1, hop + 1)]
    near_pairs = [routes[n % hop][0][n // hop] for n in range(near)]
    near_send = jnp.asarray(
        np.stack([routes[n % hop][1][n // hop] for n in range(near)], axis=1)
    )[my_index]
    near_receive = jnp.asarray(
        np.stack([routes[n % hop][2][n // hop] for n in range(near)], axis=1)
    )[my_index]
    far_pairs, far_send_table, far_receive_table = colored_moves(count, hop)
    far_send = jnp.asarray(far_send_table.T)[my_index]
    far_receive = jnp.asarray(far_receive_table.T)[my_index]
    doc_ends = jnp.cumsum(lengths).astype(jnp.int32)

    whole_spec = pl.BlockSpec(index_map=lambda m, *_: (0, 0))
    pair_spec = pl.BlockSpec((row_count, pair_width), lambda m, *_: (0, m))
    move_spec = pl.BlockSpec((block_rows, pair_width), lambda m, *_: (0, m))
    run_spec = pl.BlockSpec((hop * block_rows, pair_width), lambda m, *_: (0, m))
    prep = pl.pallas_call(
        prep_kernel,
        grid_spec=pltpu.PrefetchScalarGridSpec(
            num_scalar_prefetch=1,
            grid=(1,),
            in_specs=[whole_spec, whole_spec],
            out_specs=[whole_spec] * (near + 1),
        ),
        out_shape=[jax.ShapeDtypeStruct((row_count, width), jnp.bfloat16)]
        + [jax.ShapeDtypeStruct((block_rows, width), jnp.bfloat16)] * near,
    )
    own_kv, *payloads = prep(near_send, key_rows, value_rows)
    received = [permute(payloads[n], near_pairs[n]) for n in range(near)]

    def near_block(slot, distance):
        first = received[distance - 1]
        second = received[hop + distance - 1]
        return jnp.where(near_receive[distance - 1] == slot, first, second)

    runs = [
        jnp.concatenate([near_block(slot, d) for d in range(1, hop + 1)]) for slot in range(2)
    ]
    far_received = [
        permute(jnp.where(far_send[c] == 1, runs[1], runs[0]), far_pairs[c]) for c in range(2)
    ]

    head_group = QUERY_HEADS // KEY_VALUE_HEADS * HEAD_SIZE
    query_spec = pl.BlockSpec((row_count, head_group), lambda m, *_: (0, m))
    part_spec = pl.BlockSpec((2 * span, pair_width), lambda m, *_: (0, m))
    meta = jnp.concatenate([my_index.reshape(1).astype(jnp.int32), near_receive, far_receive])
    kernel = pl.pallas_call(
        lambda *refs: attention_kernel(
            *refs, count=count, reach=reach, hop=hop, docs=docs, scale=score_scale
        ),
        grid_spec=pltpu.PrefetchScalarGridSpec(
            num_scalar_prefetch=2,
            grid=(KEY_VALUE_HEADS,),
            in_specs=[query_spec, query_spec, pair_spec] + [move_spec] * near + [run_spec] * 2,
            out_specs=[query_spec, query_spec, part_spec],
            scratch_shapes=[pltpu.VMEM((span, pair_width), jnp.bfloat16)],
        ),
        out_shape=[
            jax.ShapeDtypeStruct(queries.shape, jnp.bfloat16),
            jax.ShapeDtypeStruct(queries.shape, jnp.bfloat16),
            jax.ShapeDtypeStruct((2 * span, width), jnp.float32),
        ],
    )
    attended, query_grad, part = kernel(
        meta, doc_ends, queries, output_gradient, own_kv, *received, *far_received
    )
    part = part.reshape(2, window, block_rows, width)

    lower_grad = part[0, reach]
    upper_grad = part[1, reach]
    relay_sum = [jnp.zeros_like(lower_grad), jnp.zeros_like(lower_grad)]
    for n in range(near):
        distance = n % hop + 1
        slot_is_upper = near_receive[n] == 1
        pieces = [
            jnp.where(slot_is_upper, part[1, w], part[0, w])
            for w in (reach - distance, reach - hop - distance)
        ]
        payload = jnp.concatenate(pieces).astype(jnp.bfloat16)
        back = permute(payload, [(t, s) for s, t in near_pairs[n]]).astype(jnp.float32)
        own_back, relay_back = back[:block_rows], back[block_rows:]
        to_upper = near_send[n] == 1
        lower_grad = lower_grad + jnp.where(to_upper, 0.0, own_back)
        upper_grad = upper_grad + jnp.where(to_upper, own_back, 0.0)
        relay_sum[0] = relay_sum[0] + jnp.where(to_upper, 0.0, relay_back)
        relay_sum[1] = relay_sum[1] + jnp.where(to_upper, relay_back, 0.0)
    for c in range(2):
        payload = jnp.where(far_receive[c] == 1, relay_sum[1], relay_sum[0])
        back = permute(payload.astype(jnp.bfloat16), [(t, s) for s, t in far_pairs[c]])
        back = back.astype(jnp.float32)
        lower_grad = lower_grad + jnp.where(far_send[c] == 1, 0.0, back)
        upper_grad = upper_grad + jnp.where(far_send[c] == 1, back, 0.0)
    grad_both = jnp.concatenate([lower_grad, upper_grad]).reshape(
        row_count, KEY_VALUE_HEADS, 2, HEAD_SIZE
    )
    key_width = KEY_VALUE_HEADS * HEAD_SIZE
    return (
        attended,
        query_grad,
        grad_both[:, :, 0].reshape(row_count, key_width).astype(jnp.bfloat16),
        grad_both[:, :, 1].reshape(row_count, key_width).astype(jnp.bfloat16),
    )


def solution(mesh):
    return jax.shard_map(
        on_device,
        mesh=mesh,
        in_specs=(
            P(("groups", "ctx"), None),
            P(("groups", "ctx"), None),
            P(("groups", "ctx"), None),
            P(("groups", "ctx"), None),
            P("groups"),
        ),
        out_specs=(
            P(("groups", "ctx"), None),
            P(("groups", "ctx"), None),
            P(("groups", "ctx"), None),
            P(("groups", "ctx"), None),
        ),
        check_vma=False,
    )
```

```python
import math

import jax
import jax.numpy as jnp
import numpy as np
from jax import lax
from jax.experimental import pallas as pl
from jax.experimental.pallas import tpu as pltpu
from jax.sharding import PartitionSpec as P

QUERY_HEADS = 16
KEY_VALUE_HEADS = 4
HEAD_SIZE = 128
DOCUMENT_REACH = 8

NEGATIVE_FLOOR = -1e30


def block_home(count, block):
    if block < count:
        return block, 0
    return 2 * count - 1 - block, 1


def colored_moves(count, distance):
    edges = []
    for block in range(2 * count - distance):
        source, source_slot = block_home(count, block)
        target, target_slot = block_home(count, block + distance)
        edges.append((source, source_slot, target, target_slot))
    by_source, by_target = {}, {}
    for i, (s, _, t, _) in enumerate(edges):
        by_source.setdefault(s, []).append(i)
        by_target.setdefault(t, []).append(i)

    def partner(table, key, i):
        rest = [j for j in table[key] if j != i]
        return rest[0] if rest else None

    color = [None] * len(edges)

    def walk(i, through_target):
        while True:
            s, _, t, _ = edges[i]
            j = partner(by_target, t, i) if through_target else partner(by_source, s, i)
            if j is None or color[j] is not None:
                return
            color[j] = 1 - color[i]
            i, through_target = j, not through_target

    def degree(i):
        s, _, t, _ = edges[i]
        return min(len(by_source[s]), len(by_target[t]))

    for i in sorted(range(len(edges)), key=degree):
        if color[i] is None:
            color[i] = 0
            walk(i, True)
            walk(i, False)
    pairs = [[], []]
    send_slot = np.zeros((2, count), np.int32)
    receive_slot = np.full((2, count), -1, np.int32)
    for (s, ss, t, ts), c in zip(edges, color):
        pairs[c].append((s, t))
        send_slot[c, s] = ss
        receive_slot[c, t] = ts
    for c in range(2):
        assert len({s for s, _ in pairs[c]}) == len(pairs[c])
        assert len({t for _, t in pairs[c]}) == len(pairs[c])
    return pairs, send_slot, receive_slot


def permute(value, pairs):
    if not pairs:
        return jnp.zeros_like(value)
    return lax.ppermute(value, "ctx", pairs)


def prep_kernel(send_ref, key_ref, value_ref, own_ref, *pay_refs):
    heads = key_ref.shape[1] // HEAD_SIZE
    both = jnp.concatenate(
        [
            part
            for m in range(heads)
            for part in (
                key_ref[:, m * HEAD_SIZE : (m + 1) * HEAD_SIZE],
                value_ref[:, m * HEAD_SIZE : (m + 1) * HEAD_SIZE],
            )
        ],
        axis=1,
    )
    own_ref[...] = both
    rows = both.shape[0] // 2
    for n, pay_ref in enumerate(pay_refs):
        upper = send_ref[n] == 1

        @pl.when(upper)
        def _():
            pay_ref[...] = both[rows:]

        @pl.when(jnp.logical_not(upper))
        def _():
            pay_ref[...] = both[:rows]


def finish_kernel(send_ref, lower_ref, upper_ref, first_ref, second_ref, key_ref, value_ref):
    block_rows = lower_ref.shape[0]
    grads = [lower_ref[...], upper_ref[...]]
    for c, back_ref in enumerate((first_ref, second_ref)):
        back = back_ref[...].astype(jnp.float32)
        upper = (send_ref[c] == 1).astype(jnp.float32)
        grads[0] = grads[0] + back * (1.0 - upper)
        grads[1] = grads[1] + back * upper
    for slot in range(2):
        rows = slice(slot * block_rows, (slot + 1) * block_rows)
        for m in range(key_ref.shape[1] // HEAD_SIZE):
            cols = slice(m * HEAD_SIZE, (m + 1) * HEAD_SIZE)
            base = 2 * m * HEAD_SIZE
            key_ref[rows, cols] = grads[slot][:, base : base + HEAD_SIZE].astype(key_ref.dtype)
            value_ref[rows, cols] = grads[slot][:, base + HEAD_SIZE : base + 2 * HEAD_SIZE].astype(
                value_ref.dtype
            )


def attention_kernel(
    meta_ref, ends_ref, query_ref, grad_ref, own_ref, *refs, count, reach, hop, docs, scale
):
    near = 2 * hop
    near_refs = refs[:near]
    far_refs = refs[near : near + 2]
    out_ref, dquery_ref, part_ref = refs[near + 2 : near + 5]
    window_ref = refs[near + 5]
    block_rows = own_ref.shape[0] // 2
    window = reach + 1
    span = window * block_rows
    group_width = QUERY_HEADS // KEY_VALUE_HEADS
    my_index = meta_ref[0]

    def fill(w, first, second, first_ref, second_ref, rows):
        @pl.when(first)
        def _():
            window_ref[w * block_rows : (w + 1) * block_rows, :] = first_ref[rows, :]

        @pl.when(jnp.logical_and(second, jnp.logical_not(first)))
        def _():
            window_ref[w * block_rows : (w + 1) * block_rows, :] = second_ref[rows, :]

        @pl.when(jnp.logical_and(jnp.logical_not(second), jnp.logical_not(first)))
        def _():
            window_ref[w * block_rows : (w + 1) * block_rows, :] = jnp.zeros(
                (block_rows, window_ref.shape[1]), window_ref.dtype
            )

    for slot in range(2):
        own_block = my_index if slot == 0 else 2 * count - 1 - my_index
        window_ref[reach * block_rows :, :] = own_ref[
            slot * block_rows : (slot + 1) * block_rows, :
        ]
        for distance in range(1, hop + 1):
            fill(
                reach - distance,
                meta_ref[distance] == slot,
                meta_ref[hop + distance] == slot,
                near_refs[distance - 1],
                near_refs[hop + distance - 1],
                slice(0, block_rows),
            )
        for k in range(hop):
            fill(
                reach - hop - 1 - k,
                meta_ref[1 + near] == slot,
                meta_ref[2 + near] == slot,
                far_refs[0],
                far_refs[1],
                slice(k * block_rows, (k + 1) * block_rows),
            )

        query_place = own_block * block_rows + lax.broadcasted_iota(
            jnp.int32, (block_rows, 1), 0
        )
        key_place = (own_block - reach) * block_rows + lax.broadcasted_iota(
            jnp.int32, (1, span), 1
        )
        query_doc = jnp.zeros((block_rows, 1), jnp.int32)
        key_doc = jnp.zeros((1, span), jnp.int32)
        for j in range(docs):
            end = ends_ref[j]
            query_doc = query_doc + (query_place >= end).astype(jnp.int32)
            key_doc = key_doc + (key_place >= end).astype(jnp.int32)
        visible = (query_doc == key_doc) & (key_place <= query_place) & (key_place >= 0)
        mask = jnp.concatenate([visible] * group_width, axis=0)

        rows = slice(slot * block_rows, (slot + 1) * block_rows)
        query = jnp.concatenate(
            [query_ref[rows, g * HEAD_SIZE : (g + 1) * HEAD_SIZE] for g in range(group_width)],
            axis=0,
        )
        grad = jnp.concatenate(
            [grad_ref[rows, g * HEAD_SIZE : (g + 1) * HEAD_SIZE] for g in range(group_width)],
            axis=0,
        )
        keys = window_ref[:, :HEAD_SIZE]
        values = window_ref[:, HEAD_SIZE:]
        contract_last = (((1,), (1,)), ((), ()))
        contract_first = (((0,), (0,)), ((), ()))
        scores = (
            lax.dot_general(query, keys, contract_last, preferred_element_type=jnp.float32)
            * scale
        )
        masked = jnp.where(mask, scores, NEGATIVE_FLOOR)
        row_maximum = jnp.max(masked, axis=1, keepdims=True)
        row_sum = jnp.sum(jnp.exp(masked - row_maximum), axis=1, keepdims=True)
        log_norm = row_maximum + jnp.log(row_sum)
        probs = jnp.exp(masked - log_norm)
        probs_b = probs.astype(jnp.bfloat16)
        attended = jnp.dot(probs_b, values, preferred_element_type=jnp.float32)
        attended_b = attended.astype(jnp.bfloat16)
        delta = jnp.sum(
            grad.astype(jnp.float32) * attended_b.astype(jnp.float32), axis=1, keepdims=True
        )
        dprob = lax.dot_general(grad, values, contract_last, preferred_element_type=jnp.float32)
        dscore = (probs * (dprob - delta)).astype(jnp.bfloat16)
        dquery = jnp.dot(dscore, keys, preferred_element_type=jnp.float32) * scale
        dkey = (
            lax.dot_general(dscore, query, contract_first, preferred_element_type=jnp.float32)
            * scale
        )
        dvalue = lax.dot_general(
            probs_b, grad, contract_first, preferred_element_type=jnp.float32
        )
        dquery_b = dquery.astype(jnp.bfloat16)
        for g in range(group_width):
            cols = slice(g * HEAD_SIZE, (g + 1) * HEAD_SIZE)
            out_ref[rows, cols] = attended_b[g * block_rows : (g + 1) * block_rows]
            dquery_ref[rows, cols] = dquery_b[g * block_rows : (g + 1) * block_rows]
        part_ref[slot * span : (slot + 1) * span, :HEAD_SIZE] = dkey
        part_ref[slot * span : (slot + 1) * span, HEAD_SIZE:] = dvalue


def on_device(queries, key_rows, value_rows, output_gradient, lengths):
    count = lax.axis_size("ctx")
    my_index = lax.axis_index("ctx")
    row_count = queries.shape[0]
    block_rows = row_count // 2
    pair_width = 2 * HEAD_SIZE
    width = KEY_VALUE_HEADS * pair_width
    reach = DOCUMENT_REACH
    hop = reach // 2
    near = 2 * hop
    window = reach + 1
    span = window * block_rows
    docs = lengths.shape[0]
    score_scale = 1.0 / math.sqrt(HEAD_SIZE)

    routes = [colored_moves(count, distance) for distance in range(1, hop + 1)]
    near_pairs = [routes[n % hop][0][n // hop] for n in range(near)]
    near_send = jnp.asarray(
        np.stack([routes[n % hop][1][n // hop] for n in range(near)], axis=1)
    )[my_index]
    near_receive = jnp.asarray(
        np.stack([routes[n % hop][2][n // hop] for n in range(near)], axis=1)
    )[my_index]
    far_pairs, far_send_table, far_receive_table = colored_moves(count, hop)
    far_send = jnp.asarray(far_send_table.T)[my_index]
    far_receive = jnp.asarray(far_receive_table.T)[my_index]
    doc_ends = jnp.cumsum(lengths).astype(jnp.int32)

    whole_spec = pl.BlockSpec(index_map=lambda m, *_: (0, 0))
    pair_spec = pl.BlockSpec((row_count, pair_width), lambda m, *_: (0, m))
    move_spec = pl.BlockSpec((block_rows, pair_width), lambda m, *_: (0, m))
    run_spec = pl.BlockSpec((hop * block_rows, pair_width), lambda m, *_: (0, m))
    prep = pl.pallas_call(
        prep_kernel,
        grid_spec=pltpu.PrefetchScalarGridSpec(
            num_scalar_prefetch=1,
            grid=(1,),
            in_specs=[whole_spec, whole_spec],
            out_specs=[whole_spec] * (near + 1),
        ),
        out_shape=[jax.ShapeDtypeStruct((row_count, width), jnp.bfloat16)]
        + [jax.ShapeDtypeStruct((block_rows, width), jnp.bfloat16)] * near,
    )
    own_kv, *payloads = prep(near_send, key_rows, value_rows)
    received = [permute(payloads[n], near_pairs[n]) for n in range(near)]

    def near_block(slot, distance):
        first = received[distance - 1]
        second = received[hop + distance - 1]
        return jnp.where(near_receive[distance - 1] == slot, first, second)

    runs = [
        jnp.concatenate([near_block(slot, d) for d in range(1, hop + 1)]) for slot in range(2)
    ]
    far_received = [
        permute(jnp.where(far_send[c] == 1, runs[1], runs[0]), far_pairs[c]) for c in range(2)
    ]

    head_group = QUERY_HEADS // KEY_VALUE_HEADS * HEAD_SIZE
    query_spec = pl.BlockSpec((row_count, head_group), lambda m, *_: (0, m))
    part_spec = pl.BlockSpec((2 * span, pair_width), lambda m, *_: (0, m))
    meta = jnp.concatenate([my_index.reshape(1).astype(jnp.int32), near_receive, far_receive])
    kernel = pl.pallas_call(
        lambda *refs: attention_kernel(
            *refs, count=count, reach=reach, hop=hop, docs=docs, scale=score_scale
        ),
        grid_spec=pltpu.PrefetchScalarGridSpec(
            num_scalar_prefetch=2,
            grid=(KEY_VALUE_HEADS,),
            in_specs=[query_spec, query_spec, pair_spec] + [move_spec] * near + [run_spec] * 2,
            out_specs=[query_spec, query_spec, part_spec],
            scratch_shapes=[pltpu.VMEM((span, pair_width), jnp.bfloat16)],
        ),
        out_shape=[
            jax.ShapeDtypeStruct(queries.shape, jnp.bfloat16),
            jax.ShapeDtypeStruct(queries.shape, jnp.bfloat16),
            jax.ShapeDtypeStruct((2 * span, width), jnp.float32),
        ],
    )
    attended, query_grad, part = kernel(
        meta, doc_ends, queries, output_gradient, own_kv, *received, *far_received
    )
    part = part.reshape(2, window, block_rows, width)

    lower_grad = part[0, reach]
    upper_grad = part[1, reach]
    relay_sum = [jnp.zeros_like(lower_grad), jnp.zeros_like(lower_grad)]
    for n in range(near):
        distance = n % hop + 1
        slot_is_upper = near_receive[n] == 1
        pieces = [
            jnp.where(slot_is_upper, part[1, w], part[0, w])
            for w in (reach - distance, reach - hop - distance)
        ]
        payload = jnp.concatenate(pieces).astype(jnp.bfloat16)
        back = permute(payload, [(t, s) for s, t in near_pairs[n]]).astype(jnp.float32)
        own_back, relay_back = back[:block_rows], back[block_rows:]
        to_upper = near_send[n] == 1
        lower_grad = lower_grad + jnp.where(to_upper, 0.0, own_back)
        upper_grad = upper_grad + jnp.where(to_upper, own_back, 0.0)
        relay_sum[0] = relay_sum[0] + jnp.where(to_upper, 0.0, relay_back)
        relay_sum[1] = relay_sum[1] + jnp.where(to_upper, relay_back, 0.0)
    returned = []
    for c in range(2):
        payload = jnp.where(far_receive[c] == 1, relay_sum[1], relay_sum[0])
        returned.append(
            permute(payload.astype(jnp.bfloat16), [(t, s) for s, t in far_pairs[c]])
        )
    key_width = KEY_VALUE_HEADS * HEAD_SIZE
    finish = pl.pallas_call(
        finish_kernel,
        grid_spec=pltpu.PrefetchScalarGridSpec(
            num_scalar_prefetch=1,
            grid=(1,),
            in_specs=[whole_spec] * 4,
            out_specs=[whole_spec] * 2,
        ),
        out_shape=[jax.ShapeDtypeStruct((row_count, key_width), jnp.bfloat16)] * 2,
    )
    key_grad, value_grad = finish(far_send, lower_grad, upper_grad, *returned)
    return attended, query_grad, key_grad, value_grad


def solution(mesh):
    return jax.shard_map(
        on_device,
        mesh=mesh,
        in_specs=(
            P(("groups", "ctx"), None),
            P(("groups", "ctx"), None),
            P(("groups", "ctx"), None),
            P(("groups", "ctx"), None),
            P("groups"),
        ),
        out_specs=(
            P(("groups", "ctx"), None),
            P(("groups", "ctx"), None),
            P(("groups", "ctx"), None),
            P(("groups", "ctx"), None),
        ),
        check_vma=False,
    )
```

```python
import math

import jax
import jax.numpy as jnp
import numpy as np
from jax import lax
from jax.experimental import pallas as pl
from jax.experimental.pallas import tpu as pltpu
from jax.sharding import PartitionSpec as P

QUERY_HEADS = 16
KEY_VALUE_HEADS = 4
HEAD_SIZE = 128
DOCUMENT_REACH = 8

NEGATIVE_FLOOR = -1e30


def block_home(count, block):
    if block < count:
        return block, 0
    return 2 * count - 1 - block, 1


def colored_moves(count, distance):
    edges = []
    for block in range(2 * count - distance):
        source, source_slot = block_home(count, block)
        target, target_slot = block_home(count, block + distance)
        edges.append((source, source_slot, target, target_slot))
    by_source, by_target = {}, {}
    for i, (s, _, t, _) in enumerate(edges):
        by_source.setdefault(s, []).append(i)
        by_target.setdefault(t, []).append(i)

    def partner(table, key, i):
        rest = [j for j in table[key] if j != i]
        return rest[0] if rest else None

    color = [None] * len(edges)

    def walk(i, through_target):
        while True:
            s, _, t, _ = edges[i]
            j = partner(by_target, t, i) if through_target else partner(by_source, s, i)
            if j is None or color[j] is not None:
                return
            color[j] = 1 - color[i]
            i, through_target = j, not through_target

    def degree(i):
        s, _, t, _ = edges[i]
        return min(len(by_source[s]), len(by_target[t]))

    for i in sorted(range(len(edges)), key=degree):
        if color[i] is None:
            color[i] = 0
            walk(i, True)
            walk(i, False)
    pairs = [[], []]
    send_slot = np.zeros((2, count), np.int32)
    receive_slot = np.full((2, count), -1, np.int32)
    for (s, ss, t, ts), c in zip(edges, color):
        pairs[c].append((s, t))
        send_slot[c, s] = ss
        receive_slot[c, t] = ts
    for c in range(2):
        assert len({s for s, _ in pairs[c]}) == len(pairs[c])
        assert len({t for _, t in pairs[c]}) == len(pairs[c])
    return pairs, send_slot, receive_slot


def permute(value, pairs):
    if not pairs:
        return jnp.zeros_like(value)
    return lax.ppermute(value, "ctx", pairs)


def prep_kernel(send_ref, key_ref, value_ref, own_ref, *pay_refs):
    heads = key_ref.shape[1] // HEAD_SIZE
    both = jnp.concatenate(
        [
            part
            for m in range(heads)
            for part in (
                key_ref[:, m * HEAD_SIZE : (m + 1) * HEAD_SIZE],
                value_ref[:, m * HEAD_SIZE : (m + 1) * HEAD_SIZE],
            )
        ],
        axis=1,
    )
    own_ref[...] = both
    rows = both.shape[0] // 2
    for n, pay_ref in enumerate(pay_refs):
        upper = send_ref[n] == 1

        @pl.when(upper)
        def _():
            pay_ref[...] = both[rows:]

        @pl.when(jnp.logical_not(upper))
        def _():
            pay_ref[...] = both[:rows]


def attention_kernel(
    meta_ref, ends_ref, query_ref, grad_ref, own_ref, *refs, count, reach, hop, docs, scale
):
    near = 2 * hop
    near_refs = refs[:near]
    out_ref, dquery_ref, part_ref = refs[near : near + 3]
    window_ref = refs[near + 3]
    block_rows = own_ref.shape[0] // 2
    window = reach + 1
    span = window * block_rows
    group_width = QUERY_HEADS // KEY_VALUE_HEADS
    my_index = meta_ref[0]

    def fill(w, first, second, first_ref, second_ref, rows):
        @pl.when(first)
        def _():
            window_ref[w * block_rows : (w + 1) * block_rows, :] = first_ref[rows, :]

        @pl.when(jnp.logical_and(second, jnp.logical_not(first)))
        def _():
            window_ref[w * block_rows : (w + 1) * block_rows, :] = second_ref[rows, :]

        @pl.when(jnp.logical_and(jnp.logical_not(second), jnp.logical_not(first)))
        def _():
            window_ref[w * block_rows : (w + 1) * block_rows, :] = jnp.zeros(
                (block_rows, window_ref.shape[1]), window_ref.dtype
            )

    for slot in range(2):
        own_block = my_index if slot == 0 else 2 * count - 1 - my_index
        window_ref[reach * block_rows :, :] = own_ref[
            slot * block_rows : (slot + 1) * block_rows, :
        ]
        for distance in range(1, hop + 1):
            for half in range(2):
                fill(
                    reach - distance - half * hop,
                    meta_ref[distance] == slot,
                    meta_ref[hop + distance] == slot,
                    near_refs[distance - 1],
                    near_refs[hop + distance - 1],
                    slice(half * block_rows, (half + 1) * block_rows),
                )

        query_place = own_block * block_rows + lax.broadcasted_iota(
            jnp.int32, (block_rows, 1), 0
        )
        key_place = (own_block - reach) * block_rows + lax.broadcasted_iota(
            jnp.int32, (1, span), 1
        )
        query_doc = jnp.zeros((block_rows, 1), jnp.int32)
        key_doc = jnp.zeros((1, span), jnp.int32)
        for j in range(docs):
            end = ends_ref[j]
            query_doc = query_doc + (query_place >= end).astype(jnp.int32)
            key_doc = key_doc + (key_place >= end).astype(jnp.int32)
        visible = (query_doc == key_doc) & (key_place <= query_place) & (key_place >= 0)
        mask = jnp.concatenate([visible] * group_width, axis=0)

        rows = slice(slot * block_rows, (slot + 1) * block_rows)
        query = jnp.concatenate(
            [query_ref[rows, g * HEAD_SIZE : (g + 1) * HEAD_SIZE] for g in range(group_width)],
            axis=0,
        )
        grad = jnp.concatenate(
            [grad_ref[rows, g * HEAD_SIZE : (g + 1) * HEAD_SIZE] for g in range(group_width)],
            axis=0,
        )
        keys = window_ref[:, :HEAD_SIZE]
        values = window_ref[:, HEAD_SIZE:]
        contract_last = (((1,), (1,)), ((), ()))
        contract_first = (((0,), (0,)), ((), ()))
        scores = (
            lax.dot_general(query, keys, contract_last, preferred_element_type=jnp.float32)
            * scale
        )
        masked = jnp.where(mask, scores, NEGATIVE_FLOOR)
        row_maximum = jnp.max(masked, axis=1, keepdims=True)
        row_sum = jnp.sum(jnp.exp(masked - row_maximum), axis=1, keepdims=True)
        log_norm = row_maximum + jnp.log(row_sum)
        probs = jnp.exp(masked - log_norm)
        probs_b = probs.astype(jnp.bfloat16)
        attended = jnp.dot(probs_b, values, preferred_element_type=jnp.float32)
        attended_b = attended.astype(jnp.bfloat16)
        delta = jnp.sum(
            grad.astype(jnp.float32) * attended_b.astype(jnp.float32), axis=1, keepdims=True
        )
        dprob = lax.dot_general(grad, values, contract_last, preferred_element_type=jnp.float32)
        dscore = (probs * (dprob - delta)).astype(jnp.bfloat16)
        dquery = jnp.dot(dscore, keys, preferred_element_type=jnp.float32) * scale
        dkey = (
            lax.dot_general(dscore, query, contract_first, preferred_element_type=jnp.float32)
            * scale
        )
        dvalue = lax.dot_general(
            probs_b, grad, contract_first, preferred_element_type=jnp.float32
        )
        dquery_b = dquery.astype(jnp.bfloat16)
        for g in range(group_width):
            cols = slice(g * HEAD_SIZE, (g + 1) * HEAD_SIZE)
            out_ref[rows, cols] = attended_b[g * block_rows : (g + 1) * block_rows]
            dquery_ref[rows, cols] = dquery_b[g * block_rows : (g + 1) * block_rows]
        part_ref[slot * span : (slot + 1) * span, :HEAD_SIZE] = dkey
        part_ref[slot * span : (slot + 1) * span, HEAD_SIZE:] = dvalue


def on_device(queries, key_rows, value_rows, output_gradient, lengths):
    count = lax.axis_size("ctx")
    my_index = lax.axis_index("ctx")
    row_count = queries.shape[0]
    block_rows = row_count // 2
    pair_width = 2 * HEAD_SIZE
    width = KEY_VALUE_HEADS * pair_width
    reach = DOCUMENT_REACH
    hop = reach // 2
    near = 2 * hop
    window = reach + 1
    span = window * block_rows
    docs = lengths.shape[0]
    score_scale = 1.0 / math.sqrt(HEAD_SIZE)

    routes = [colored_moves(count, distance) for distance in range(1, hop + 1)]
    near_pairs = [routes[n % hop][0][n // hop] for n in range(near)]
    near_send = jnp.asarray(
        np.stack([routes[n % hop][1][n // hop] for n in range(near)], axis=1)
    )[my_index]
    near_receive = jnp.asarray(
        np.stack([routes[n % hop][2][n // hop] for n in range(near)], axis=1)
    )[my_index]
    far_pairs, far_send_table, far_receive_table = colored_moves(count, hop)
    far_send = jnp.asarray(far_send_table.T)[my_index]
    far_receive = jnp.asarray(far_receive_table.T)[my_index]
    doc_ends = jnp.cumsum(lengths).astype(jnp.int32)

    whole_spec = pl.BlockSpec(index_map=lambda m, *_: (0, 0))
    pair_spec = pl.BlockSpec((row_count, pair_width), lambda m, *_: (0, m))
    move_spec = pl.BlockSpec((block_rows, pair_width), lambda m, *_: (0, m))
    pair_move_spec = pl.BlockSpec((2 * block_rows, pair_width), lambda m, *_: (0, m))
    prep = pl.pallas_call(
        prep_kernel,
        grid_spec=pltpu.PrefetchScalarGridSpec(
            num_scalar_prefetch=1,
            grid=(1,),
            in_specs=[whole_spec, whole_spec],
            out_specs=[whole_spec] * 3,
        ),
        out_shape=[jax.ShapeDtypeStruct((row_count, width), jnp.bfloat16)]
        + [jax.ShapeDtypeStruct((block_rows, width), jnp.bfloat16)] * 2,
    )
    own_kv, *far_payloads = prep(far_send, key_rows, value_rows)
    far_received = [permute(far_payloads[c], far_pairs[c]) for c in range(2)]
    own_blocks = [own_kv[:block_rows], own_kv[block_rows:]]
    relayed = [
        jnp.where(far_receive[0] == slot, far_received[0], far_received[1]) for slot in range(2)
    ]
    pairs_of = [jnp.concatenate([own_blocks[slot], relayed[slot]]) for slot in range(2)]
    received = [
        permute(jnp.where(near_send[n] == 1, pairs_of[1], pairs_of[0]), near_pairs[n])
        for n in range(near)
    ]

    head_group = QUERY_HEADS // KEY_VALUE_HEADS * HEAD_SIZE
    query_spec = pl.BlockSpec((row_count, head_group), lambda m, *_: (0, m))
    part_spec = pl.BlockSpec((2 * span, pair_width), lambda m, *_: (0, m))
    meta = jnp.concatenate([my_index.reshape(1).astype(jnp.int32), near_receive, far_receive])
    kernel = pl.pallas_call(
        lambda *refs: attention_kernel(
            *refs, count=count, reach=reach, hop=hop, docs=docs, scale=score_scale
        ),
        grid_spec=pltpu.PrefetchScalarGridSpec(
            num_scalar_prefetch=2,
            grid=(KEY_VALUE_HEADS,),
            in_specs=[query_spec, query_spec, pair_spec] + [pair_move_spec] * near,
            out_specs=[query_spec, query_spec, part_spec],
            scratch_shapes=[pltpu.VMEM((span, pair_width), jnp.bfloat16)],
        ),
        out_shape=[
            jax.ShapeDtypeStruct(queries.shape, jnp.bfloat16),
            jax.ShapeDtypeStruct(queries.shape, jnp.bfloat16),
            jax.ShapeDtypeStruct((2 * span, width), jnp.float32),
        ],
    )
    attended, query_grad, part = kernel(
        meta, doc_ends, queries, output_gradient, own_kv, *received
    )
    part = part.reshape(2, window, block_rows, width)

    lower_grad = part[0, reach]
    upper_grad = part[1, reach]
    relay_sum = [jnp.zeros_like(lower_grad), jnp.zeros_like(lower_grad)]
    for n in range(near):
        distance = n % hop + 1
        slot_is_upper = near_receive[n] == 1
        pieces = [
            jnp.where(slot_is_upper, part[1, w], part[0, w])
            for w in (reach - distance, reach - hop - distance)
        ]
        payload = jnp.concatenate(pieces).astype(jnp.bfloat16)
        back = permute(payload, [(t, s) for s, t in near_pairs[n]]).astype(jnp.float32)
        own_back, relay_back = back[:block_rows], back[block_rows:]
        to_upper = near_send[n] == 1
        lower_grad = lower_grad + jnp.where(to_upper, 0.0, own_back)
        upper_grad = upper_grad + jnp.where(to_upper, own_back, 0.0)
        relay_sum[0] = relay_sum[0] + jnp.where(to_upper, 0.0, relay_back)
        relay_sum[1] = relay_sum[1] + jnp.where(to_upper, relay_back, 0.0)
    for c in range(2):
        payload = jnp.where(far_receive[c] == 1, relay_sum[1], relay_sum[0])
        back = permute(payload.astype(jnp.bfloat16), [(t, s) for s, t in far_pairs[c]])
        back = back.astype(jnp.float32)
        lower_grad = lower_grad + jnp.where(far_send[c] == 1, 0.0, back)
        upper_grad = upper_grad + jnp.where(far_send[c] == 1, back, 0.0)
    grad_both = jnp.concatenate([lower_grad, upper_grad]).reshape(
        row_count, KEY_VALUE_HEADS, 2, HEAD_SIZE
    )
    key_width = KEY_VALUE_HEADS * HEAD_SIZE
    return (
        attended,
        query_grad,
        grad_both[:, :, 0].reshape(row_count, key_width).astype(jnp.bfloat16),
        grad_both[:, :, 1].reshape(row_count, key_width).astype(jnp.bfloat16),
    )


def solution(mesh):
    return jax.shard_map(
        on_device,
        mesh=mesh,
        in_specs=(
            P(("groups", "ctx"), None),
            P(("groups", "ctx"), None),
            P(("groups", "ctx"), None),
            P(("groups", "ctx"), None),
            P("groups"),
        ),
        out_specs=(
            P(("groups", "ctx"), None),
            P(("groups", "ctx"), None),
            P(("groups", "ctx"), None),
            P(("groups", "ctx"), None),
        ),
        check_vma=False,
    )
```

```python
import math

import jax
import jax.numpy as jnp
import numpy as np
from jax import lax
from jax.experimental import pallas as pl
from jax.experimental.pallas import tpu as pltpu
from jax.sharding import PartitionSpec as P

QUERY_HEADS = 16
KEY_VALUE_HEADS = 4
HEAD_SIZE = 128
DOCUMENT_REACH = 8

NEGATIVE_FLOOR = -1e30


def block_home(count, block):
    if block < count:
        return block, 0
    return 2 * count - 1 - block, 1


def colored_moves(count, distance):
    edges = []
    for block in range(2 * count - distance):
        source, source_slot = block_home(count, block)
        target, target_slot = block_home(count, block + distance)
        edges.append((source, source_slot, target, target_slot))
    by_source, by_target = {}, {}
    for i, (s, _, t, _) in enumerate(edges):
        by_source.setdefault(s, []).append(i)
        by_target.setdefault(t, []).append(i)

    def partner(table, key, i):
        rest = [j for j in table[key] if j != i]
        return rest[0] if rest else None

    color = [None] * len(edges)

    def walk(i, through_target):
        while True:
            s, _, t, _ = edges[i]
            j = partner(by_target, t, i) if through_target else partner(by_source, s, i)
            if j is None or color[j] is not None:
                return
            color[j] = 1 - color[i]
            i, through_target = j, not through_target

    def degree(i):
        s, _, t, _ = edges[i]
        return min(len(by_source[s]), len(by_target[t]))

    for i in sorted(range(len(edges)), key=degree):
        if color[i] is None:
            color[i] = 0
            walk(i, True)
            walk(i, False)
    pairs = [[], []]
    send_slot = np.zeros((2, count), np.int32)
    receive_slot = np.full((2, count), -1, np.int32)
    for (s, ss, t, ts), c in zip(edges, color):
        pairs[c].append((s, t))
        send_slot[c, s] = ss
        receive_slot[c, t] = ts
    for c in range(2):
        assert len({s for s, _ in pairs[c]}) == len(pairs[c])
        assert len({t for _, t in pairs[c]}) == len(pairs[c])
    return pairs, send_slot, receive_slot


def permute(value, pairs):
    if not pairs:
        return jnp.zeros_like(value)
    return lax.ppermute(value, "ctx", pairs)


def prep_kernel(send_ref, key_ref, value_ref, own_ref, *pay_refs):
    heads = key_ref.shape[1] // HEAD_SIZE
    both = jnp.concatenate(
        [
            part
            for m in range(heads)
            for part in (
                key_ref[:, m * HEAD_SIZE : (m + 1) * HEAD_SIZE],
                value_ref[:, m * HEAD_SIZE : (m + 1) * HEAD_SIZE],
            )
        ],
        axis=1,
    )
    own_ref[...] = both
    rows = both.shape[0] // 2
    for n, pay_ref in enumerate(pay_refs):
        upper = send_ref[n] == 1

        @pl.when(upper)
        def _():
            pay_ref[...] = both[rows:]

        @pl.when(jnp.logical_not(upper))
        def _():
            pay_ref[...] = both[:rows]


def attention_kernel(
    meta_ref, ends_ref, query_ref, grad_ref, own_ref, *refs, count, reach, hop, docs, scale
):
    near = 2 * hop
    near_refs = refs[:near]
    far_refs = refs[near : near + 2]
    out_ref, dquery_ref, own_grad_ref = refs[near + 2 : near + 5]
    pay_refs = refs[near + 5 : 2 * near + 5]
    window_ref = refs[2 * near + 5]
    block_rows = own_ref.shape[0] // 2
    window = reach + 1
    span = window * block_rows
    group_width = QUERY_HEADS // KEY_VALUE_HEADS
    my_index = meta_ref[0]

    def fill(w, first, second, first_ref, second_ref, rows):
        @pl.when(first)
        def _():
            window_ref[w * block_rows : (w + 1) * block_rows, :] = first_ref[rows, :]

        @pl.when(jnp.logical_and(second, jnp.logical_not(first)))
        def _():
            window_ref[w * block_rows : (w + 1) * block_rows, :] = second_ref[rows, :]

        @pl.when(jnp.logical_and(jnp.logical_not(second), jnp.logical_not(first)))
        def _():
            window_ref[w * block_rows : (w + 1) * block_rows, :] = jnp.zeros(
                (block_rows, window_ref.shape[1]), window_ref.dtype
            )

    for n in range(near):

        @pl.when(meta_ref[1 + n] < 0)
        def _():
            pay_refs[n][...] = jnp.zeros(pay_refs[n].shape, pay_refs[n].dtype)

    for slot in range(2):
        own_block = my_index if slot == 0 else 2 * count - 1 - my_index
        window_ref[reach * block_rows :, :] = own_ref[
            slot * block_rows : (slot + 1) * block_rows, :
        ]
        for distance in range(1, hop + 1):
            fill(
                reach - distance,
                meta_ref[distance] == slot,
                meta_ref[hop + distance] == slot,
                near_refs[distance - 1],
                near_refs[hop + distance - 1],
                slice(0, block_rows),
            )
        for k in range(hop):
            fill(
                reach - hop - 1 - k,
                meta_ref[1 + near] == slot,
                meta_ref[2 + near] == slot,
                far_refs[0],
                far_refs[1],
                slice(k * block_rows, (k + 1) * block_rows),
            )

        query_place = own_block * block_rows + lax.broadcasted_iota(
            jnp.int32, (block_rows, 1), 0
        )
        key_place = (own_block - reach) * block_rows + lax.broadcasted_iota(
            jnp.int32, (1, span), 1
        )
        query_doc = jnp.zeros((block_rows, 1), jnp.int32)
        key_doc = jnp.zeros((1, span), jnp.int32)
        for j in range(docs):
            end = ends_ref[j]
            query_doc = query_doc + (query_place >= end).astype(jnp.int32)
            key_doc = key_doc + (key_place >= end).astype(jnp.int32)
        visible = (query_doc == key_doc) & (key_place <= query_place) & (key_place >= 0)
        mask = jnp.concatenate([visible] * group_width, axis=0)

        rows = slice(slot * block_rows, (slot + 1) * block_rows)
        query = jnp.concatenate(
            [query_ref[rows, g * HEAD_SIZE : (g + 1) * HEAD_SIZE] for g in range(group_width)],
            axis=0,
        )
        grad = jnp.concatenate(
            [grad_ref[rows, g * HEAD_SIZE : (g + 1) * HEAD_SIZE] for g in range(group_width)],
            axis=0,
        )
        keys = window_ref[:, :HEAD_SIZE]
        values = window_ref[:, HEAD_SIZE:]
        contract_last = (((1,), (1,)), ((), ()))
        contract_first = (((0,), (0,)), ((), ()))
        scores = (
            lax.dot_general(query, keys, contract_last, preferred_element_type=jnp.float32)
            * scale
        )
        masked = jnp.where(mask, scores, NEGATIVE_FLOOR)
        row_maximum = jnp.max(masked, axis=1, keepdims=True)
        row_sum = jnp.sum(jnp.exp(masked - row_maximum), axis=1, keepdims=True)
        log_norm = row_maximum + jnp.log(row_sum)
        probs = jnp.exp(masked - log_norm)
        probs_b = probs.astype(jnp.bfloat16)
        attended = jnp.dot(probs_b, values, preferred_element_type=jnp.float32)
        attended_b = attended.astype(jnp.bfloat16)
        delta = jnp.sum(
            grad.astype(jnp.float32) * attended_b.astype(jnp.float32), axis=1, keepdims=True
        )
        dprob = lax.dot_general(grad, values, contract_last, preferred_element_type=jnp.float32)
        dscore = (probs * (dprob - delta)).astype(jnp.bfloat16)
        dquery = jnp.dot(dscore, keys, preferred_element_type=jnp.float32) * scale
        dkey = (
            lax.dot_general(dscore, query, contract_first, preferred_element_type=jnp.float32)
            * scale
        )
        dvalue = lax.dot_general(
            probs_b, grad, contract_first, preferred_element_type=jnp.float32
        )
        dquery_b = dquery.astype(jnp.bfloat16)
        for g in range(group_width):
            cols = slice(g * HEAD_SIZE, (g + 1) * HEAD_SIZE)
            out_ref[rows, cols] = attended_b[g * block_rows : (g + 1) * block_rows]
            dquery_ref[rows, cols] = dquery_b[g * block_rows : (g + 1) * block_rows]
        own_grad_ref[rows, :HEAD_SIZE] = dkey[reach * block_rows :]
        own_grad_ref[rows, HEAD_SIZE:] = dvalue[reach * block_rows :]
        for n in range(near):
            distance = n % hop + 1

            @pl.when(meta_ref[1 + n] == slot)
            def _():
                for half in range(2):
                    w = reach - distance - half * hop
                    source = slice(w * block_rows, (w + 1) * block_rows)
                    target = slice(half * block_rows, (half + 1) * block_rows)
                    pay_refs[n][target, :HEAD_SIZE] = dkey[source].astype(jnp.bfloat16)
                    pay_refs[n][target, HEAD_SIZE:] = dvalue[source].astype(jnp.bfloat16)


def on_device(queries, key_rows, value_rows, output_gradient, lengths):
    count = lax.axis_size("ctx")
    my_index = lax.axis_index("ctx")
    row_count = queries.shape[0]
    block_rows = row_count // 2
    pair_width = 2 * HEAD_SIZE
    width = KEY_VALUE_HEADS * pair_width
    reach = DOCUMENT_REACH
    hop = reach // 2
    near = 2 * hop
    window = reach + 1
    span = window * block_rows
    docs = lengths.shape[0]
    score_scale = 1.0 / math.sqrt(HEAD_SIZE)

    routes = [colored_moves(count, distance) for distance in range(1, hop + 1)]
    near_pairs = [routes[n % hop][0][n // hop] for n in range(near)]
    near_send = jnp.asarray(
        np.stack([routes[n % hop][1][n // hop] for n in range(near)], axis=1)
    )[my_index]
    near_receive = jnp.asarray(
        np.stack([routes[n % hop][2][n // hop] for n in range(near)], axis=1)
    )[my_index]
    far_pairs, far_send_table, far_receive_table = colored_moves(count, hop)
    far_send = jnp.asarray(far_send_table.T)[my_index]
    far_receive = jnp.asarray(far_receive_table.T)[my_index]
    doc_ends = jnp.cumsum(lengths).astype(jnp.int32)

    whole_spec = pl.BlockSpec(index_map=lambda m, *_: (0, 0))
    pair_spec = pl.BlockSpec((row_count, pair_width), lambda m, *_: (0, m))
    move_spec = pl.BlockSpec((block_rows, pair_width), lambda m, *_: (0, m))
    run_spec = pl.BlockSpec((hop * block_rows, pair_width), lambda m, *_: (0, m))
    pair_move_spec = pl.BlockSpec((2 * block_rows, pair_width), lambda m, *_: (0, m))
    prep = pl.pallas_call(
        prep_kernel,
        grid_spec=pltpu.PrefetchScalarGridSpec(
            num_scalar_prefetch=1,
            grid=(1,),
            in_specs=[whole_spec, whole_spec],
            out_specs=[whole_spec] * (near + 1),
        ),
        out_shape=[jax.ShapeDtypeStruct((row_count, width), jnp.bfloat16)]
        + [jax.ShapeDtypeStruct((block_rows, width), jnp.bfloat16)] * near,
    )
    own_kv, *payloads = prep(near_send, key_rows, value_rows)
    received = [permute(payloads[n], near_pairs[n]) for n in range(near)]

    def near_block(slot, distance):
        first = received[distance - 1]
        second = received[hop + distance - 1]
        return jnp.where(near_receive[distance - 1] == slot, first, second)

    runs = [
        jnp.concatenate([near_block(slot, d) for d in range(1, hop + 1)]) for slot in range(2)
    ]
    far_received = [
        permute(jnp.where(far_send[c] == 1, runs[1], runs[0]), far_pairs[c]) for c in range(2)
    ]

    head_group = QUERY_HEADS // KEY_VALUE_HEADS * HEAD_SIZE
    query_spec = pl.BlockSpec((row_count, head_group), lambda m, *_: (0, m))
    part_spec = pl.BlockSpec((2 * span, pair_width), lambda m, *_: (0, m))
    meta = jnp.concatenate([my_index.reshape(1).astype(jnp.int32), near_receive, far_receive])
    kernel = pl.pallas_call(
        lambda *refs: attention_kernel(
            *refs, count=count, reach=reach, hop=hop, docs=docs, scale=score_scale
        ),
        grid_spec=pltpu.PrefetchScalarGridSpec(
            num_scalar_prefetch=2,
            grid=(KEY_VALUE_HEADS,),
            in_specs=[query_spec, query_spec, pair_spec] + [move_spec] * near + [run_spec] * 2,
            out_specs=[query_spec, query_spec, pair_spec] + [pair_move_spec] * near,
            scratch_shapes=[pltpu.VMEM((span, pair_width), jnp.bfloat16)],
        ),
        out_shape=[
            jax.ShapeDtypeStruct(queries.shape, jnp.bfloat16),
            jax.ShapeDtypeStruct(queries.shape, jnp.bfloat16),
            jax.ShapeDtypeStruct((row_count, width), jnp.float32),
        ]
        + [jax.ShapeDtypeStruct((2 * block_rows, width), jnp.bfloat16)] * near,
    )
    attended, query_grad, own_grad, *payloads_back = kernel(
        meta, doc_ends, queries, output_gradient, own_kv, *received, *far_received
    )
    lower_grad = own_grad[:block_rows]
    upper_grad = own_grad[block_rows:]
    relay_sum = [jnp.zeros_like(lower_grad), jnp.zeros_like(lower_grad)]
    for n in range(near):
        payload = payloads_back[n]
        back = permute(payload, [(t, s) for s, t in near_pairs[n]]).astype(jnp.float32)
        own_back, relay_back = back[:block_rows], back[block_rows:]
        to_upper = near_send[n] == 1
        lower_grad = lower_grad + jnp.where(to_upper, 0.0, own_back)
        upper_grad = upper_grad + jnp.where(to_upper, own_back, 0.0)
        relay_sum[0] = relay_sum[0] + jnp.where(to_upper, 0.0, relay_back)
        relay_sum[1] = relay_sum[1] + jnp.where(to_upper, relay_back, 0.0)
    for c in range(2):
        payload = jnp.where(far_receive[c] == 1, relay_sum[1], relay_sum[0])
        back = permute(payload.astype(jnp.bfloat16), [(t, s) for s, t in far_pairs[c]])
        back = back.astype(jnp.float32)
        lower_grad = lower_grad + jnp.where(far_send[c] == 1, 0.0, back)
        upper_grad = upper_grad + jnp.where(far_send[c] == 1, back, 0.0)
    grad_both = jnp.concatenate([lower_grad, upper_grad]).reshape(
        row_count, KEY_VALUE_HEADS, 2, HEAD_SIZE
    )
    key_width = KEY_VALUE_HEADS * HEAD_SIZE
    return (
        attended,
        query_grad,
        grad_both[:, :, 0].reshape(row_count, key_width).astype(jnp.bfloat16),
        grad_both[:, :, 1].reshape(row_count, key_width).astype(jnp.bfloat16),
    )


def solution(mesh):
    return jax.shard_map(
        on_device,
        mesh=mesh,
        in_specs=(
            P(("groups", "ctx"), None),
            P(("groups", "ctx"), None),
            P(("groups", "ctx"), None),
            P(("groups", "ctx"), None),
            P("groups"),
        ),
        out_specs=(
            P(("groups", "ctx"), None),
            P(("groups", "ctx"), None),
            P(("groups", "ctx"), None),
            P(("groups", "ctx"), None),
        ),
        check_vma=False,
    )
```

```python
import math

import jax
import jax.numpy as jnp
import numpy as np
from jax import lax
from jax.experimental import pallas as pl
from jax.experimental.pallas import tpu as pltpu
from jax.sharding import PartitionSpec as P

QUERY_HEADS = 16
KEY_VALUE_HEADS = 4
HEAD_SIZE = 128
DOCUMENT_REACH = 8

NEGATIVE_FLOOR = -1e30


def block_home(count, block):
    if block < count:
        return block, 0
    return 2 * count - 1 - block, 1


def colored_moves(count, distance):
    edges = []
    for block in range(2 * count - distance):
        source, source_slot = block_home(count, block)
        target, target_slot = block_home(count, block + distance)
        edges.append((source, source_slot, target, target_slot))
    by_source, by_target = {}, {}
    for i, (s, _, t, _) in enumerate(edges):
        by_source.setdefault(s, []).append(i)
        by_target.setdefault(t, []).append(i)

    def partner(table, key, i):
        rest = [j for j in table[key] if j != i]
        return rest[0] if rest else None

    color = [None] * len(edges)

    def walk(i, through_target):
        while True:
            s, _, t, _ = edges[i]
            j = partner(by_target, t, i) if through_target else partner(by_source, s, i)
            if j is None or color[j] is not None:
                return
            color[j] = 1 - color[i]
            i, through_target = j, not through_target

    def degree(i):
        s, _, t, _ = edges[i]
        return min(len(by_source[s]), len(by_target[t]))

    for i in sorted(range(len(edges)), key=degree):
        if color[i] is None:
            color[i] = 0
            walk(i, True)
            walk(i, False)
    pairs = [[], []]
    send_slot = np.zeros((2, count), np.int32)
    receive_slot = np.full((2, count), -1, np.int32)
    for (s, ss, t, ts), c in zip(edges, color):
        pairs[c].append((s, t))
        send_slot[c, s] = ss
        receive_slot[c, t] = ts
    for c in range(2):
        assert len({s for s, _ in pairs[c]}) == len(pairs[c])
        assert len({t for _, t in pairs[c]}) == len(pairs[c])
    return pairs, send_slot, receive_slot


def permute(value, pairs):
    if not pairs:
        return jnp.zeros_like(value)
    return lax.ppermute(value, "ctx", pairs)


def prep_kernel(send_ref, key_ref, value_ref, own_ref, *pay_refs):
    heads = key_ref.shape[1] // HEAD_SIZE
    both = jnp.concatenate(
        [
            part
            for m in range(heads)
            for part in (
                key_ref[:, m * HEAD_SIZE : (m + 1) * HEAD_SIZE],
                value_ref[:, m * HEAD_SIZE : (m + 1) * HEAD_SIZE],
            )
        ],
        axis=1,
    )
    own_ref[...] = both
    rows = both.shape[0] // 2
    me = lax.axis_index("ctx")
    for n, pay_ref in enumerate(pay_refs):
        upper = send_ref[me * len(pay_refs) + n] == 1

        @pl.when(upper)
        def _():
            pay_ref[...] = both[rows:]

        @pl.when(jnp.logical_not(upper))
        def _():
            pay_ref[...] = both[:rows]


def attention_kernel(
    meta_ref, ends_ref, query_ref, grad_ref, own_ref, *refs, count, reach, hop, docs, scale
):
    near = 2 * hop
    near_refs = refs[:near]
    far_refs = refs[near : near + 2]
    out_ref, dquery_ref, own_grad_ref = refs[near + 2 : near + 5]
    pay_refs = refs[near + 5 : 2 * near + 5]
    window_ref = refs[2 * near + 5]
    block_rows = own_ref.shape[0] // 2
    window = reach + 1
    span = window * block_rows
    group_width = QUERY_HEADS // KEY_VALUE_HEADS
    my_index = meta_ref[0]

    def fill(w, first, second, first_ref, second_ref, rows):
        @pl.when(first)
        def _():
            window_ref[w * block_rows : (w + 1) * block_rows, :] = first_ref[rows, :]

        @pl.when(jnp.logical_and(second, jnp.logical_not(first)))
        def _():
            window_ref[w * block_rows : (w + 1) * block_rows, :] = second_ref[rows, :]

        @pl.when(jnp.logical_and(jnp.logical_not(second), jnp.logical_not(first)))
        def _():
            window_ref[w * block_rows : (w + 1) * block_rows, :] = jnp.zeros(
                (block_rows, window_ref.shape[1]), window_ref.dtype
            )

    for n in range(near):

        @pl.when(meta_ref[1 + n] < 0)
        def _():
            pay_refs[n][...] = jnp.zeros(pay_refs[n].shape, pay_refs[n].dtype)

    for slot in range(2):
        own_block = my_index if slot == 0 else 2 * count - 1 - my_index
        window_ref[reach * block_rows :, :] = own_ref[
            slot * block_rows : (slot + 1) * block_rows, :
        ]
        for distance in range(1, hop + 1):
            fill(
                reach - distance,
                meta_ref[distance] == slot,
                meta_ref[hop + distance] == slot,
                near_refs[distance - 1],
                near_refs[hop + distance - 1],
                slice(0, block_rows),
            )
        for k in range(hop):
            fill(
                reach - hop - 1 - k,
                meta_ref[1 + near] == slot,
                meta_ref[2 + near] == slot,
                far_refs[0],
                far_refs[1],
                slice(k * block_rows, (k + 1) * block_rows),
            )

        query_place = own_block * block_rows + lax.broadcasted_iota(
            jnp.int32, (block_rows, 1), 0
        )
        key_place = (own_block - reach) * block_rows + lax.broadcasted_iota(
            jnp.int32, (1, span), 1
        )
        query_doc = jnp.zeros((block_rows, 1), jnp.int32)
        key_doc = jnp.zeros((1, span), jnp.int32)
        for j in range(docs):
            end = ends_ref[j]
            query_doc = query_doc + (query_place >= end).astype(jnp.int32)
            key_doc = key_doc + (key_place >= end).astype(jnp.int32)
        visible = (query_doc == key_doc) & (key_place <= query_place) & (key_place >= 0)
        mask = jnp.concatenate([visible] * group_width, axis=0)

        rows = slice(slot * block_rows, (slot + 1) * block_rows)
        query = jnp.concatenate(
            [query_ref[rows, g * HEAD_SIZE : (g + 1) * HEAD_SIZE] for g in range(group_width)],
            axis=0,
        )
        grad = jnp.concatenate(
            [grad_ref[rows, g * HEAD_SIZE : (g + 1) * HEAD_SIZE] for g in range(group_width)],
            axis=0,
        )
        keys = window_ref[:, :HEAD_SIZE]
        values = window_ref[:, HEAD_SIZE:]
        contract_last = (((1,), (1,)), ((), ()))
        contract_first = (((0,), (0,)), ((), ()))
        scores = (
            lax.dot_general(query, keys, contract_last, preferred_element_type=jnp.float32)
            * scale
        )
        masked = jnp.where(mask, scores, NEGATIVE_FLOOR)
        row_maximum = jnp.max(masked, axis=1, keepdims=True)
        row_sum = jnp.sum(jnp.exp(masked - row_maximum), axis=1, keepdims=True)
        log_norm = row_maximum + jnp.log(row_sum)
        probs = jnp.exp(masked - log_norm)
        probs_b = probs.astype(jnp.bfloat16)
        attended = jnp.dot(probs_b, values, preferred_element_type=jnp.float32)
        attended_b = attended.astype(jnp.bfloat16)
        delta = jnp.sum(
            grad.astype(jnp.float32) * attended_b.astype(jnp.float32), axis=1, keepdims=True
        )
        dprob = lax.dot_general(grad, values, contract_last, preferred_element_type=jnp.float32)
        dscore = (probs * (dprob - delta)).astype(jnp.bfloat16)
        dquery = jnp.dot(dscore, keys, preferred_element_type=jnp.float32) * scale
        dkey = (
            lax.dot_general(dscore, query, contract_first, preferred_element_type=jnp.float32)
            * scale
        )
        dvalue = lax.dot_general(
            probs_b, grad, contract_first, preferred_element_type=jnp.float32
        )
        dquery_b = dquery.astype(jnp.bfloat16)
        for g in range(group_width):
            cols = slice(g * HEAD_SIZE, (g + 1) * HEAD_SIZE)
            out_ref[rows, cols] = attended_b[g * block_rows : (g + 1) * block_rows]
            dquery_ref[rows, cols] = dquery_b[g * block_rows : (g + 1) * block_rows]
        own_grad_ref[rows, :HEAD_SIZE] = dkey[reach * block_rows :]
        own_grad_ref[rows, HEAD_SIZE:] = dvalue[reach * block_rows :]
        for n in range(near):
            distance = n % hop + 1

            @pl.when(meta_ref[1 + n] == slot)
            def _():
                for half in range(2):
                    w = reach - distance - half * hop
                    source = slice(w * block_rows, (w + 1) * block_rows)
                    target = slice(half * block_rows, (half + 1) * block_rows)
                    pay_refs[n][target, :HEAD_SIZE] = dkey[source].astype(jnp.bfloat16)
                    pay_refs[n][target, HEAD_SIZE:] = dvalue[source].astype(jnp.bfloat16)


def on_device(queries, key_rows, value_rows, output_gradient, lengths):
    count = lax.axis_size("ctx")
    my_index = lax.axis_index("ctx")
    row_count = queries.shape[0]
    block_rows = row_count // 2
    pair_width = 2 * HEAD_SIZE
    width = KEY_VALUE_HEADS * pair_width
    reach = DOCUMENT_REACH
    hop = reach // 2
    near = 2 * hop
    window = reach + 1
    span = window * block_rows
    docs = lengths.shape[0]
    score_scale = 1.0 / math.sqrt(HEAD_SIZE)

    routes = [colored_moves(count, distance) for distance in range(1, hop + 1)]
    near_pairs = [routes[n % hop][0][n // hop] for n in range(near)]
    near_send_table = np.stack([routes[n % hop][1][n // hop] for n in range(near)], axis=1)
    near_send = jnp.asarray(near_send_table)[my_index]
    near_receive = jnp.asarray(
        np.stack([routes[n % hop][2][n // hop] for n in range(near)], axis=1)
    )[my_index]
    far_pairs, far_send_table, far_receive_table = colored_moves(count, hop)
    far_send = jnp.asarray(far_send_table.T)[my_index]
    far_receive = jnp.asarray(far_receive_table.T)[my_index]
    doc_ends = jnp.cumsum(lengths).astype(jnp.int32)

    whole_spec = pl.BlockSpec(index_map=lambda m, *_: (0, 0))
    pair_spec = pl.BlockSpec((row_count, pair_width), lambda m, *_: (0, m))
    move_spec = pl.BlockSpec((block_rows, pair_width), lambda m, *_: (0, m))
    run_spec = pl.BlockSpec((hop * block_rows, pair_width), lambda m, *_: (0, m))
    pair_move_spec = pl.BlockSpec((2 * block_rows, pair_width), lambda m, *_: (0, m))
    prep = pl.pallas_call(
        prep_kernel,
        grid_spec=pltpu.PrefetchScalarGridSpec(
            num_scalar_prefetch=1,
            grid=(1,),
            in_specs=[whole_spec, whole_spec],
            out_specs=[whole_spec] * (near + 1),
        ),
        out_shape=[jax.ShapeDtypeStruct((row_count, width), jnp.bfloat16)]
        + [jax.ShapeDtypeStruct((block_rows, width), jnp.bfloat16)] * near,
    )
    own_kv, *payloads = prep(
        jnp.asarray(near_send_table.reshape(-1).astype(np.int32)), key_rows, value_rows
    )
    received = [permute(payloads[n], near_pairs[n]) for n in range(near)]

    def near_block(slot, distance):
        first = received[distance - 1]
        second = received[hop + distance - 1]
        return jnp.where(near_receive[distance - 1] == slot, first, second)

    runs = [
        jnp.concatenate([near_block(slot, d) for d in range(1, hop + 1)]) for slot in range(2)
    ]
    far_received = [
        permute(jnp.where(far_send[c] == 1, runs[1], runs[0]), far_pairs[c]) for c in range(2)
    ]

    head_group = QUERY_HEADS // KEY_VALUE_HEADS * HEAD_SIZE
    query_spec = pl.BlockSpec((row_count, head_group), lambda m, *_: (0, m))
    part_spec = pl.BlockSpec((2 * span, pair_width), lambda m, *_: (0, m))
    meta = jnp.concatenate([my_index.reshape(1).astype(jnp.int32), near_receive, far_receive])
    kernel = pl.pallas_call(
        lambda *refs: attention_kernel(
            *refs, count=count, reach=reach, hop=hop, docs=docs, scale=score_scale
        ),
        grid_spec=pltpu.PrefetchScalarGridSpec(
            num_scalar_prefetch=2,
            grid=(KEY_VALUE_HEADS,),
            in_specs=[query_spec, query_spec, pair_spec] + [move_spec] * near + [run_spec] * 2,
            out_specs=[query_spec, query_spec, pair_spec] + [pair_move_spec] * near,
            scratch_shapes=[pltpu.VMEM((span, pair_width), jnp.bfloat16)],
        ),
        out_shape=[
            jax.ShapeDtypeStruct(queries.shape, jnp.bfloat16),
            jax.ShapeDtypeStruct(queries.shape, jnp.bfloat16),
            jax.ShapeDtypeStruct((row_count, width), jnp.float32),
        ]
        + [jax.ShapeDtypeStruct((2 * block_rows, width), jnp.bfloat16)] * near,
    )
    attended, query_grad, own_grad, *payloads_back = kernel(
        meta, doc_ends, queries, output_gradient, own_kv, *received, *far_received
    )
    lower_grad = own_grad[:block_rows]
    upper_grad = own_grad[block_rows:]
    relay_sum = [jnp.zeros_like(lower_grad), jnp.zeros_like(lower_grad)]
    for n in range(near):
        payload = payloads_back[n]
        back = permute(payload, [(t, s) for s, t in near_pairs[n]]).astype(jnp.float32)
        own_back, relay_back = back[:block_rows], back[block_rows:]
        to_upper = near_send[n] == 1
        lower_grad = lower_grad + jnp.where(to_upper, 0.0, own_back)
        upper_grad = upper_grad + jnp.where(to_upper, own_back, 0.0)
        relay_sum[0] = relay_sum[0] + jnp.where(to_upper, 0.0, relay_back)
        relay_sum[1] = relay_sum[1] + jnp.where(to_upper, relay_back, 0.0)
    for c in range(2):
        payload = jnp.where(far_receive[c] == 1, relay_sum[1], relay_sum[0])
        back = permute(payload.astype(jnp.bfloat16), [(t, s) for s, t in far_pairs[c]])
        back = back.astype(jnp.float32)
        lower_grad = lower_grad + jnp.where(far_send[c] == 1, 0.0, back)
        upper_grad = upper_grad + jnp.where(far_send[c] == 1, back, 0.0)
    grad_both = jnp.concatenate([lower_grad, upper_grad]).reshape(
        row_count, KEY_VALUE_HEADS, 2, HEAD_SIZE
    )
    key_width = KEY_VALUE_HEADS * HEAD_SIZE
    return (
        attended,
        query_grad,
        grad_both[:, :, 0].reshape(row_count, key_width).astype(jnp.bfloat16),
        grad_both[:, :, 1].reshape(row_count, key_width).astype(jnp.bfloat16),
    )


def solution(mesh):
    return jax.shard_map(
        on_device,
        mesh=mesh,
        in_specs=(
            P(("groups", "ctx"), None),
            P(("groups", "ctx"), None),
            P(("groups", "ctx"), None),
            P(("groups", "ctx"), None),
            P("groups"),
        ),
        out_specs=(
            P(("groups", "ctx"), None),
            P(("groups", "ctx"), None),
            P(("groups", "ctx"), None),
            P(("groups", "ctx"), None),
        ),
        check_vma=False,
    )
```

```python
import math

import jax
import jax.numpy as jnp
import numpy as np
from jax import lax
from jax.experimental import pallas as pl
from jax.experimental.pallas import tpu as pltpu
from jax.sharding import PartitionSpec as P

QUERY_HEADS = 16
KEY_VALUE_HEADS = 4
HEAD_SIZE = 128
DOCUMENT_REACH = 8

NEGATIVE_FLOOR = -1e30


def block_home(count, block):
    if block < count:
        return block, 0
    return 2 * count - 1 - block, 1


def colored_moves(count, distance):
    edges = []
    for block in range(2 * count - distance):
        source, source_slot = block_home(count, block)
        target, target_slot = block_home(count, block + distance)
        edges.append((source, source_slot, target, target_slot))
    by_source, by_target = {}, {}
    for i, (s, _, t, _) in enumerate(edges):
        by_source.setdefault(s, []).append(i)
        by_target.setdefault(t, []).append(i)

    def partner(table, key, i):
        rest = [j for j in table[key] if j != i]
        return rest[0] if rest else None

    color = [None] * len(edges)

    def walk(i, through_target):
        while True:
            s, _, t, _ = edges[i]
            j = partner(by_target, t, i) if through_target else partner(by_source, s, i)
            if j is None or color[j] is not None:
                return
            color[j] = 1 - color[i]
            i, through_target = j, not through_target

    def degree(i):
        s, _, t, _ = edges[i]
        return min(len(by_source[s]), len(by_target[t]))

    for i in sorted(range(len(edges)), key=degree):
        if color[i] is None:
            color[i] = 0
            walk(i, True)
            walk(i, False)
    pairs = [[], []]
    send_slot = np.zeros((2, count), np.int32)
    receive_slot = np.full((2, count), -1, np.int32)
    for (s, ss, t, ts), c in zip(edges, color):
        pairs[c].append((s, t))
        send_slot[c, s] = ss
        receive_slot[c, t] = ts
    for c in range(2):
        assert len({s for s, _ in pairs[c]}) == len(pairs[c])
        assert len({t for _, t in pairs[c]}) == len(pairs[c])
    return pairs, send_slot, receive_slot


def permute(value, pairs):
    if not pairs:
        return jnp.zeros_like(value)
    return lax.ppermute(value, "ctx", pairs)


def prep_kernel(send_ref, key_ref, value_ref, own_ref, *pay_refs):
    heads = key_ref.shape[1] // HEAD_SIZE
    both = jnp.concatenate(
        [
            part
            for m in range(heads)
            for part in (
                key_ref[:, m * HEAD_SIZE : (m + 1) * HEAD_SIZE],
                value_ref[:, m * HEAD_SIZE : (m + 1) * HEAD_SIZE],
            )
        ],
        axis=1,
    )
    own_ref[...] = both
    rows = both.shape[0] // 2
    me = lax.axis_index("ctx")
    for n, pay_ref in enumerate(pay_refs):
        upper = send_ref[me * len(pay_refs) + n] == 1

        @pl.when(upper)
        def _():
            pay_ref[...] = both[rows:]

        @pl.when(jnp.logical_not(upper))
        def _():
            pay_ref[...] = both[:rows]


def attention_kernel(
    meta_ref, ends_ref, query_ref, grad_ref, own_ref, *refs, count, reach, hop, docs, scale
):
    near = 2 * hop
    near_refs = refs[:near]
    far_refs = refs[near : near + 2]
    out_ref, dquery_ref, own_grad_ref = refs[near + 2 : near + 5]
    pay_refs = refs[near + 5 : 2 * near + 5]
    window_ref = refs[2 * near + 5]
    block_rows = own_ref.shape[0] // 2
    window = reach + 1
    span = window * block_rows
    group_width = QUERY_HEADS // KEY_VALUE_HEADS
    my_index = meta_ref[0]

    def fill(w, first, second, first_ref, second_ref, rows):
        take_first = first.astype(jnp.int32)
        take_second = jnp.logical_and(second, jnp.logical_not(first)).astype(jnp.int32)
        shape = (block_rows, window_ref.shape[1])
        chosen = jnp.where(
            jnp.full(shape, take_first, jnp.int32) > 0,
            first_ref[rows, :],
            jnp.where(
                jnp.full(shape, take_second, jnp.int32) > 0,
                second_ref[rows, :],
                jnp.zeros(shape, window_ref.dtype),
            ),
        )
        window_ref[w * block_rows : (w + 1) * block_rows, :] = chosen

    for n in range(near):

        @pl.when(meta_ref[1 + n] < 0)
        def _():
            pay_refs[n][...] = jnp.zeros(pay_refs[n].shape, pay_refs[n].dtype)

    for slot in range(2):
        own_block = my_index if slot == 0 else 2 * count - 1 - my_index
        window_ref[reach * block_rows :, :] = own_ref[
            slot * block_rows : (slot + 1) * block_rows, :
        ]
        for distance in range(1, hop + 1):
            fill(
                reach - distance,
                meta_ref[distance] == slot,
                meta_ref[hop + distance] == slot,
                near_refs[distance - 1],
                near_refs[hop + distance - 1],
                slice(0, block_rows),
            )
        for k in range(hop):
            fill(
                reach - hop - 1 - k,
                meta_ref[1 + near] == slot,
                meta_ref[2 + near] == slot,
                far_refs[0],
                far_refs[1],
                slice(k * block_rows, (k + 1) * block_rows),
            )

        query_place = own_block * block_rows + lax.broadcasted_iota(
            jnp.int32, (block_rows, 1), 0
        )
        key_place = (own_block - reach) * block_rows + lax.broadcasted_iota(
            jnp.int32, (1, span), 1
        )
        query_doc = jnp.zeros((block_rows, 1), jnp.int32)
        key_doc = jnp.zeros((1, span), jnp.int32)
        for j in range(docs):
            end = ends_ref[j]
            query_doc = query_doc + (query_place >= end).astype(jnp.int32)
            key_doc = key_doc + (key_place >= end).astype(jnp.int32)
        visible = (query_doc == key_doc) & (key_place <= query_place) & (key_place >= 0)
        mask = jnp.concatenate([visible] * group_width, axis=0)

        rows = slice(slot * block_rows, (slot + 1) * block_rows)
        query = jnp.concatenate(
            [query_ref[rows, g * HEAD_SIZE : (g + 1) * HEAD_SIZE] for g in range(group_width)],
            axis=0,
        )
        grad = jnp.concatenate(
            [grad_ref[rows, g * HEAD_SIZE : (g + 1) * HEAD_SIZE] for g in range(group_width)],
            axis=0,
        )
        keys = window_ref[:, :HEAD_SIZE]
        values = window_ref[:, HEAD_SIZE:]
        contract_last = (((1,), (1,)), ((), ()))
        contract_first = (((0,), (0,)), ((), ()))
        scores = (
            lax.dot_general(query, keys, contract_last, preferred_element_type=jnp.float32)
            * scale
        )
        masked = jnp.where(mask, scores, NEGATIVE_FLOOR)
        row_maximum = jnp.max(masked, axis=1, keepdims=True)
        row_sum = jnp.sum(jnp.exp(masked - row_maximum), axis=1, keepdims=True)
        log_norm = row_maximum + jnp.log(row_sum)
        probs = jnp.exp(masked - log_norm)
        probs_b = probs.astype(jnp.bfloat16)
        attended = jnp.dot(probs_b, values, preferred_element_type=jnp.float32)
        attended_b = attended.astype(jnp.bfloat16)
        delta = jnp.sum(
            grad.astype(jnp.float32) * attended_b.astype(jnp.float32), axis=1, keepdims=True
        )
        dprob = lax.dot_general(grad, values, contract_last, preferred_element_type=jnp.float32)
        dscore = (probs * (dprob - delta)).astype(jnp.bfloat16)
        dquery = jnp.dot(dscore, keys, preferred_element_type=jnp.float32) * scale
        dkey = (
            lax.dot_general(dscore, query, contract_first, preferred_element_type=jnp.float32)
            * scale
        )
        dvalue = lax.dot_general(
            probs_b, grad, contract_first, preferred_element_type=jnp.float32
        )
        dquery_b = dquery.astype(jnp.bfloat16)
        for g in range(group_width):
            cols = slice(g * HEAD_SIZE, (g + 1) * HEAD_SIZE)
            out_ref[rows, cols] = attended_b[g * block_rows : (g + 1) * block_rows]
            dquery_ref[rows, cols] = dquery_b[g * block_rows : (g + 1) * block_rows]
        own_grad_ref[rows, :HEAD_SIZE] = dkey[reach * block_rows :]
        own_grad_ref[rows, HEAD_SIZE:] = dvalue[reach * block_rows :]
        for n in range(near):
            distance = n % hop + 1

            @pl.when(meta_ref[1 + n] == slot)
            def _():
                for half in range(2):
                    w = reach - distance - half * hop
                    source = slice(w * block_rows, (w + 1) * block_rows)
                    target = slice(half * block_rows, (half + 1) * block_rows)
                    pay_refs[n][target, :HEAD_SIZE] = dkey[source].astype(jnp.bfloat16)
                    pay_refs[n][target, HEAD_SIZE:] = dvalue[source].astype(jnp.bfloat16)


def on_device(queries, key_rows, value_rows, output_gradient, lengths):
    count = lax.axis_size("ctx")
    my_index = lax.axis_index("ctx")
    row_count = queries.shape[0]
    block_rows = row_count // 2
    pair_width = 2 * HEAD_SIZE
    width = KEY_VALUE_HEADS * pair_width
    reach = DOCUMENT_REACH
    hop = reach // 2
    near = 2 * hop
    window = reach + 1
    span = window * block_rows
    docs = lengths.shape[0]
    score_scale = 1.0 / math.sqrt(HEAD_SIZE)

    routes = [colored_moves(count, distance) for distance in range(1, hop + 1)]
    near_pairs = [routes[n % hop][0][n // hop] for n in range(near)]
    near_send_table = np.stack([routes[n % hop][1][n // hop] for n in range(near)], axis=1)
    near_send = jnp.asarray(near_send_table)[my_index]
    near_receive = jnp.asarray(
        np.stack([routes[n % hop][2][n // hop] for n in range(near)], axis=1)
    )[my_index]
    far_pairs, far_send_table, far_receive_table = colored_moves(count, hop)
    far_send = jnp.asarray(far_send_table.T)[my_index]
    far_receive = jnp.asarray(far_receive_table.T)[my_index]
    doc_ends = jnp.cumsum(lengths).astype(jnp.int32)

    whole_spec = pl.BlockSpec(index_map=lambda m, *_: (0, 0))
    pair_spec = pl.BlockSpec((row_count, pair_width), lambda m, *_: (0, m))
    move_spec = pl.BlockSpec((block_rows, pair_width), lambda m, *_: (0, m))
    run_spec = pl.BlockSpec((hop * block_rows, pair_width), lambda m, *_: (0, m))
    pair_move_spec = pl.BlockSpec((2 * block_rows, pair_width), lambda m, *_: (0, m))
    prep = pl.pallas_call(
        prep_kernel,
        grid_spec=pltpu.PrefetchScalarGridSpec(
            num_scalar_prefetch=1,
            grid=(1,),
            in_specs=[whole_spec, whole_spec],
            out_specs=[whole_spec] * (near + 1),
        ),
        out_shape=[jax.ShapeDtypeStruct((row_count, width), jnp.bfloat16)]
        + [jax.ShapeDtypeStruct((block_rows, width), jnp.bfloat16)] * near,
    )
    own_kv, *payloads = prep(
        jnp.asarray(near_send_table.reshape(-1).astype(np.int32)), key_rows, value_rows
    )
    received = [permute(payloads[n], near_pairs[n]) for n in range(near)]

    def near_block(slot, distance):
        first = received[distance - 1]
        second = received[hop + distance - 1]
        return jnp.where(near_receive[distance - 1] == slot, first, second)

    runs = [
        jnp.concatenate([near_block(slot, d) for d in range(1, hop + 1)]) for slot in range(2)
    ]
    far_received = [
        permute(jnp.where(far_send[c] == 1, runs[1], runs[0]), far_pairs[c]) for c in range(2)
    ]

    head_group = QUERY_HEADS // KEY_VALUE_HEADS * HEAD_SIZE
    query_spec = pl.BlockSpec((row_count, head_group), lambda m, *_: (0, m))
    part_spec = pl.BlockSpec((2 * span, pair_width), lambda m, *_: (0, m))
    meta = jnp.concatenate([my_index.reshape(1).astype(jnp.int32), near_receive, far_receive])
    kernel = pl.pallas_call(
        lambda *refs: attention_kernel(
            *refs, count=count, reach=reach, hop=hop, docs=docs, scale=score_scale
        ),
        grid_spec=pltpu.PrefetchScalarGridSpec(
            num_scalar_prefetch=2,
            grid=(KEY_VALUE_HEADS,),
            in_specs=[query_spec, query_spec, pair_spec] + [move_spec] * near + [run_spec] * 2,
            out_specs=[query_spec, query_spec, pair_spec] + [pair_move_spec] * near,
            scratch_shapes=[pltpu.VMEM((span, pair_width), jnp.bfloat16)],
        ),
        out_shape=[
            jax.ShapeDtypeStruct(queries.shape, jnp.bfloat16),
            jax.ShapeDtypeStruct(queries.shape, jnp.bfloat16),
            jax.ShapeDtypeStruct((row_count, width), jnp.float32),
        ]
        + [jax.ShapeDtypeStruct((2 * block_rows, width), jnp.bfloat16)] * near,
    )
    attended, query_grad, own_grad, *payloads_back = kernel(
        meta, doc_ends, queries, output_gradient, own_kv, *received, *far_received
    )
    lower_grad = own_grad[:block_rows]
    upper_grad = own_grad[block_rows:]
    relay_sum = [jnp.zeros_like(lower_grad), jnp.zeros_like(lower_grad)]
    for n in range(near):
        payload = payloads_back[n]
        back = permute(payload, [(t, s) for s, t in near_pairs[n]]).astype(jnp.float32)
        own_back, relay_back = back[:block_rows], back[block_rows:]
        to_upper = near_send[n] == 1
        lower_grad = lower_grad + jnp.where(to_upper, 0.0, own_back)
        upper_grad = upper_grad + jnp.where(to_upper, own_back, 0.0)
        relay_sum[0] = relay_sum[0] + jnp.where(to_upper, 0.0, relay_back)
        relay_sum[1] = relay_sum[1] + jnp.where(to_upper, relay_back, 0.0)
    for c in range(2):
        payload = jnp.where(far_receive[c] == 1, relay_sum[1], relay_sum[0])
        back = permute(payload.astype(jnp.bfloat16), [(t, s) for s, t in far_pairs[c]])
        back = back.astype(jnp.float32)
        lower_grad = lower_grad + jnp.where(far_send[c] == 1, 0.0, back)
        upper_grad = upper_grad + jnp.where(far_send[c] == 1, back, 0.0)
    grad_both = jnp.concatenate([lower_grad, upper_grad]).reshape(
        row_count, KEY_VALUE_HEADS, 2, HEAD_SIZE
    )
    key_width = KEY_VALUE_HEADS * HEAD_SIZE
    return (
        attended,
        query_grad,
        grad_both[:, :, 0].reshape(row_count, key_width).astype(jnp.bfloat16),
        grad_both[:, :, 1].reshape(row_count, key_width).astype(jnp.bfloat16),
    )


def solution(mesh):
    return jax.shard_map(
        on_device,
        mesh=mesh,
        in_specs=(
            P(("groups", "ctx"), None),
            P(("groups", "ctx"), None),
            P(("groups", "ctx"), None),
            P(("groups", "ctx"), None),
            P("groups"),
        ),
        out_specs=(
            P(("groups", "ctx"), None),
            P(("groups", "ctx"), None),
            P(("groups", "ctx"), None),
            P(("groups", "ctx"), None),
        ),
        check_vma=False,
    )
```

```python
import math

import jax
import jax.numpy as jnp
import numpy as np
from jax import lax
from jax.experimental import pallas as pl
from jax.experimental.pallas import tpu as pltpu
from jax.sharding import PartitionSpec as P

QUERY_HEADS = 16
KEY_VALUE_HEADS = 4
HEAD_SIZE = 128
DOCUMENT_REACH = 8

NEGATIVE_FLOOR = -1e30


def block_home(count, block):
    if block < count:
        return block, 0
    return 2 * count - 1 - block, 1


def colored_moves(count, distance):
    edges = []
    for block in range(2 * count - distance):
        source, source_slot = block_home(count, block)
        target, target_slot = block_home(count, block + distance)
        edges.append((source, source_slot, target, target_slot))
    by_source, by_target = {}, {}
    for i, (s, _, t, _) in enumerate(edges):
        by_source.setdefault(s, []).append(i)
        by_target.setdefault(t, []).append(i)

    def partner(table, key, i):
        rest = [j for j in table[key] if j != i]
        return rest[0] if rest else None

    color = [None] * len(edges)

    def walk(i, through_target):
        while True:
            s, _, t, _ = edges[i]
            j = partner(by_target, t, i) if through_target else partner(by_source, s, i)
            if j is None or color[j] is not None:
                return
            color[j] = 1 - color[i]
            i, through_target = j, not through_target

    def degree(i):
        s, _, t, _ = edges[i]
        return min(len(by_source[s]), len(by_target[t]))

    for i in sorted(range(len(edges)), key=degree):
        if color[i] is None:
            color[i] = 0
            walk(i, True)
            walk(i, False)
    pairs = [[], []]
    send_slot = np.zeros((2, count), np.int32)
    receive_slot = np.full((2, count), -1, np.int32)
    for (s, ss, t, ts), c in zip(edges, color):
        pairs[c].append((s, t))
        send_slot[c, s] = ss
        receive_slot[c, t] = ts
    for c in range(2):
        assert len({s for s, _ in pairs[c]}) == len(pairs[c])
        assert len({t for _, t in pairs[c]}) == len(pairs[c])
    return pairs, send_slot, receive_slot


def permute(value, pairs):
    if not pairs:
        return jnp.zeros_like(value)
    return lax.ppermute(value, "ctx", pairs)


def prep_kernel(send_ref, key_ref, value_ref, own_ref, *pay_refs):
    heads = key_ref.shape[1] // HEAD_SIZE
    both = jnp.concatenate(
        [
            part
            for m in range(heads)
            for part in (
                key_ref[:, m * HEAD_SIZE : (m + 1) * HEAD_SIZE],
                value_ref[:, m * HEAD_SIZE : (m + 1) * HEAD_SIZE],
            )
        ],
        axis=1,
    )
    own_ref[...] = both
    rows = both.shape[0] // 2
    me = lax.axis_index("ctx")
    for n, pay_ref in enumerate(pay_refs):
        upper = send_ref[me * len(pay_refs) + n] == 1

        @pl.when(upper)
        def _():
            pay_ref[...] = both[rows:]

        @pl.when(jnp.logical_not(upper))
        def _():
            pay_ref[...] = both[:rows]


def attention_kernel(
    meta_ref, ends_ref, query_ref, grad_ref, own_ref, *refs, count, reach, hop, docs, scale
):
    near = 2 * hop
    near_refs = refs[:near]
    far_refs = refs[near : near + 2]
    out_ref, dquery_ref, own_grad_ref = refs[near + 2 : near + 5]
    pay_refs = refs[near + 5 : 2 * near + 5]
    window_ref = refs[2 * near + 5]
    block_rows = own_ref.shape[0] // 2
    window = reach + 1
    span = window * block_rows
    group_width = QUERY_HEADS // KEY_VALUE_HEADS
    my_index = meta_ref[0]

    def fill(w, first, second, first_ref, second_ref, rows):
        take_first = first.astype(jnp.int32)
        take_second = jnp.logical_and(second, jnp.logical_not(first)).astype(jnp.int32)
        shape = (block_rows, window_ref.shape[1])
        chosen = jnp.where(
            jnp.full(shape, take_first, jnp.int32) > 0,
            first_ref[rows, :],
            jnp.where(
                jnp.full(shape, take_second, jnp.int32) > 0,
                second_ref[rows, :],
                jnp.zeros(shape, window_ref.dtype),
            ),
        )
        window_ref[w * block_rows : (w + 1) * block_rows, :] = chosen

    for slot in range(2):
        own_block = my_index if slot == 0 else 2 * count - 1 - my_index
        window_ref[reach * block_rows :, :] = own_ref[
            slot * block_rows : (slot + 1) * block_rows, :
        ]
        for distance in range(1, hop + 1):
            fill(
                reach - distance,
                meta_ref[distance] == slot,
                meta_ref[hop + distance] == slot,
                near_refs[distance - 1],
                near_refs[hop + distance - 1],
                slice(0, block_rows),
            )
        for k in range(hop):
            fill(
                reach - hop - 1 - k,
                meta_ref[1 + near] == slot,
                meta_ref[2 + near] == slot,
                far_refs[0],
                far_refs[1],
                slice(k * block_rows, (k + 1) * block_rows),
            )

        query_place = own_block * block_rows + lax.broadcasted_iota(
            jnp.int32, (block_rows, 1), 0
        )
        key_place = (own_block - reach) * block_rows + lax.broadcasted_iota(
            jnp.int32, (1, span), 1
        )
        query_doc = jnp.zeros((block_rows, 1), jnp.int32)
        key_doc = jnp.zeros((1, span), jnp.int32)
        for j in range(docs):
            end = ends_ref[j]
            query_doc = query_doc + (query_place >= end).astype(jnp.int32)
            key_doc = key_doc + (key_place >= end).astype(jnp.int32)
        visible = (query_doc == key_doc) & (key_place <= query_place) & (key_place >= 0)
        mask = jnp.concatenate([visible] * group_width, axis=0)

        rows = slice(slot * block_rows, (slot + 1) * block_rows)
        query = jnp.concatenate(
            [query_ref[rows, g * HEAD_SIZE : (g + 1) * HEAD_SIZE] for g in range(group_width)],
            axis=0,
        )
        grad = jnp.concatenate(
            [grad_ref[rows, g * HEAD_SIZE : (g + 1) * HEAD_SIZE] for g in range(group_width)],
            axis=0,
        )
        keys = window_ref[:, :HEAD_SIZE]
        values = window_ref[:, HEAD_SIZE:]
        contract_last = (((1,), (1,)), ((), ()))
        contract_first = (((0,), (0,)), ((), ()))
        scores = (
            lax.dot_general(query, keys, contract_last, preferred_element_type=jnp.float32)
            * scale
        )
        masked = jnp.where(mask, scores, NEGATIVE_FLOOR)
        row_maximum = jnp.max(masked, axis=1, keepdims=True)
        row_sum = jnp.sum(jnp.exp(masked - row_maximum), axis=1, keepdims=True)
        log_norm = row_maximum + jnp.log(row_sum)
        probs = jnp.exp(masked - log_norm)
        probs_b = probs.astype(jnp.bfloat16)
        attended = jnp.dot(probs_b, values, preferred_element_type=jnp.float32)
        attended_b = attended.astype(jnp.bfloat16)
        delta = jnp.sum(
            grad.astype(jnp.float32) * attended_b.astype(jnp.float32), axis=1, keepdims=True
        )
        dprob = lax.dot_general(grad, values, contract_last, preferred_element_type=jnp.float32)
        dscore = (probs * (dprob - delta)).astype(jnp.bfloat16)
        dquery = jnp.dot(dscore, keys, preferred_element_type=jnp.float32) * scale
        dkey = (
            lax.dot_general(dscore, query, contract_first, preferred_element_type=jnp.float32)
            * scale
        )
        dvalue = lax.dot_general(
            probs_b, grad, contract_first, preferred_element_type=jnp.float32
        )
        dquery_b = dquery.astype(jnp.bfloat16)
        for g in range(group_width):
            cols = slice(g * HEAD_SIZE, (g + 1) * HEAD_SIZE)
            out_ref[rows, cols] = attended_b[g * block_rows : (g + 1) * block_rows]
            dquery_ref[rows, cols] = dquery_b[g * block_rows : (g + 1) * block_rows]
        own_grad_ref[rows, :HEAD_SIZE] = dkey[reach * block_rows :]
        own_grad_ref[rows, HEAD_SIZE:] = dvalue[reach * block_rows :]
        for n in range(near):
            distance = n % hop + 1
            mine = meta_ref[1 + n] == slot
            for half in range(2):
                w = reach - distance - half * hop
                source = slice(w * block_rows, (w + 1) * block_rows)
                target = slice(half * block_rows, (half + 1) * block_rows)
                fresh = jnp.concatenate([dkey[source], dvalue[source]], axis=1).astype(
                    jnp.bfloat16
                )
                if slot == 0:
                    kept = jnp.zeros(fresh.shape, fresh.dtype)
                else:
                    kept = pay_refs[n][target, :]
                pick = jnp.full(fresh.shape, mine.astype(jnp.int32), jnp.int32) > 0
                pay_refs[n][target, :] = jnp.where(pick, fresh, kept)


def on_device(queries, key_rows, value_rows, output_gradient, lengths):
    count = lax.axis_size("ctx")
    my_index = lax.axis_index("ctx")
    row_count = queries.shape[0]
    block_rows = row_count // 2
    pair_width = 2 * HEAD_SIZE
    width = KEY_VALUE_HEADS * pair_width
    reach = DOCUMENT_REACH
    hop = reach // 2
    near = 2 * hop
    window = reach + 1
    span = window * block_rows
    docs = lengths.shape[0]
    score_scale = 1.0 / math.sqrt(HEAD_SIZE)

    routes = [colored_moves(count, distance) for distance in range(1, hop + 1)]
    near_pairs = [routes[n % hop][0][n // hop] for n in range(near)]
    near_send_table = np.stack([routes[n % hop][1][n // hop] for n in range(near)], axis=1)
    near_send = jnp.asarray(near_send_table)[my_index]
    near_receive = jnp.asarray(
        np.stack([routes[n % hop][2][n // hop] for n in range(near)], axis=1)
    )[my_index]
    far_pairs, far_send_table, far_receive_table = colored_moves(count, hop)
    far_send = jnp.asarray(far_send_table.T)[my_index]
    far_receive = jnp.asarray(far_receive_table.T)[my_index]
    doc_ends = jnp.cumsum(lengths).astype(jnp.int32)

    whole_spec = pl.BlockSpec(index_map=lambda m, *_: (0, 0))
    pair_spec = pl.BlockSpec((row_count, pair_width), lambda m, *_: (0, m))
    move_spec = pl.BlockSpec((block_rows, pair_width), lambda m, *_: (0, m))
    run_spec = pl.BlockSpec((hop * block_rows, pair_width), lambda m, *_: (0, m))
    pair_move_spec = pl.BlockSpec((2 * block_rows, pair_width), lambda m, *_: (0, m))
    prep = pl.pallas_call(
        prep_kernel,
        grid_spec=pltpu.PrefetchScalarGridSpec(
            num_scalar_prefetch=1,
            grid=(1,),
            in_specs=[whole_spec, whole_spec],
            out_specs=[whole_spec] * (near + 1),
        ),
        out_shape=[jax.ShapeDtypeStruct((row_count, width), jnp.bfloat16)]
        + [jax.ShapeDtypeStruct((block_rows, width), jnp.bfloat16)] * near,
    )
    own_kv, *payloads = prep(
        jnp.asarray(near_send_table.reshape(-1).astype(np.int32)), key_rows, value_rows
    )
    received = [permute(payloads[n], near_pairs[n]) for n in range(near)]

    def near_block(slot, distance):
        first = received[distance - 1]
        second = received[hop + distance - 1]
        return jnp.where(near_receive[distance - 1] == slot, first, second)

    runs = [
        jnp.concatenate([near_block(slot, d) for d in range(1, hop + 1)]) for slot in range(2)
    ]
    far_received = [
        permute(jnp.where(far_send[c] == 1, runs[1], runs[0]), far_pairs[c]) for c in range(2)
    ]

    head_group = QUERY_HEADS // KEY_VALUE_HEADS * HEAD_SIZE
    query_spec = pl.BlockSpec((row_count, head_group), lambda m, *_: (0, m))
    part_spec = pl.BlockSpec((2 * span, pair_width), lambda m, *_: (0, m))
    meta = jnp.concatenate([my_index.reshape(1).astype(jnp.int32), near_receive, far_receive])
    kernel = pl.pallas_call(
        lambda *refs: attention_kernel(
            *refs, count=count, reach=reach, hop=hop, docs=docs, scale=score_scale
        ),
        grid_spec=pltpu.PrefetchScalarGridSpec(
            num_scalar_prefetch=2,
            grid=(KEY_VALUE_HEADS,),
            in_specs=[query_spec, query_spec, pair_spec] + [move_spec] * near + [run_spec] * 2,
            out_specs=[query_spec, query_spec, pair_spec] + [pair_move_spec] * near,
            scratch_shapes=[pltpu.VMEM((span, pair_width), jnp.bfloat16)],
        ),
        out_shape=[
            jax.ShapeDtypeStruct(queries.shape, jnp.bfloat16),
            jax.ShapeDtypeStruct(queries.shape, jnp.bfloat16),
            jax.ShapeDtypeStruct((row_count, width), jnp.float32),
        ]
        + [jax.ShapeDtypeStruct((2 * block_rows, width), jnp.bfloat16)] * near,
    )
    attended, query_grad, own_grad, *payloads_back = kernel(
        meta, doc_ends, queries, output_gradient, own_kv, *received, *far_received
    )
    lower_grad = own_grad[:block_rows]
    upper_grad = own_grad[block_rows:]
    relay_sum = [jnp.zeros_like(lower_grad), jnp.zeros_like(lower_grad)]
    for n in range(near):
        payload = payloads_back[n]
        back = permute(payload, [(t, s) for s, t in near_pairs[n]]).astype(jnp.float32)
        own_back, relay_back = back[:block_rows], back[block_rows:]
        to_upper = near_send[n] == 1
        lower_grad = lower_grad + jnp.where(to_upper, 0.0, own_back)
        upper_grad = upper_grad + jnp.where(to_upper, own_back, 0.0)
        relay_sum[0] = relay_sum[0] + jnp.where(to_upper, 0.0, relay_back)
        relay_sum[1] = relay_sum[1] + jnp.where(to_upper, relay_back, 0.0)
    for c in range(2):
        payload = jnp.where(far_receive[c] == 1, relay_sum[1], relay_sum[0])
        back = permute(payload.astype(jnp.bfloat16), [(t, s) for s, t in far_pairs[c]])
        back = back.astype(jnp.float32)
        lower_grad = lower_grad + jnp.where(far_send[c] == 1, 0.0, back)
        upper_grad = upper_grad + jnp.where(far_send[c] == 1, back, 0.0)
    grad_both = jnp.concatenate([lower_grad, upper_grad]).reshape(
        row_count, KEY_VALUE_HEADS, 2, HEAD_SIZE
    )
    key_width = KEY_VALUE_HEADS * HEAD_SIZE
    return (
        attended,
        query_grad,
        grad_both[:, :, 0].reshape(row_count, key_width).astype(jnp.bfloat16),
        grad_both[:, :, 1].reshape(row_count, key_width).astype(jnp.bfloat16),
    )


def solution(mesh):
    return jax.shard_map(
        on_device,
        mesh=mesh,
        in_specs=(
            P(("groups", "ctx"), None),
            P(("groups", "ctx"), None),
            P(("groups", "ctx"), None),
            P(("groups", "ctx"), None),
            P("groups"),
        ),
        out_specs=(
            P(("groups", "ctx"), None),
            P(("groups", "ctx"), None),
            P(("groups", "ctx"), None),
            P(("groups", "ctx"), None),
        ),
        check_vma=False,
    )
```

```python
import math

import jax
import jax.numpy as jnp
import numpy as np
from jax import lax
from jax.experimental import pallas as pl
from jax.experimental.pallas import tpu as pltpu
from jax.sharding import PartitionSpec as P

QUERY_HEADS = 16
KEY_VALUE_HEADS = 4
HEAD_SIZE = 128
DOCUMENT_REACH = 8

NEGATIVE_FLOOR = -1e30


def block_home(count, block):
    if block < count:
        return block, 0
    return 2 * count - 1 - block, 1


def colored_moves(count, distance):
    edges = []
    for block in range(2 * count - distance):
        source, source_slot = block_home(count, block)
        target, target_slot = block_home(count, block + distance)
        edges.append((source, source_slot, target, target_slot))
    by_source, by_target = {}, {}
    for i, (s, _, t, _) in enumerate(edges):
        by_source.setdefault(s, []).append(i)
        by_target.setdefault(t, []).append(i)

    def partner(table, key, i):
        rest = [j for j in table[key] if j != i]
        return rest[0] if rest else None

    color = [None] * len(edges)

    def walk(i, through_target):
        while True:
            s, _, t, _ = edges[i]
            j = partner(by_target, t, i) if through_target else partner(by_source, s, i)
            if j is None or color[j] is not None:
                return
            color[j] = 1 - color[i]
            i, through_target = j, not through_target

    def degree(i):
        s, _, t, _ = edges[i]
        return min(len(by_source[s]), len(by_target[t]))

    for i in sorted(range(len(edges)), key=degree):
        if color[i] is None:
            color[i] = 0
            walk(i, True)
            walk(i, False)
    pairs = [[], []]
    send_slot = np.zeros((2, count), np.int32)
    receive_slot = np.full((2, count), -1, np.int32)
    for (s, ss, t, ts), c in zip(edges, color):
        pairs[c].append((s, t))
        send_slot[c, s] = ss
        receive_slot[c, t] = ts
    for c in range(2):
        assert len({s for s, _ in pairs[c]}) == len(pairs[c])
        assert len({t for _, t in pairs[c]}) == len(pairs[c])
    return pairs, send_slot, receive_slot


def permute(value, pairs):
    if not pairs:
        return jnp.zeros_like(value)
    return lax.ppermute(value, "ctx", pairs)


def prep_kernel(send_ref, key_ref, value_ref, own_ref, *pay_refs):
    heads = key_ref.shape[1] // HEAD_SIZE
    both = jnp.concatenate(
        [
            part
            for m in range(heads)
            for part in (
                key_ref[:, m * HEAD_SIZE : (m + 1) * HEAD_SIZE],
                value_ref[:, m * HEAD_SIZE : (m + 1) * HEAD_SIZE],
            )
        ],
        axis=1,
    )
    own_ref[...] = both
    rows = both.shape[0] // 2
    me = lax.axis_index("ctx")
    lower_half, upper_half = both[:rows], both[rows:]
    for n, pay_ref in enumerate(pay_refs):
        upper = send_ref[me * len(pay_refs) + n]
        pick = jnp.full(lower_half.shape, upper, jnp.int32) == 1
        pay_ref[...] = jnp.where(pick, upper_half, lower_half)


def attention_kernel(
    meta_ref, ends_ref, query_ref, grad_ref, own_ref, *refs, count, reach, hop, docs, scale
):
    near = 2 * hop
    near_refs = refs[:near]
    far_refs = refs[near : near + 2]
    out_ref, dquery_ref, own_grad_ref = refs[near + 2 : near + 5]
    pay_refs = refs[near + 5 : 2 * near + 5]
    window_ref = refs[2 * near + 5]
    block_rows = own_ref.shape[0] // 2
    window = reach + 1
    span = window * block_rows
    group_width = QUERY_HEADS // KEY_VALUE_HEADS
    my_index = meta_ref[0]

    def fill(w, first, second, first_ref, second_ref, rows):
        take_first = first.astype(jnp.int32)
        take_second = jnp.logical_and(second, jnp.logical_not(first)).astype(jnp.int32)
        shape = (block_rows, window_ref.shape[1])
        chosen = jnp.where(
            jnp.full(shape, take_first, jnp.int32) > 0,
            first_ref[rows, :],
            jnp.where(
                jnp.full(shape, take_second, jnp.int32) > 0,
                second_ref[rows, :],
                jnp.zeros(shape, window_ref.dtype),
            ),
        )
        window_ref[w * block_rows : (w + 1) * block_rows, :] = chosen

    for slot in range(2):
        own_block = my_index if slot == 0 else 2 * count - 1 - my_index
        window_ref[reach * block_rows :, :] = own_ref[
            slot * block_rows : (slot + 1) * block_rows, :
        ]
        for distance in range(1, hop + 1):
            fill(
                reach - distance,
                meta_ref[distance] == slot,
                meta_ref[hop + distance] == slot,
                near_refs[distance - 1],
                near_refs[hop + distance - 1],
                slice(0, block_rows),
            )
        for k in range(hop):
            fill(
                reach - hop - 1 - k,
                meta_ref[1 + near] == slot,
                meta_ref[2 + near] == slot,
                far_refs[0],
                far_refs[1],
                slice(k * block_rows, (k + 1) * block_rows),
            )

        query_place = own_block * block_rows + lax.broadcasted_iota(
            jnp.int32, (block_rows, 1), 0
        )
        key_place = (own_block - reach) * block_rows + lax.broadcasted_iota(
            jnp.int32, (1, span), 1
        )
        query_doc = jnp.zeros((block_rows, 1), jnp.int32)
        key_doc = jnp.zeros((1, span), jnp.int32)
        for j in range(docs):
            end = ends_ref[j]
            query_doc = query_doc + (query_place >= end).astype(jnp.int32)
            key_doc = key_doc + (key_place >= end).astype(jnp.int32)
        visible = (query_doc == key_doc) & (key_place <= query_place) & (key_place >= 0)
        mask = jnp.concatenate([visible] * group_width, axis=0)

        rows = slice(slot * block_rows, (slot + 1) * block_rows)
        query = jnp.concatenate(
            [query_ref[rows, g * HEAD_SIZE : (g + 1) * HEAD_SIZE] for g in range(group_width)],
            axis=0,
        )
        grad = jnp.concatenate(
            [grad_ref[rows, g * HEAD_SIZE : (g + 1) * HEAD_SIZE] for g in range(group_width)],
            axis=0,
        )
        keys = window_ref[:, :HEAD_SIZE]
        values = window_ref[:, HEAD_SIZE:]
        contract_last = (((1,), (1,)), ((), ()))
        contract_first = (((0,), (0,)), ((), ()))
        scores = (
            lax.dot_general(query, keys, contract_last, preferred_element_type=jnp.float32)
            * scale
        )
        masked = jnp.where(mask, scores, NEGATIVE_FLOOR)
        row_maximum = jnp.max(masked, axis=1, keepdims=True)
        row_sum = jnp.sum(jnp.exp(masked - row_maximum), axis=1, keepdims=True)
        log_norm = row_maximum + jnp.log(row_sum)
        probs = jnp.exp(masked - log_norm)
        probs_b = probs.astype(jnp.bfloat16)
        attended = jnp.dot(probs_b, values, preferred_element_type=jnp.float32)
        attended_b = attended.astype(jnp.bfloat16)
        delta = jnp.sum(
            grad.astype(jnp.float32) * attended_b.astype(jnp.float32), axis=1, keepdims=True
        )
        dprob = lax.dot_general(grad, values, contract_last, preferred_element_type=jnp.float32)
        dscore = (probs * (dprob - delta)).astype(jnp.bfloat16)
        dquery = jnp.dot(dscore, keys, preferred_element_type=jnp.float32) * scale
        dkey = (
            lax.dot_general(dscore, query, contract_first, preferred_element_type=jnp.float32)
            * scale
        )
        dvalue = lax.dot_general(
            probs_b, grad, contract_first, preferred_element_type=jnp.float32
        )
        dquery_b = dquery.astype(jnp.bfloat16)
        for g in range(group_width):
            cols = slice(g * HEAD_SIZE, (g + 1) * HEAD_SIZE)
            out_ref[rows, cols] = attended_b[g * block_rows : (g + 1) * block_rows]
            dquery_ref[rows, cols] = dquery_b[g * block_rows : (g + 1) * block_rows]
        own_grad_ref[rows, :HEAD_SIZE] = dkey[reach * block_rows :]
        own_grad_ref[rows, HEAD_SIZE:] = dvalue[reach * block_rows :]
        for n in range(near):
            distance = n % hop + 1
            mine = meta_ref[1 + n] == slot
            for half in range(2):
                w = reach - distance - half * hop
                source = slice(w * block_rows, (w + 1) * block_rows)
                target = slice(half * block_rows, (half + 1) * block_rows)
                fresh = jnp.concatenate([dkey[source], dvalue[source]], axis=1).astype(
                    jnp.bfloat16
                )
                if slot == 0:
                    kept = jnp.zeros(fresh.shape, fresh.dtype)
                else:
                    kept = pay_refs[n][target, :]
                pick = jnp.full(fresh.shape, mine.astype(jnp.int32), jnp.int32) > 0
                pay_refs[n][target, :] = jnp.where(pick, fresh, kept)


def on_device(queries, key_rows, value_rows, output_gradient, lengths):
    count = lax.axis_size("ctx")
    my_index = lax.axis_index("ctx")
    row_count = queries.shape[0]
    block_rows = row_count // 2
    pair_width = 2 * HEAD_SIZE
    width = KEY_VALUE_HEADS * pair_width
    reach = DOCUMENT_REACH
    hop = reach // 2
    near = 2 * hop
    window = reach + 1
    span = window * block_rows
    docs = lengths.shape[0]
    score_scale = 1.0 / math.sqrt(HEAD_SIZE)

    routes = [colored_moves(count, distance) for distance in range(1, hop + 1)]
    near_pairs = [routes[n % hop][0][n // hop] for n in range(near)]
    near_send_table = np.stack([routes[n % hop][1][n // hop] for n in range(near)], axis=1)
    near_send = jnp.asarray(near_send_table)[my_index]
    near_receive = jnp.asarray(
        np.stack([routes[n % hop][2][n // hop] for n in range(near)], axis=1)
    )[my_index]
    far_pairs, far_send_table, far_receive_table = colored_moves(count, hop)
    far_send = jnp.asarray(far_send_table.T)[my_index]
    far_receive = jnp.asarray(far_receive_table.T)[my_index]
    doc_ends = jnp.cumsum(lengths).astype(jnp.int32)

    whole_spec = pl.BlockSpec(index_map=lambda m, *_: (0, 0))
    pair_spec = pl.BlockSpec((row_count, pair_width), lambda m, *_: (0, m))
    move_spec = pl.BlockSpec((block_rows, pair_width), lambda m, *_: (0, m))
    run_spec = pl.BlockSpec((hop * block_rows, pair_width), lambda m, *_: (0, m))
    pair_move_spec = pl.BlockSpec((2 * block_rows, pair_width), lambda m, *_: (0, m))
    prep = pl.pallas_call(
        prep_kernel,
        grid_spec=pltpu.PrefetchScalarGridSpec(
            num_scalar_prefetch=1,
            grid=(1,),
            in_specs=[whole_spec, whole_spec],
            out_specs=[whole_spec] * (near + 1),
        ),
        out_shape=[jax.ShapeDtypeStruct((row_count, width), jnp.bfloat16)]
        + [jax.ShapeDtypeStruct((block_rows, width), jnp.bfloat16)] * near,
    )
    own_kv, *payloads = prep(
        jnp.asarray(near_send_table.reshape(-1).astype(np.int32)), key_rows, value_rows
    )
    received = [permute(payloads[n], near_pairs[n]) for n in range(near)]

    def near_block(slot, distance):
        first = received[distance - 1]
        second = received[hop + distance - 1]
        return jnp.where(near_receive[distance - 1] == slot, first, second)

    runs = [
        jnp.concatenate([near_block(slot, d) for d in range(1, hop + 1)]) for slot in range(2)
    ]
    far_received = [
        permute(jnp.where(far_send[c] == 1, runs[1], runs[0]), far_pairs[c]) for c in range(2)
    ]

    head_group = QUERY_HEADS // KEY_VALUE_HEADS * HEAD_SIZE
    query_spec = pl.BlockSpec((row_count, head_group), lambda m, *_: (0, m))
    part_spec = pl.BlockSpec((2 * span, pair_width), lambda m, *_: (0, m))
    meta = jnp.concatenate([my_index.reshape(1).astype(jnp.int32), near_receive, far_receive])
    kernel = pl.pallas_call(
        lambda *refs: attention_kernel(
            *refs, count=count, reach=reach, hop=hop, docs=docs, scale=score_scale
        ),
        grid_spec=pltpu.PrefetchScalarGridSpec(
            num_scalar_prefetch=2,
            grid=(KEY_VALUE_HEADS,),
            in_specs=[query_spec, query_spec, pair_spec] + [move_spec] * near + [run_spec] * 2,
            out_specs=[query_spec, query_spec, pair_spec] + [pair_move_spec] * near,
            scratch_shapes=[pltpu.VMEM((span, pair_width), jnp.bfloat16)],
        ),
        out_shape=[
            jax.ShapeDtypeStruct(queries.shape, jnp.bfloat16),
            jax.ShapeDtypeStruct(queries.shape, jnp.bfloat16),
            jax.ShapeDtypeStruct((row_count, width), jnp.float32),
        ]
        + [jax.ShapeDtypeStruct((2 * block_rows, width), jnp.bfloat16)] * near,
    )
    attended, query_grad, own_grad, *payloads_back = kernel(
        meta, doc_ends, queries, output_gradient, own_kv, *received, *far_received
    )
    lower_grad = own_grad[:block_rows]
    upper_grad = own_grad[block_rows:]
    relay_sum = [jnp.zeros_like(lower_grad), jnp.zeros_like(lower_grad)]
    for n in range(near):
        payload = payloads_back[n]
        back = permute(payload, [(t, s) for s, t in near_pairs[n]]).astype(jnp.float32)
        own_back, relay_back = back[:block_rows], back[block_rows:]
        to_upper = near_send[n] == 1
        lower_grad = lower_grad + jnp.where(to_upper, 0.0, own_back)
        upper_grad = upper_grad + jnp.where(to_upper, own_back, 0.0)
        relay_sum[0] = relay_sum[0] + jnp.where(to_upper, 0.0, relay_back)
        relay_sum[1] = relay_sum[1] + jnp.where(to_upper, relay_back, 0.0)
    for c in range(2):
        payload = jnp.where(far_receive[c] == 1, relay_sum[1], relay_sum[0])
        back = permute(payload.astype(jnp.bfloat16), [(t, s) for s, t in far_pairs[c]])
        back = back.astype(jnp.float32)
        lower_grad = lower_grad + jnp.where(far_send[c] == 1, 0.0, back)
        upper_grad = upper_grad + jnp.where(far_send[c] == 1, back, 0.0)
    grad_both = jnp.concatenate([lower_grad, upper_grad]).reshape(
        row_count, KEY_VALUE_HEADS, 2, HEAD_SIZE
    )
    key_width = KEY_VALUE_HEADS * HEAD_SIZE
    return (
        attended,
        query_grad,
        grad_both[:, :, 0].reshape(row_count, key_width).astype(jnp.bfloat16),
        grad_both[:, :, 1].reshape(row_count, key_width).astype(jnp.bfloat16),
    )


def solution(mesh):
    return jax.shard_map(
        on_device,
        mesh=mesh,
        in_specs=(
            P(("groups", "ctx"), None),
            P(("groups", "ctx"), None),
            P(("groups", "ctx"), None),
            P(("groups", "ctx"), None),
            P("groups"),
        ),
        out_specs=(
            P(("groups", "ctx"), None),
            P(("groups", "ctx"), None),
            P(("groups", "ctx"), None),
            P(("groups", "ctx"), None),
        ),
        check_vma=False,
    )
```

```python
import math

import jax
import jax.numpy as jnp
import numpy as np
from jax import lax
from jax.experimental import pallas as pl
from jax.experimental.pallas import tpu as pltpu
from jax.sharding import PartitionSpec as P

QUERY_HEADS = 16
KEY_VALUE_HEADS = 4
HEAD_SIZE = 128
DOCUMENT_REACH = 8

NEGATIVE_FLOOR = -1e30


def block_home(count, block):
    if block < count:
        return block, 0
    return 2 * count - 1 - block, 1


def colored_moves(count, distance):
    edges = []
    for block in range(2 * count - distance):
        source, source_slot = block_home(count, block)
        target, target_slot = block_home(count, block + distance)
        edges.append((source, source_slot, target, target_slot))
    by_source, by_target = {}, {}
    for i, (s, _, t, _) in enumerate(edges):
        by_source.setdefault(s, []).append(i)
        by_target.setdefault(t, []).append(i)

    def partner(table, key, i):
        rest = [j for j in table[key] if j != i]
        return rest[0] if rest else None

    color = [None] * len(edges)

    def walk(i, through_target):
        while True:
            s, _, t, _ = edges[i]
            j = partner(by_target, t, i) if through_target else partner(by_source, s, i)
            if j is None or color[j] is not None:
                return
            color[j] = 1 - color[i]
            i, through_target = j, not through_target

    def degree(i):
        s, _, t, _ = edges[i]
        return min(len(by_source[s]), len(by_target[t]))

    for i in sorted(range(len(edges)), key=degree):
        if color[i] is None:
            color[i] = 0
            walk(i, True)
            walk(i, False)
    pairs = [[], []]
    send_slot = np.zeros((2, count), np.int32)
    receive_slot = np.full((2, count), -1, np.int32)
    for (s, ss, t, ts), c in zip(edges, color):
        pairs[c].append((s, t))
        send_slot[c, s] = ss
        receive_slot[c, t] = ts
    for c in range(2):
        assert len({s for s, _ in pairs[c]}) == len(pairs[c])
        assert len({t for _, t in pairs[c]}) == len(pairs[c])
    return pairs, send_slot, receive_slot


def permute(value, pairs):
    if not pairs:
        return jnp.zeros_like(value)
    return lax.ppermute(value, "ctx", pairs)


def prep_kernel(send_ref, key_ref, value_ref, own_ref, *pay_refs):
    heads = key_ref.shape[1] // HEAD_SIZE
    both = jnp.concatenate(
        [
            part
            for m in range(heads)
            for part in (
                key_ref[:, m * HEAD_SIZE : (m + 1) * HEAD_SIZE],
                value_ref[:, m * HEAD_SIZE : (m + 1) * HEAD_SIZE],
            )
        ],
        axis=1,
    )
    own_ref[...] = both
    rows = both.shape[0] // 2
    me = lax.axis_index("ctx")
    lower_half, upper_half = both[:rows], both[rows:]
    for n, pay_ref in enumerate(pay_refs):
        upper = send_ref[me * len(pay_refs) + n]
        pick = jnp.full(lower_half.shape, upper, jnp.int32) == 1
        pay_ref[...] = jnp.where(pick, upper_half, lower_half)


def attention_kernel(
    meta_ref, ends_ref, query_ref, grad_ref, own_ref, *refs, count, reach, hop, docs, scale
):
    near = 2 * hop
    near_refs = refs[:near]
    far_refs = refs[near : near + 2]
    out_ref, dquery_ref, own_grad_ref = refs[near + 2 : near + 5]
    pay_refs = refs[near + 5 : 2 * near + 5]
    window_ref = refs[2 * near + 5]
    block_rows = own_ref.shape[0] // 2
    window = reach + 1
    span = window * block_rows
    group_width = QUERY_HEADS // KEY_VALUE_HEADS
    my_index = meta_ref[0]

    def fill(w, first, second, first_ref, second_ref, rows):
        take_first = first.astype(jnp.int32)
        take_second = jnp.logical_and(second, jnp.logical_not(first)).astype(jnp.int32)
        shape = (block_rows, window_ref.shape[1])
        chosen = jnp.where(
            jnp.full(shape, take_first, jnp.int32) > 0,
            first_ref[rows, :],
            jnp.where(
                jnp.full(shape, take_second, jnp.int32) > 0,
                second_ref[rows, :],
                jnp.zeros(shape, window_ref.dtype),
            ),
        )
        window_ref[w * block_rows : (w + 1) * block_rows, :] = chosen

    for slot in range(2):
        own_block = my_index if slot == 0 else 2 * count - 1 - my_index
        window_ref[reach * block_rows :, :] = own_ref[
            slot * block_rows : (slot + 1) * block_rows, :
        ]
        for distance in range(1, hop + 1):
            fill(
                reach - distance,
                meta_ref[distance] == slot,
                meta_ref[hop + distance] == slot,
                near_refs[distance - 1],
                near_refs[hop + distance - 1],
                slice(0, block_rows),
            )
        for k in range(hop):
            fill(
                reach - hop - 1 - k,
                meta_ref[1 + near] == slot,
                meta_ref[2 + near] == slot,
                far_refs[0],
                far_refs[1],
                slice(k * block_rows, (k + 1) * block_rows),
            )

        query_place = own_block * block_rows + lax.broadcasted_iota(
            jnp.int32, (block_rows, 1), 0
        )
        key_place = (own_block - reach) * block_rows + lax.broadcasted_iota(
            jnp.int32, (1, span), 1
        )
        query_doc = jnp.zeros((block_rows, 1), jnp.int32)
        key_doc = jnp.zeros((1, span), jnp.int32)
        for j in range(docs):
            end = ends_ref[j]
            query_doc = query_doc + (query_place >= end).astype(jnp.int32)
            key_doc = key_doc + (key_place >= end).astype(jnp.int32)
        visible = (query_doc == key_doc) & (key_place <= query_place) & (key_place >= 0)

        rows = slice(slot * block_rows, (slot + 1) * block_rows)
        query = jnp.concatenate(
            [query_ref[rows, g * HEAD_SIZE : (g + 1) * HEAD_SIZE] for g in range(group_width)],
            axis=0,
        )
        grad = jnp.concatenate(
            [grad_ref[rows, g * HEAD_SIZE : (g + 1) * HEAD_SIZE] for g in range(group_width)],
            axis=0,
        )
        keys = window_ref[:, :HEAD_SIZE]
        values = window_ref[:, HEAD_SIZE:]
        contract_last = (((1,), (1,)), ((), ()))
        contract_first = (((0,), (0,)), ((), ()))
        scores = (
            lax.dot_general(query, keys, contract_last, preferred_element_type=jnp.float32)
            * scale
        )
        masked = jnp.where(
            visible[None], scores.reshape(group_width, block_rows, span), NEGATIVE_FLOOR
        ).reshape(group_width * block_rows, span)
        row_maximum = jnp.max(masked, axis=1, keepdims=True)
        row_sum = jnp.sum(jnp.exp(masked - row_maximum), axis=1, keepdims=True)
        log_norm = row_maximum + jnp.log(row_sum)
        probs = jnp.exp(masked - log_norm)
        probs_b = probs.astype(jnp.bfloat16)
        attended = jnp.dot(probs_b, values, preferred_element_type=jnp.float32)
        attended_b = attended.astype(jnp.bfloat16)
        delta = jnp.sum(
            grad.astype(jnp.float32) * attended_b.astype(jnp.float32), axis=1, keepdims=True
        )
        dprob = lax.dot_general(grad, values, contract_last, preferred_element_type=jnp.float32)
        dscore = (probs * (dprob - delta)).astype(jnp.bfloat16)
        dquery = jnp.dot(dscore, keys, preferred_element_type=jnp.float32) * scale
        dkey = (
            lax.dot_general(dscore, query, contract_first, preferred_element_type=jnp.float32)
            * scale
        )
        dvalue = lax.dot_general(
            probs_b, grad, contract_first, preferred_element_type=jnp.float32
        )
        dquery_b = dquery.astype(jnp.bfloat16)
        for g in range(group_width):
            cols = slice(g * HEAD_SIZE, (g + 1) * HEAD_SIZE)
            out_ref[rows, cols] = attended_b[g * block_rows : (g + 1) * block_rows]
            dquery_ref[rows, cols] = dquery_b[g * block_rows : (g + 1) * block_rows]
        own_grad_ref[rows, :HEAD_SIZE] = dkey[reach * block_rows :]
        own_grad_ref[rows, HEAD_SIZE:] = dvalue[reach * block_rows :]
        for n in range(near):
            distance = n % hop + 1
            mine = meta_ref[1 + n] == slot
            for half in range(2):
                w = reach - distance - half * hop
                source = slice(w * block_rows, (w + 1) * block_rows)
                target = slice(half * block_rows, (half + 1) * block_rows)
                fresh = jnp.concatenate([dkey[source], dvalue[source]], axis=1).astype(
                    jnp.bfloat16
                )
                if slot == 0:
                    kept = jnp.zeros(fresh.shape, fresh.dtype)
                else:
                    kept = pay_refs[n][target, :]
                pick = jnp.full(fresh.shape, mine.astype(jnp.int32), jnp.int32) > 0
                pay_refs[n][target, :] = jnp.where(pick, fresh, kept)


def on_device(queries, key_rows, value_rows, output_gradient, lengths):
    count = lax.axis_size("ctx")
    my_index = lax.axis_index("ctx")
    row_count = queries.shape[0]
    block_rows = row_count // 2
    pair_width = 2 * HEAD_SIZE
    width = KEY_VALUE_HEADS * pair_width
    reach = DOCUMENT_REACH
    hop = reach // 2
    near = 2 * hop
    window = reach + 1
    span = window * block_rows
    docs = lengths.shape[0]
    score_scale = 1.0 / math.sqrt(HEAD_SIZE)

    routes = [colored_moves(count, distance) for distance in range(1, hop + 1)]
    near_pairs = [routes[n % hop][0][n // hop] for n in range(near)]
    near_send_table = np.stack([routes[n % hop][1][n // hop] for n in range(near)], axis=1)
    near_send = jnp.asarray(near_send_table)[my_index]
    near_receive = jnp.asarray(
        np.stack([routes[n % hop][2][n // hop] for n in range(near)], axis=1)
    )[my_index]
    far_pairs, far_send_table, far_receive_table = colored_moves(count, hop)
    far_send = jnp.asarray(far_send_table.T)[my_index]
    far_receive = jnp.asarray(far_receive_table.T)[my_index]
    doc_ends = jnp.cumsum(lengths).astype(jnp.int32)

    whole_spec = pl.BlockSpec(index_map=lambda m, *_: (0, 0))
    pair_spec = pl.BlockSpec((row_count, pair_width), lambda m, *_: (0, m))
    move_spec = pl.BlockSpec((block_rows, pair_width), lambda m, *_: (0, m))
    run_spec = pl.BlockSpec((hop * block_rows, pair_width), lambda m, *_: (0, m))
    pair_move_spec = pl.BlockSpec((2 * block_rows, pair_width), lambda m, *_: (0, m))
    prep = pl.pallas_call(
        prep_kernel,
        grid_spec=pltpu.PrefetchScalarGridSpec(
            num_scalar_prefetch=1,
            grid=(1,),
            in_specs=[whole_spec, whole_spec],
            out_specs=[whole_spec] * (near + 1),
        ),
        out_shape=[jax.ShapeDtypeStruct((row_count, width), jnp.bfloat16)]
        + [jax.ShapeDtypeStruct((block_rows, width), jnp.bfloat16)] * near,
    )
    own_kv, *payloads = prep(
        jnp.asarray(near_send_table.reshape(-1).astype(np.int32)), key_rows, value_rows
    )
    received = [permute(payloads[n], near_pairs[n]) for n in range(near)]

    def near_block(slot, distance):
        first = received[distance - 1]
        second = received[hop + distance - 1]
        return jnp.where(near_receive[distance - 1] == slot, first, second)

    runs = [
        jnp.concatenate([near_block(slot, d) for d in range(1, hop + 1)]) for slot in range(2)
    ]
    far_received = [
        permute(jnp.where(far_send[c] == 1, runs[1], runs[0]), far_pairs[c]) for c in range(2)
    ]

    head_group = QUERY_HEADS // KEY_VALUE_HEADS * HEAD_SIZE
    query_spec = pl.BlockSpec((row_count, head_group), lambda m, *_: (0, m))
    part_spec = pl.BlockSpec((2 * span, pair_width), lambda m, *_: (0, m))
    meta = jnp.concatenate([my_index.reshape(1).astype(jnp.int32), near_receive, far_receive])
    kernel = pl.pallas_call(
        lambda *refs: attention_kernel(
            *refs, count=count, reach=reach, hop=hop, docs=docs, scale=score_scale
        ),
        grid_spec=pltpu.PrefetchScalarGridSpec(
            num_scalar_prefetch=2,
            grid=(KEY_VALUE_HEADS,),
            in_specs=[query_spec, query_spec, pair_spec] + [move_spec] * near + [run_spec] * 2,
            out_specs=[query_spec, query_spec, pair_spec] + [pair_move_spec] * near,
            scratch_shapes=[pltpu.VMEM((span, pair_width), jnp.bfloat16)],
        ),
        out_shape=[
            jax.ShapeDtypeStruct(queries.shape, jnp.bfloat16),
            jax.ShapeDtypeStruct(queries.shape, jnp.bfloat16),
            jax.ShapeDtypeStruct((row_count, width), jnp.float32),
        ]
        + [jax.ShapeDtypeStruct((2 * block_rows, width), jnp.bfloat16)] * near,
    )
    attended, query_grad, own_grad, *payloads_back = kernel(
        meta, doc_ends, queries, output_gradient, own_kv, *received, *far_received
    )
    lower_grad = own_grad[:block_rows]
    upper_grad = own_grad[block_rows:]
    relay_sum = [jnp.zeros_like(lower_grad), jnp.zeros_like(lower_grad)]
    for n in range(near):
        payload = payloads_back[n]
        back = permute(payload, [(t, s) for s, t in near_pairs[n]]).astype(jnp.float32)
        own_back, relay_back = back[:block_rows], back[block_rows:]
        to_upper = near_send[n] == 1
        lower_grad = lower_grad + jnp.where(to_upper, 0.0, own_back)
        upper_grad = upper_grad + jnp.where(to_upper, own_back, 0.0)
        relay_sum[0] = relay_sum[0] + jnp.where(to_upper, 0.0, relay_back)
        relay_sum[1] = relay_sum[1] + jnp.where(to_upper, relay_back, 0.0)
    for c in range(2):
        payload = jnp.where(far_receive[c] == 1, relay_sum[1], relay_sum[0])
        back = permute(payload.astype(jnp.bfloat16), [(t, s) for s, t in far_pairs[c]])
        back = back.astype(jnp.float32)
        lower_grad = lower_grad + jnp.where(far_send[c] == 1, 0.0, back)
        upper_grad = upper_grad + jnp.where(far_send[c] == 1, back, 0.0)
    grad_both = jnp.concatenate([lower_grad, upper_grad]).reshape(
        row_count, KEY_VALUE_HEADS, 2, HEAD_SIZE
    )
    key_width = KEY_VALUE_HEADS * HEAD_SIZE
    return (
        attended,
        query_grad,
        grad_both[:, :, 0].reshape(row_count, key_width).astype(jnp.bfloat16),
        grad_both[:, :, 1].reshape(row_count, key_width).astype(jnp.bfloat16),
    )


def solution(mesh):
    return jax.shard_map(
        on_device,
        mesh=mesh,
        in_specs=(
            P(("groups", "ctx"), None),
            P(("groups", "ctx"), None),
            P(("groups", "ctx"), None),
            P(("groups", "ctx"), None),
            P("groups"),
        ),
        out_specs=(
            P(("groups", "ctx"), None),
            P(("groups", "ctx"), None),
            P(("groups", "ctx"), None),
            P(("groups", "ctx"), None),
        ),
        check_vma=False,
    )
```

```python
import math

import jax
import jax.numpy as jnp
import numpy as np
from jax import lax
from jax.experimental import pallas as pl
from jax.experimental.pallas import tpu as pltpu
from jax.sharding import PartitionSpec as P

QUERY_HEADS = 16
KEY_VALUE_HEADS = 4
HEAD_SIZE = 128
DOCUMENT_REACH = 8

NEGATIVE_FLOOR = -1e30


def block_home(count, block):
    if block < count:
        return block, 0
    return 2 * count - 1 - block, 1


def colored_moves(count, distance):
    edges = []
    for block in range(2 * count - distance):
        source, source_slot = block_home(count, block)
        target, target_slot = block_home(count, block + distance)
        edges.append((source, source_slot, target, target_slot))
    by_source, by_target = {}, {}
    for i, (s, _, t, _) in enumerate(edges):
        by_source.setdefault(s, []).append(i)
        by_target.setdefault(t, []).append(i)

    def partner(table, key, i):
        rest = [j for j in table[key] if j != i]
        return rest[0] if rest else None

    color = [None] * len(edges)

    def walk(i, through_target):
        while True:
            s, _, t, _ = edges[i]
            j = partner(by_target, t, i) if through_target else partner(by_source, s, i)
            if j is None or color[j] is not None:
                return
            color[j] = 1 - color[i]
            i, through_target = j, not through_target

    def degree(i):
        s, _, t, _ = edges[i]
        return min(len(by_source[s]), len(by_target[t]))

    for i in sorted(range(len(edges)), key=degree):
        if color[i] is None:
            color[i] = 0
            walk(i, True)
            walk(i, False)
    pairs = [[], []]
    send_slot = np.zeros((2, count), np.int32)
    receive_slot = np.full((2, count), -1, np.int32)
    for (s, ss, t, ts), c in zip(edges, color):
        pairs[c].append((s, t))
        send_slot[c, s] = ss
        receive_slot[c, t] = ts
    for c in range(2):
        assert len({s for s, _ in pairs[c]}) == len(pairs[c])
        assert len({t for _, t in pairs[c]}) == len(pairs[c])
    return pairs, send_slot, receive_slot


def permute(value, pairs):
    if not pairs:
        return jnp.zeros_like(value)
    return lax.ppermute(value, "ctx", pairs)


def prep_kernel(send_ref, key_ref, value_ref, own_ref, *pay_refs):
    heads = key_ref.shape[1] // HEAD_SIZE
    both = jnp.concatenate(
        [
            part
            for m in range(heads)
            for part in (
                key_ref[:, m * HEAD_SIZE : (m + 1) * HEAD_SIZE],
                value_ref[:, m * HEAD_SIZE : (m + 1) * HEAD_SIZE],
            )
        ],
        axis=1,
    )
    own_ref[...] = both
    rows = both.shape[0] // 2
    me = lax.axis_index("ctx")
    lower_half, upper_half = both[:rows], both[rows:]
    for n, pay_ref in enumerate(pay_refs):
        upper = send_ref[me * len(pay_refs) + n]
        pick = jnp.full(lower_half.shape, upper, jnp.int32) == 1
        pay_ref[...] = jnp.where(pick, upper_half, lower_half)


def attention_kernel(
    meta_ref, ends_ref, query_ref, grad_ref, own_ref, *refs, count, reach, hop, docs, scale
):
    near = 2 * hop
    near_refs = refs[:near]
    far_refs = refs[near : near + 4]
    out_ref, dquery_ref, own_grad_ref = refs[near + 4 : near + 7]
    pay_refs = refs[near + 7 : 2 * near + 7]
    window_ref = refs[2 * near + 7]
    block_rows = own_ref.shape[0] // 2
    window = reach + 1
    span = window * block_rows
    group_width = QUERY_HEADS // KEY_VALUE_HEADS
    my_index = meta_ref[0]

    def fill(w, first, second, first_ref, second_ref, rows):
        take_first = first.astype(jnp.int32)
        take_second = jnp.logical_and(second, jnp.logical_not(first)).astype(jnp.int32)
        shape = (block_rows, window_ref.shape[1])
        chosen = jnp.where(
            jnp.full(shape, take_first, jnp.int32) > 0,
            first_ref[rows, :],
            jnp.where(
                jnp.full(shape, take_second, jnp.int32) > 0,
                second_ref[rows, :],
                jnp.zeros(shape, window_ref.dtype),
            ),
        )
        window_ref[w * block_rows : (w + 1) * block_rows, :] = chosen

    for slot in range(2):
        own_block = my_index if slot == 0 else 2 * count - 1 - my_index
        window_ref[reach * block_rows :, :] = own_ref[
            slot * block_rows : (slot + 1) * block_rows, :
        ]
        for distance in range(1, hop + 1):
            fill(
                reach - distance,
                meta_ref[distance] == slot,
                meta_ref[hop + distance] == slot,
                near_refs[distance - 1],
                near_refs[hop + distance - 1],
                slice(0, block_rows),
            )
        half_hop = hop // 2
        for k in range(hop):
            part = k // half_hop
            row = k % half_hop
            fill(
                reach - hop - 1 - k,
                meta_ref[1 + near] == slot,
                meta_ref[2 + near] == slot,
                far_refs[2 * part],
                far_refs[2 * part + 1],
                slice(row * block_rows, (row + 1) * block_rows),
            )

        query_place = own_block * block_rows + lax.broadcasted_iota(
            jnp.int32, (block_rows, 1), 0
        )
        key_place = (own_block - reach) * block_rows + lax.broadcasted_iota(
            jnp.int32, (1, span), 1
        )
        query_doc = jnp.zeros((block_rows, 1), jnp.int32)
        key_doc = jnp.zeros((1, span), jnp.int32)
        for j in range(docs):
            end = ends_ref[j]
            query_doc = query_doc + (query_place >= end).astype(jnp.int32)
            key_doc = key_doc + (key_place >= end).astype(jnp.int32)
        visible = (query_doc == key_doc) & (key_place <= query_place) & (key_place >= 0)

        rows = slice(slot * block_rows, (slot + 1) * block_rows)
        query = jnp.concatenate(
            [query_ref[rows, g * HEAD_SIZE : (g + 1) * HEAD_SIZE] for g in range(group_width)],
            axis=0,
        )
        grad = jnp.concatenate(
            [grad_ref[rows, g * HEAD_SIZE : (g + 1) * HEAD_SIZE] for g in range(group_width)],
            axis=0,
        )
        keys = window_ref[:, :HEAD_SIZE]
        values = window_ref[:, HEAD_SIZE:]
        contract_last = (((1,), (1,)), ((), ()))
        contract_first = (((0,), (0,)), ((), ()))
        scores = (
            lax.dot_general(query, keys, contract_last, preferred_element_type=jnp.float32)
            * scale
        )
        masked = jnp.where(
            visible[None], scores.reshape(group_width, block_rows, span), NEGATIVE_FLOOR
        ).reshape(group_width * block_rows, span)
        row_maximum = jnp.max(masked, axis=1, keepdims=True)
        row_sum = jnp.sum(jnp.exp(masked - row_maximum), axis=1, keepdims=True)
        log_norm = row_maximum + jnp.log(row_sum)
        probs = jnp.exp(masked - log_norm)
        probs_b = probs.astype(jnp.bfloat16)
        attended = jnp.dot(probs_b, values, preferred_element_type=jnp.float32)
        attended_b = attended.astype(jnp.bfloat16)
        delta = jnp.sum(
            grad.astype(jnp.float32) * attended_b.astype(jnp.float32), axis=1, keepdims=True
        )
        dprob = lax.dot_general(grad, values, contract_last, preferred_element_type=jnp.float32)
        dscore = (probs * (dprob - delta)).astype(jnp.bfloat16)
        dquery = jnp.dot(dscore, keys, preferred_element_type=jnp.float32) * scale
        dkey = (
            lax.dot_general(dscore, query, contract_first, preferred_element_type=jnp.float32)
            * scale
        )
        dvalue = lax.dot_general(
            probs_b, grad, contract_first, preferred_element_type=jnp.float32
        )
        dquery_b = dquery.astype(jnp.bfloat16)
        for g in range(group_width):
            cols = slice(g * HEAD_SIZE, (g + 1) * HEAD_SIZE)
            out_ref[rows, cols] = attended_b[g * block_rows : (g + 1) * block_rows]
            dquery_ref[rows, cols] = dquery_b[g * block_rows : (g + 1) * block_rows]
        own_grad_ref[rows, :HEAD_SIZE] = dkey[reach * block_rows :]
        own_grad_ref[rows, HEAD_SIZE:] = dvalue[reach * block_rows :]
        for n in range(near):
            distance = n % hop + 1
            mine = meta_ref[1 + n] == slot
            for half in range(2):
                w = reach - distance - half * hop
                source = slice(w * block_rows, (w + 1) * block_rows)
                target = slice(half * block_rows, (half + 1) * block_rows)
                fresh = jnp.concatenate([dkey[source], dvalue[source]], axis=1).astype(
                    jnp.bfloat16
                )
                if slot == 0:
                    kept = jnp.zeros(fresh.shape, fresh.dtype)
                else:
                    kept = pay_refs[n][target, :]
                pick = jnp.full(fresh.shape, mine.astype(jnp.int32), jnp.int32) > 0
                pay_refs[n][target, :] = jnp.where(pick, fresh, kept)


def on_device(queries, key_rows, value_rows, output_gradient, lengths):
    count = lax.axis_size("ctx")
    my_index = lax.axis_index("ctx")
    row_count = queries.shape[0]
    block_rows = row_count // 2
    pair_width = 2 * HEAD_SIZE
    width = KEY_VALUE_HEADS * pair_width
    reach = DOCUMENT_REACH
    hop = reach // 2
    near = 2 * hop
    window = reach + 1
    span = window * block_rows
    docs = lengths.shape[0]
    score_scale = 1.0 / math.sqrt(HEAD_SIZE)

    routes = [colored_moves(count, distance) for distance in range(1, hop + 1)]
    near_pairs = [routes[n % hop][0][n // hop] for n in range(near)]
    near_send_table = np.stack([routes[n % hop][1][n // hop] for n in range(near)], axis=1)
    near_send = jnp.asarray(near_send_table)[my_index]
    near_receive = jnp.asarray(
        np.stack([routes[n % hop][2][n // hop] for n in range(near)], axis=1)
    )[my_index]
    far_pairs, far_send_table, far_receive_table = colored_moves(count, hop)
    far_send = jnp.asarray(far_send_table.T)[my_index]
    far_receive = jnp.asarray(far_receive_table.T)[my_index]
    doc_ends = jnp.cumsum(lengths).astype(jnp.int32)

    whole_spec = pl.BlockSpec(index_map=lambda m, *_: (0, 0))
    pair_spec = pl.BlockSpec((row_count, pair_width), lambda m, *_: (0, m))
    move_spec = pl.BlockSpec((block_rows, pair_width), lambda m, *_: (0, m))
    run_spec = pl.BlockSpec((hop // 2 * block_rows, pair_width), lambda m, *_: (0, m))
    pair_move_spec = pl.BlockSpec((2 * block_rows, pair_width), lambda m, *_: (0, m))
    prep = pl.pallas_call(
        prep_kernel,
        grid_spec=pltpu.PrefetchScalarGridSpec(
            num_scalar_prefetch=1,
            grid=(1,),
            in_specs=[whole_spec, whole_spec],
            out_specs=[whole_spec] * (near + 1),
        ),
        out_shape=[jax.ShapeDtypeStruct((row_count, width), jnp.bfloat16)]
        + [jax.ShapeDtypeStruct((block_rows, width), jnp.bfloat16)] * near,
    )
    own_kv, *payloads = prep(
        jnp.asarray(near_send_table.reshape(-1).astype(np.int32)), key_rows, value_rows
    )
    received = [permute(payloads[n], near_pairs[n]) for n in range(near)]

    def near_block(slot, distance):
        first = received[distance - 1]
        second = received[hop + distance - 1]
        return jnp.where(near_receive[distance - 1] == slot, first, second)

    half_hop = hop // 2
    far_received = []
    for first in (1, 1 + half_hop):
        runs = [
            jnp.concatenate([near_block(slot, d) for d in range(first, first + half_hop)])
            for slot in range(2)
        ]
        far_received += [
            permute(jnp.where(far_send[c] == 1, runs[1], runs[0]), far_pairs[c])
            for c in range(2)
        ]

    head_group = QUERY_HEADS // KEY_VALUE_HEADS * HEAD_SIZE
    query_spec = pl.BlockSpec((row_count, head_group), lambda m, *_: (0, m))
    part_spec = pl.BlockSpec((2 * span, pair_width), lambda m, *_: (0, m))
    meta = jnp.concatenate([my_index.reshape(1).astype(jnp.int32), near_receive, far_receive])
    kernel = pl.pallas_call(
        lambda *refs: attention_kernel(
            *refs, count=count, reach=reach, hop=hop, docs=docs, scale=score_scale
        ),
        grid_spec=pltpu.PrefetchScalarGridSpec(
            num_scalar_prefetch=2,
            grid=(KEY_VALUE_HEADS,),
            in_specs=[query_spec, query_spec, pair_spec] + [move_spec] * near + [run_spec] * 4,
            out_specs=[query_spec, query_spec, pair_spec] + [pair_move_spec] * near,
            scratch_shapes=[pltpu.VMEM((span, pair_width), jnp.bfloat16)],
        ),
        out_shape=[
            jax.ShapeDtypeStruct(queries.shape, jnp.bfloat16),
            jax.ShapeDtypeStruct(queries.shape, jnp.bfloat16),
            jax.ShapeDtypeStruct((row_count, width), jnp.float32),
        ]
        + [jax.ShapeDtypeStruct((2 * block_rows, width), jnp.bfloat16)] * near,
    )
    attended, query_grad, own_grad, *payloads_back = kernel(
        meta, doc_ends, queries, output_gradient, own_kv, *received, *far_received
    )
    lower_grad = own_grad[:block_rows]
    upper_grad = own_grad[block_rows:]
    relay_sum = [jnp.zeros_like(lower_grad), jnp.zeros_like(lower_grad)]
    for n in range(near):
        payload = payloads_back[n]
        back = permute(payload, [(t, s) for s, t in near_pairs[n]]).astype(jnp.float32)
        own_back, relay_back = back[:block_rows], back[block_rows:]
        to_upper = near_send[n] == 1
        lower_grad = lower_grad + jnp.where(to_upper, 0.0, own_back)
        upper_grad = upper_grad + jnp.where(to_upper, own_back, 0.0)
        relay_sum[0] = relay_sum[0] + jnp.where(to_upper, 0.0, relay_back)
        relay_sum[1] = relay_sum[1] + jnp.where(to_upper, relay_back, 0.0)
    for c in range(2):
        payload = jnp.where(far_receive[c] == 1, relay_sum[1], relay_sum[0])
        back = permute(payload.astype(jnp.bfloat16), [(t, s) for s, t in far_pairs[c]])
        back = back.astype(jnp.float32)
        lower_grad = lower_grad + jnp.where(far_send[c] == 1, 0.0, back)
        upper_grad = upper_grad + jnp.where(far_send[c] == 1, back, 0.0)
    grad_both = jnp.concatenate([lower_grad, upper_grad]).reshape(
        row_count, KEY_VALUE_HEADS, 2, HEAD_SIZE
    )
    key_width = KEY_VALUE_HEADS * HEAD_SIZE
    return (
        attended,
        query_grad,
        grad_both[:, :, 0].reshape(row_count, key_width).astype(jnp.bfloat16),
        grad_both[:, :, 1].reshape(row_count, key_width).astype(jnp.bfloat16),
    )


def solution(mesh):
    return jax.shard_map(
        on_device,
        mesh=mesh,
        in_specs=(
            P(("groups", "ctx"), None),
            P(("groups", "ctx"), None),
            P(("groups", "ctx"), None),
            P(("groups", "ctx"), None),
            P("groups"),
        ),
        out_specs=(
            P(("groups", "ctx"), None),
            P(("groups", "ctx"), None),
            P(("groups", "ctx"), None),
            P(("groups", "ctx"), None),
        ),
        check_vma=False,
    )
```

```python
import math

import jax
import jax.numpy as jnp
import numpy as np
from jax import lax
from jax.experimental import pallas as pl
from jax.experimental.pallas import tpu as pltpu
from jax.sharding import PartitionSpec as P

QUERY_HEADS = 16
KEY_VALUE_HEADS = 4
HEAD_SIZE = 128
DOCUMENT_REACH = 8

NEGATIVE_FLOOR = -1e30


def block_home(count, block):
    if block < count:
        return block, 0
    return 2 * count - 1 - block, 1


def colored_moves(count, distance):
    edges = []
    for block in range(2 * count - distance):
        source, source_slot = block_home(count, block)
        target, target_slot = block_home(count, block + distance)
        edges.append((source, source_slot, target, target_slot))
    by_source, by_target = {}, {}
    for i, (s, _, t, _) in enumerate(edges):
        by_source.setdefault(s, []).append(i)
        by_target.setdefault(t, []).append(i)

    def partner(table, key, i):
        rest = [j for j in table[key] if j != i]
        return rest[0] if rest else None

    color = [None] * len(edges)

    def walk(i, through_target):
        while True:
            s, _, t, _ = edges[i]
            j = partner(by_target, t, i) if through_target else partner(by_source, s, i)
            if j is None or color[j] is not None:
                return
            color[j] = 1 - color[i]
            i, through_target = j, not through_target

    def degree(i):
        s, _, t, _ = edges[i]
        return min(len(by_source[s]), len(by_target[t]))

    for i in sorted(range(len(edges)), key=degree):
        if color[i] is None:
            color[i] = 0
            walk(i, True)
            walk(i, False)
    pairs = [[], []]
    send_slot = np.zeros((2, count), np.int32)
    receive_slot = np.full((2, count), -1, np.int32)
    for (s, ss, t, ts), c in zip(edges, color):
        pairs[c].append((s, t))
        send_slot[c, s] = ss
        receive_slot[c, t] = ts
    for c in range(2):
        assert len({s for s, _ in pairs[c]}) == len(pairs[c])
        assert len({t for _, t in pairs[c]}) == len(pairs[c])
    return pairs, send_slot, receive_slot


def permute(value, pairs):
    if not pairs:
        return jnp.zeros_like(value)
    return lax.ppermute(value, "ctx", pairs)


def prep_kernel(send_ref, key_ref, value_ref, own_ref, *pay_refs):
    heads = key_ref.shape[1] // HEAD_SIZE
    both = jnp.concatenate(
        [
            part
            for m in range(heads)
            for part in (
                key_ref[:, m * HEAD_SIZE : (m + 1) * HEAD_SIZE],
                value_ref[:, m * HEAD_SIZE : (m + 1) * HEAD_SIZE],
            )
        ],
        axis=1,
    )
    own_ref[...] = both
    rows = both.shape[0] // 2
    me = lax.axis_index("ctx")
    lower_half, upper_half = both[:rows], both[rows:]
    for n, pay_ref in enumerate(pay_refs):
        upper = send_ref[me * len(pay_refs) + n]
        pick = jnp.full(lower_half.shape, upper, jnp.int32) == 1
        pay_ref[...] = jnp.where(pick, upper_half, lower_half)


def attention_kernel(
    meta_ref, ends_ref, query_ref, grad_ref, own_ref, *refs, count, reach, hop, docs, scale
):
    near = 2 * hop
    near_refs = refs[:near]
    far_refs = refs[near : near + 4]
    out_ref, dquery_ref, own_grad_ref = refs[near + 4 : near + 7]
    pay_refs = refs[near + 7 : 2 * near + 7]
    window_ref = refs[2 * near + 7]
    block_rows = own_ref.shape[0] // 2
    window = reach + 1
    span = window * block_rows
    group_width = QUERY_HEADS // KEY_VALUE_HEADS
    my_index = meta_ref[0]

    def fill(w, first, second, first_ref, second_ref, rows):
        take_first = first.astype(jnp.int32)
        take_second = jnp.logical_and(second, jnp.logical_not(first)).astype(jnp.int32)
        shape = (block_rows, window_ref.shape[1])
        chosen = jnp.where(
            jnp.full(shape, take_first, jnp.int32) > 0,
            first_ref[rows, :],
            jnp.where(
                jnp.full(shape, take_second, jnp.int32) > 0,
                second_ref[rows, :],
                jnp.zeros(shape, window_ref.dtype),
            ),
        )
        window_ref[w * block_rows : (w + 1) * block_rows, :] = chosen

    for slot in range(2):
        own_block = my_index if slot == 0 else 2 * count - 1 - my_index
        window_ref[reach * block_rows :, :] = own_ref[
            slot * block_rows : (slot + 1) * block_rows, :
        ]
        for distance in range(1, hop + 1):
            fill(
                reach - distance,
                meta_ref[distance] == slot,
                meta_ref[hop + distance] == slot,
                near_refs[distance - 1],
                near_refs[hop + distance - 1],
                slice(0, block_rows),
            )
        half_hop = hop // 2
        for k in range(hop):
            part = k // half_hop
            row = k % half_hop
            fill(
                reach - hop - 1 - k,
                meta_ref[1 + near] == slot,
                meta_ref[2 + near] == slot,
                far_refs[2 * part],
                far_refs[2 * part + 1],
                slice(row * block_rows, (row + 1) * block_rows),
            )

        query_place = own_block * block_rows + lax.broadcasted_iota(
            jnp.int32, (block_rows, 1), 0
        )
        key_place = (own_block - reach) * block_rows + lax.broadcasted_iota(
            jnp.int32, (1, span), 1
        )
        query_doc = jnp.zeros((block_rows, 1), jnp.int32)
        key_doc = jnp.zeros((1, span), jnp.int32)
        for j in range(docs):
            end = ends_ref[j]
            query_doc = query_doc + (query_place >= end).astype(jnp.int32)
            key_doc = key_doc + (key_place >= end).astype(jnp.int32)
        visible = (query_doc == key_doc) & (key_place <= query_place) & (key_place >= 0)

        rows = slice(slot * block_rows, (slot + 1) * block_rows)
        query = jnp.concatenate(
            [query_ref[rows, g * HEAD_SIZE : (g + 1) * HEAD_SIZE] for g in range(group_width)],
            axis=0,
        )
        grad = jnp.concatenate(
            [grad_ref[rows, g * HEAD_SIZE : (g + 1) * HEAD_SIZE] for g in range(group_width)],
            axis=0,
        )
        keys = window_ref[:, :HEAD_SIZE]
        values = window_ref[:, HEAD_SIZE:]
        contract_last = (((1,), (1,)), ((), ()))
        contract_first = (((0,), (0,)), ((), ()))
        scores = (
            lax.dot_general(query, keys, contract_last, preferred_element_type=jnp.float32)
            * scale
        )
        masked = jnp.where(
            visible[None], scores.reshape(group_width, block_rows, span), NEGATIVE_FLOOR
        ).reshape(group_width * block_rows, span)
        row_maximum = jnp.max(masked, axis=1, keepdims=True)
        row_sum = jnp.sum(jnp.exp(masked - row_maximum), axis=1, keepdims=True)
        log_norm = row_maximum + jnp.log(row_sum)
        probs = jnp.exp(masked - log_norm)
        probs_b = probs.astype(jnp.bfloat16)
        attended = jnp.dot(probs_b, values, preferred_element_type=jnp.float32)
        attended_b = attended.astype(jnp.bfloat16)
        delta = jnp.sum(
            grad.astype(jnp.float32) * attended_b.astype(jnp.float32), axis=1, keepdims=True
        )
        dprob = lax.dot_general(grad, values, contract_last, preferred_element_type=jnp.float32)
        dscore = (probs * (dprob - delta)).astype(jnp.bfloat16)
        dquery = jnp.dot(dscore, keys, preferred_element_type=jnp.float32) * scale
        dkey = (
            lax.dot_general(dscore, query, contract_first, preferred_element_type=jnp.float32)
            * scale
        )
        dvalue = lax.dot_general(
            probs_b, grad, contract_first, preferred_element_type=jnp.float32
        )
        dquery_b = dquery.astype(jnp.bfloat16)
        for g in range(group_width):
            cols = slice(g * HEAD_SIZE, (g + 1) * HEAD_SIZE)
            out_ref[rows, cols] = attended_b[g * block_rows : (g + 1) * block_rows]
            dquery_ref[rows, cols] = dquery_b[g * block_rows : (g + 1) * block_rows]
        own_grad_ref[rows, :HEAD_SIZE] = dkey[reach * block_rows :]
        own_grad_ref[rows, HEAD_SIZE:] = dvalue[reach * block_rows :]
        for n in range(near):
            distance = n % hop + 1
            mine = meta_ref[1 + n] == slot
            for half in range(2):
                w = reach - distance - half * hop
                source = slice(w * block_rows, (w + 1) * block_rows)
                target = slice(half * block_rows, (half + 1) * block_rows)
                fresh = jnp.concatenate([dkey[source], dvalue[source]], axis=1).astype(
                    jnp.bfloat16
                )
                if slot == 0:
                    kept = jnp.zeros(fresh.shape, fresh.dtype)
                else:
                    kept = pay_refs[n][target, :]
                pick = jnp.full(fresh.shape, mine.astype(jnp.int32), jnp.int32) > 0
                pay_refs[n][target, :] = jnp.where(pick, fresh, kept)


def on_device(queries, key_rows, value_rows, output_gradient, lengths):
    count = lax.axis_size("ctx")
    my_index = lax.axis_index("ctx")
    row_count = queries.shape[0]
    block_rows = row_count // 2
    pair_width = 2 * HEAD_SIZE
    width = KEY_VALUE_HEADS * pair_width
    reach = DOCUMENT_REACH
    hop = reach // 2
    near = 2 * hop
    window = reach + 1
    span = window * block_rows
    docs = lengths.shape[0]
    score_scale = 1.0 / math.sqrt(HEAD_SIZE)

    routes = [colored_moves(count, distance) for distance in range(1, hop + 1)]
    near_pairs = [routes[n % hop][0][n // hop] for n in range(near)]
    near_send_table = np.stack([routes[n % hop][1][n // hop] for n in range(near)], axis=1)
    near_send = jnp.asarray(near_send_table)[my_index]
    near_receive = jnp.asarray(
        np.stack([routes[n % hop][2][n // hop] for n in range(near)], axis=1)
    )[my_index]
    far_pairs, far_send_table, far_receive_table = colored_moves(count, hop)
    far_send = jnp.asarray(far_send_table.T)[my_index]
    far_receive = jnp.asarray(far_receive_table.T)[my_index]
    doc_ends = jnp.cumsum(lengths).astype(jnp.int32)

    whole_spec = pl.BlockSpec(index_map=lambda m, *_: (0, 0))
    pair_spec = pl.BlockSpec((row_count, pair_width), lambda m, *_: (0, m))
    move_spec = pl.BlockSpec((block_rows, pair_width), lambda m, *_: (0, m))
    run_spec = pl.BlockSpec((hop // 2 * block_rows, pair_width), lambda m, *_: (0, m))
    pair_move_spec = pl.BlockSpec((2 * block_rows, pair_width), lambda m, *_: (0, m))
    prep = pl.pallas_call(
        prep_kernel,
        grid_spec=pltpu.PrefetchScalarGridSpec(
            num_scalar_prefetch=1,
            grid=(1,),
            in_specs=[whole_spec, whole_spec],
            out_specs=[whole_spec] * (near + 1),
        ),
        out_shape=[jax.ShapeDtypeStruct((row_count, width), jnp.bfloat16)]
        + [jax.ShapeDtypeStruct((block_rows, width), jnp.bfloat16)] * near,
    )
    own_kv, *payloads = prep(
        jnp.asarray(near_send_table.reshape(-1).astype(np.int32)), key_rows, value_rows
    )
    received = [permute(payloads[n], near_pairs[n]) for n in range(near)]

    def near_block(slot, distance):
        first = received[distance - 1]
        second = received[hop + distance - 1]
        return jnp.where(near_receive[distance - 1] == slot, first, second)

    half_hop = hop // 2
    far_received = []
    for first in (1, 1 + half_hop):
        runs = [
            jnp.concatenate([near_block(slot, d) for d in range(first, first + half_hop)])
            for slot in range(2)
        ]
        far_received += [
            permute(jnp.where(far_send[c] == 1, runs[1], runs[0]), far_pairs[c])
            for c in range(2)
        ]

    head_group = QUERY_HEADS // KEY_VALUE_HEADS * HEAD_SIZE
    query_spec = pl.BlockSpec((row_count, head_group), lambda m, *_: (0, m))
    part_spec = pl.BlockSpec((2 * span, pair_width), lambda m, *_: (0, m))
    meta = jnp.concatenate([my_index.reshape(1).astype(jnp.int32), near_receive, far_receive])
    kernel = pl.pallas_call(
        lambda *refs: attention_kernel(
            *refs, count=count, reach=reach, hop=hop, docs=docs, scale=score_scale
        ),
        grid_spec=pltpu.PrefetchScalarGridSpec(
            num_scalar_prefetch=2,
            grid=(KEY_VALUE_HEADS,),
            in_specs=[query_spec, query_spec, pair_spec] + [move_spec] * near + [run_spec] * 4,
            out_specs=[query_spec, query_spec, pair_spec] + [pair_move_spec] * near,
            scratch_shapes=[pltpu.VMEM((span, pair_width), jnp.bfloat16)],
        ),
        out_shape=[
            jax.ShapeDtypeStruct(queries.shape, jnp.bfloat16),
            jax.ShapeDtypeStruct(queries.shape, jnp.bfloat16),
            jax.ShapeDtypeStruct((row_count, width), jnp.float32),
        ]
        + [jax.ShapeDtypeStruct((2 * block_rows, width), jnp.bfloat16)] * near,
    )
    attended, query_grad, own_grad, *payloads_back = kernel(
        meta, doc_ends, queries, output_gradient, own_kv, *received, *far_received
    )
    lower_grad = own_grad[:block_rows]
    upper_grad = own_grad[block_rows:]
    relay_sums = [[jnp.zeros_like(lower_grad)] * 2 for _ in range(2)]
    for n in range(near):
        relay_sum = relay_sums[(n % hop) // (hop // 2)]
        payload = payloads_back[n]
        back = permute(payload, [(t, s) for s, t in near_pairs[n]]).astype(jnp.float32)
        own_back, relay_back = back[:block_rows], back[block_rows:]
        to_upper = near_send[n] == 1
        lower_grad = lower_grad + jnp.where(to_upper, 0.0, own_back)
        upper_grad = upper_grad + jnp.where(to_upper, own_back, 0.0)
        relay_sum[0] = relay_sum[0] + jnp.where(to_upper, 0.0, relay_back)
        relay_sum[1] = relay_sum[1] + jnp.where(to_upper, relay_back, 0.0)
    for relay_sum, c in [(sums, c) for sums in relay_sums for c in range(2)]:
        payload = jnp.where(far_receive[c] == 1, relay_sum[1], relay_sum[0])
        back = permute(payload.astype(jnp.bfloat16), [(t, s) for s, t in far_pairs[c]])
        back = back.astype(jnp.float32)
        lower_grad = lower_grad + jnp.where(far_send[c] == 1, 0.0, back)
        upper_grad = upper_grad + jnp.where(far_send[c] == 1, back, 0.0)
    grad_both = jnp.concatenate([lower_grad, upper_grad]).reshape(
        row_count, KEY_VALUE_HEADS, 2, HEAD_SIZE
    )
    key_width = KEY_VALUE_HEADS * HEAD_SIZE
    return (
        attended,
        query_grad,
        grad_both[:, :, 0].reshape(row_count, key_width).astype(jnp.bfloat16),
        grad_both[:, :, 1].reshape(row_count, key_width).astype(jnp.bfloat16),
    )


def solution(mesh):
    return jax.shard_map(
        on_device,
        mesh=mesh,
        in_specs=(
            P(("groups", "ctx"), None),
            P(("groups", "ctx"), None),
            P(("groups", "ctx"), None),
            P(("groups", "ctx"), None),
            P("groups"),
        ),
        out_specs=(
            P(("groups", "ctx"), None),
            P(("groups", "ctx"), None),
            P(("groups", "ctx"), None),
            P(("groups", "ctx"), None),
        ),
        check_vma=False,
    )
```

```python
import math

import jax
import jax.numpy as jnp
import numpy as np
from jax import lax
from jax.experimental import pallas as pl
from jax.experimental.pallas import tpu as pltpu
from jax.sharding import PartitionSpec as P

QUERY_HEADS = 16
KEY_VALUE_HEADS = 4
HEAD_SIZE = 128
DOCUMENT_REACH = 8

NEGATIVE_FLOOR = -1e30
RELAY_RUN = 1


def block_home(count, block):
    if block < count:
        return block, 0
    return 2 * count - 1 - block, 1


def colored_moves(count, distance):
    edges = []
    for block in range(2 * count - distance):
        source, source_slot = block_home(count, block)
        target, target_slot = block_home(count, block + distance)
        edges.append((source, source_slot, target, target_slot))
    by_source, by_target = {}, {}
    for i, (s, _, t, _) in enumerate(edges):
        by_source.setdefault(s, []).append(i)
        by_target.setdefault(t, []).append(i)

    def partner(table, key, i):
        rest = [j for j in table[key] if j != i]
        return rest[0] if rest else None

    color = [None] * len(edges)

    def walk(i, through_target):
        while True:
            s, _, t, _ = edges[i]
            j = partner(by_target, t, i) if through_target else partner(by_source, s, i)
            if j is None or color[j] is not None:
                return
            color[j] = 1 - color[i]
            i, through_target = j, not through_target

    def degree(i):
        s, _, t, _ = edges[i]
        return min(len(by_source[s]), len(by_target[t]))

    for i in sorted(range(len(edges)), key=degree):
        if color[i] is None:
            color[i] = 0
            walk(i, True)
            walk(i, False)
    pairs = [[], []]
    send_slot = np.zeros((2, count), np.int32)
    receive_slot = np.full((2, count), -1, np.int32)
    for (s, ss, t, ts), c in zip(edges, color):
        pairs[c].append((s, t))
        send_slot[c, s] = ss
        receive_slot[c, t] = ts
    for c in range(2):
        assert len({s for s, _ in pairs[c]}) == len(pairs[c])
        assert len({t for _, t in pairs[c]}) == len(pairs[c])
    return pairs, send_slot, receive_slot


def permute(value, pairs):
    if not pairs:
        return jnp.zeros_like(value)
    return lax.ppermute(value, "ctx", pairs)


def prep_kernel(send_ref, key_ref, value_ref, own_ref, *pay_refs):
    heads = key_ref.shape[1] // HEAD_SIZE
    both = jnp.concatenate(
        [
            part
            for m in range(heads)
            for part in (
                key_ref[:, m * HEAD_SIZE : (m + 1) * HEAD_SIZE],
                value_ref[:, m * HEAD_SIZE : (m + 1) * HEAD_SIZE],
            )
        ],
        axis=1,
    )
    own_ref[...] = both
    rows = both.shape[0] // 2
    me = lax.axis_index("ctx")
    lower_half, upper_half = both[:rows], both[rows:]
    for n, pay_ref in enumerate(pay_refs):
        upper = send_ref[me * len(pay_refs) + n]
        pick = jnp.full(lower_half.shape, upper, jnp.int32) == 1
        pay_ref[...] = jnp.where(pick, upper_half, lower_half)


def attention_kernel(
    meta_ref, ends_ref, query_ref, grad_ref, own_ref, *refs, count, reach, hop, docs, scale
):
    near = 2 * hop
    near_refs = refs[:near]
    relays = 2 * (hop // RELAY_RUN)
    far_refs = refs[near : near + relays]
    out_ref, dquery_ref, own_grad_ref = refs[near + relays : near + relays + 3]
    pay_refs = refs[near + relays + 3 : 2 * near + relays + 3]
    window_ref = refs[2 * near + relays + 3]
    block_rows = own_ref.shape[0] // 2
    window = reach + 1
    span = window * block_rows
    group_width = QUERY_HEADS // KEY_VALUE_HEADS
    my_index = meta_ref[0]

    def fill(w, first, second, first_ref, second_ref, rows):
        take_first = first.astype(jnp.int32)
        take_second = jnp.logical_and(second, jnp.logical_not(first)).astype(jnp.int32)
        shape = (block_rows, window_ref.shape[1])
        chosen = jnp.where(
            jnp.full(shape, take_first, jnp.int32) > 0,
            first_ref[rows, :],
            jnp.where(
                jnp.full(shape, take_second, jnp.int32) > 0,
                second_ref[rows, :],
                jnp.zeros(shape, window_ref.dtype),
            ),
        )
        window_ref[w * block_rows : (w + 1) * block_rows, :] = chosen

    for slot in range(2):
        own_block = my_index if slot == 0 else 2 * count - 1 - my_index
        window_ref[reach * block_rows :, :] = own_ref[
            slot * block_rows : (slot + 1) * block_rows, :
        ]
        for distance in range(1, hop + 1):
            fill(
                reach - distance,
                meta_ref[distance] == slot,
                meta_ref[hop + distance] == slot,
                near_refs[distance - 1],
                near_refs[hop + distance - 1],
                slice(0, block_rows),
            )
        for k in range(hop):
            part = k // RELAY_RUN
            row = k % RELAY_RUN
            fill(
                reach - hop - 1 - k,
                meta_ref[1 + near] == slot,
                meta_ref[2 + near] == slot,
                far_refs[2 * part],
                far_refs[2 * part + 1],
                slice(row * block_rows, (row + 1) * block_rows),
            )

        query_place = own_block * block_rows + lax.broadcasted_iota(
            jnp.int32, (block_rows, 1), 0
        )
        key_place = (own_block - reach) * block_rows + lax.broadcasted_iota(
            jnp.int32, (1, span), 1
        )
        query_doc = jnp.zeros((block_rows, 1), jnp.int32)
        key_doc = jnp.zeros((1, span), jnp.int32)
        for j in range(docs):
            end = ends_ref[j]
            query_doc = query_doc + (query_place >= end).astype(jnp.int32)
            key_doc = key_doc + (key_place >= end).astype(jnp.int32)
        visible = (query_doc == key_doc) & (key_place <= query_place) & (key_place >= 0)

        rows = slice(slot * block_rows, (slot + 1) * block_rows)
        query = jnp.concatenate(
            [query_ref[rows, g * HEAD_SIZE : (g + 1) * HEAD_SIZE] for g in range(group_width)],
            axis=0,
        )
        grad = jnp.concatenate(
            [grad_ref[rows, g * HEAD_SIZE : (g + 1) * HEAD_SIZE] for g in range(group_width)],
            axis=0,
        )
        keys = window_ref[:, :HEAD_SIZE]
        values = window_ref[:, HEAD_SIZE:]
        contract_last = (((1,), (1,)), ((), ()))
        contract_first = (((0,), (0,)), ((), ()))
        scores = (
            lax.dot_general(query, keys, contract_last, preferred_element_type=jnp.float32)
            * scale
        )
        masked = jnp.where(
            visible[None], scores.reshape(group_width, block_rows, span), NEGATIVE_FLOOR
        ).reshape(group_width * block_rows, span)
        row_maximum = jnp.max(masked, axis=1, keepdims=True)
        row_sum = jnp.sum(jnp.exp(masked - row_maximum), axis=1, keepdims=True)
        log_norm = row_maximum + jnp.log(row_sum)
        probs = jnp.exp(masked - log_norm)
        probs_b = probs.astype(jnp.bfloat16)
        attended = jnp.dot(probs_b, values, preferred_element_type=jnp.float32)
        attended_b = attended.astype(jnp.bfloat16)
        delta = jnp.sum(
            grad.astype(jnp.float32) * attended_b.astype(jnp.float32), axis=1, keepdims=True
        )
        dprob = lax.dot_general(grad, values, contract_last, preferred_element_type=jnp.float32)
        dscore = (probs * (dprob - delta)).astype(jnp.bfloat16)
        dquery = jnp.dot(dscore, keys, preferred_element_type=jnp.float32) * scale
        dkey = (
            lax.dot_general(dscore, query, contract_first, preferred_element_type=jnp.float32)
            * scale
        )
        dvalue = lax.dot_general(
            probs_b, grad, contract_first, preferred_element_type=jnp.float32
        )
        dquery_b = dquery.astype(jnp.bfloat16)
        for g in range(group_width):
            cols = slice(g * HEAD_SIZE, (g + 1) * HEAD_SIZE)
            out_ref[rows, cols] = attended_b[g * block_rows : (g + 1) * block_rows]
            dquery_ref[rows, cols] = dquery_b[g * block_rows : (g + 1) * block_rows]
        own_grad_ref[rows, :HEAD_SIZE] = dkey[reach * block_rows :]
        own_grad_ref[rows, HEAD_SIZE:] = dvalue[reach * block_rows :]
        for n in range(near):
            distance = n % hop + 1
            mine = meta_ref[1 + n] == slot
            for half in range(2):
                w = reach - distance - half * hop
                source = slice(w * block_rows, (w + 1) * block_rows)
                target = slice(half * block_rows, (half + 1) * block_rows)
                fresh = jnp.concatenate([dkey[source], dvalue[source]], axis=1).astype(
                    jnp.bfloat16
                )
                if slot == 0:
                    kept = jnp.zeros(fresh.shape, fresh.dtype)
                else:
                    kept = pay_refs[n][target, :]
                pick = jnp.full(fresh.shape, mine.astype(jnp.int32), jnp.int32) > 0
                pay_refs[n][target, :] = jnp.where(pick, fresh, kept)


def on_device(queries, key_rows, value_rows, output_gradient, lengths):
    count = lax.axis_size("ctx")
    my_index = lax.axis_index("ctx")
    row_count = queries.shape[0]
    block_rows = row_count // 2
    pair_width = 2 * HEAD_SIZE
    width = KEY_VALUE_HEADS * pair_width
    reach = DOCUMENT_REACH
    hop = reach // 2
    near = 2 * hop
    window = reach + 1
    span = window * block_rows
    docs = lengths.shape[0]
    score_scale = 1.0 / math.sqrt(HEAD_SIZE)

    routes = [colored_moves(count, distance) for distance in range(1, hop + 1)]
    near_pairs = [routes[n % hop][0][n // hop] for n in range(near)]
    near_send_table = np.stack([routes[n % hop][1][n // hop] for n in range(near)], axis=1)
    near_send = jnp.asarray(near_send_table)[my_index]
    near_receive = jnp.asarray(
        np.stack([routes[n % hop][2][n // hop] for n in range(near)], axis=1)
    )[my_index]
    far_pairs, far_send_table, far_receive_table = colored_moves(count, hop)
    far_send = jnp.asarray(far_send_table.T)[my_index]
    far_receive = jnp.asarray(far_receive_table.T)[my_index]
    doc_ends = jnp.cumsum(lengths).astype(jnp.int32)

    whole_spec = pl.BlockSpec(index_map=lambda m, *_: (0, 0))
    pair_spec = pl.BlockSpec((row_count, pair_width), lambda m, *_: (0, m))
    move_spec = pl.BlockSpec((block_rows, pair_width), lambda m, *_: (0, m))
    run_spec = pl.BlockSpec((RELAY_RUN * block_rows, pair_width), lambda m, *_: (0, m))
    pair_move_spec = pl.BlockSpec((2 * block_rows, pair_width), lambda m, *_: (0, m))
    prep = pl.pallas_call(
        prep_kernel,
        grid_spec=pltpu.PrefetchScalarGridSpec(
            num_scalar_prefetch=1,
            grid=(1,),
            in_specs=[whole_spec, whole_spec],
            out_specs=[whole_spec] * (near + 1),
        ),
        out_shape=[jax.ShapeDtypeStruct((row_count, width), jnp.bfloat16)]
        + [jax.ShapeDtypeStruct((block_rows, width), jnp.bfloat16)] * near,
    )
    own_kv, *payloads = prep(
        jnp.asarray(near_send_table.reshape(-1).astype(np.int32)), key_rows, value_rows
    )
    received = [permute(payloads[n], near_pairs[n]) for n in range(near)]

    def near_block(slot, distance):
        first = received[distance - 1]
        second = received[hop + distance - 1]
        return jnp.where(near_receive[distance - 1] == slot, first, second)

    far_received = []
    for first in range(1, hop + 1, RELAY_RUN):
        runs = [
            jnp.concatenate([near_block(slot, d) for d in range(first, first + RELAY_RUN)])
            for slot in range(2)
        ]
        far_received += [
            permute(jnp.where(far_send[c] == 1, runs[1], runs[0]), far_pairs[c])
            for c in range(2)
        ]

    head_group = QUERY_HEADS // KEY_VALUE_HEADS * HEAD_SIZE
    query_spec = pl.BlockSpec((row_count, head_group), lambda m, *_: (0, m))
    part_spec = pl.BlockSpec((2 * span, pair_width), lambda m, *_: (0, m))
    meta = jnp.concatenate([my_index.reshape(1).astype(jnp.int32), near_receive, far_receive])
    kernel = pl.pallas_call(
        lambda *refs: attention_kernel(
            *refs, count=count, reach=reach, hop=hop, docs=docs, scale=score_scale
        ),
        grid_spec=pltpu.PrefetchScalarGridSpec(
            num_scalar_prefetch=2,
            grid=(KEY_VALUE_HEADS,),
            in_specs=[query_spec, query_spec, pair_spec] + [move_spec] * near + [run_spec] * (2 * hop // RELAY_RUN),
            out_specs=[query_spec, query_spec, pair_spec] + [pair_move_spec] * near,
            scratch_shapes=[pltpu.VMEM((span, pair_width), jnp.bfloat16)],
        ),
        out_shape=[
            jax.ShapeDtypeStruct(queries.shape, jnp.bfloat16),
            jax.ShapeDtypeStruct(queries.shape, jnp.bfloat16),
            jax.ShapeDtypeStruct((row_count, width), jnp.float32),
        ]
        + [jax.ShapeDtypeStruct((2 * block_rows, width), jnp.bfloat16)] * near,
    )
    attended, query_grad, own_grad, *payloads_back = kernel(
        meta, doc_ends, queries, output_gradient, own_kv, *received, *far_received
    )
    lower_grad = own_grad[:block_rows]
    upper_grad = own_grad[block_rows:]
    relay_sum = [jnp.zeros_like(lower_grad), jnp.zeros_like(lower_grad)]
    for n in range(near):
        payload = payloads_back[n]
        back = permute(payload, [(t, s) for s, t in near_pairs[n]]).astype(jnp.float32)
        own_back, relay_back = back[:block_rows], back[block_rows:]
        to_upper = near_send[n] == 1
        lower_grad = lower_grad + jnp.where(to_upper, 0.0, own_back)
        upper_grad = upper_grad + jnp.where(to_upper, own_back, 0.0)
        relay_sum[0] = relay_sum[0] + jnp.where(to_upper, 0.0, relay_back)
        relay_sum[1] = relay_sum[1] + jnp.where(to_upper, relay_back, 0.0)
    for c in range(2):
        payload = jnp.where(far_receive[c] == 1, relay_sum[1], relay_sum[0])
        back = permute(payload.astype(jnp.bfloat16), [(t, s) for s, t in far_pairs[c]])
        back = back.astype(jnp.float32)
        lower_grad = lower_grad + jnp.where(far_send[c] == 1, 0.0, back)
        upper_grad = upper_grad + jnp.where(far_send[c] == 1, back, 0.0)
    grad_both = jnp.concatenate([lower_grad, upper_grad]).reshape(
        row_count, KEY_VALUE_HEADS, 2, HEAD_SIZE
    )
    key_width = KEY_VALUE_HEADS * HEAD_SIZE
    return (
        attended,
        query_grad,
        grad_both[:, :, 0].reshape(row_count, key_width).astype(jnp.bfloat16),
        grad_both[:, :, 1].reshape(row_count, key_width).astype(jnp.bfloat16),
    )


def solution(mesh):
    return jax.shard_map(
        on_device,
        mesh=mesh,
        in_specs=(
            P(("groups", "ctx"), None),
            P(("groups", "ctx"), None),
            P(("groups", "ctx"), None),
            P(("groups", "ctx"), None),
            P("groups"),
        ),
        out_specs=(
            P(("groups", "ctx"), None),
            P(("groups", "ctx"), None),
            P(("groups", "ctx"), None),
            P(("groups", "ctx"), None),
        ),
        check_vma=False,
    )
```
